32 devices in a mesh: shot: 2 (over y), real: 4 (over x, core), tile: 4 (over z).
Axes of the slice: x: 2, y: 2, z: 4, core: 2. Of those that a mesh axis runs over, the one named last changes fastest.
Arguments:
- courant: float32 [4, 64, 160, 128], P('real', 'tile'), may hold values from 0.01 to 0.05
- prev_field: float32 [8, 64, 160, 128], P(('shot', 'real'), 'tile'), parts along dimension 0, may hold values from -6 to 6
- cur_field: float32 [8, 64, 160, 128], P(('shot', 'real'), 'tile'), parts along dimension 0, may hold values from -6 to 6
- adj_prev: float32 [8, 64, 160, 128], P(('shot', 'real'), 'tile'), parts along dimension 0, may hold values from -6 to 6
- adj_cur: float32 [8, 64, 160, 128], P(('shot', 'real'), 'tile'), parts along dimension 0, may hold values from -6 to 6
- buoyancy: float32 [64, 160, 128], P('tile'), may hold values from 0.4 to 2.5
- wavelet: float32 [4], P('shot'), parts along dimension 0, may hold values from -16 to 16
- src_cell: int32 [2], P('shot'), parts along dimension 0, may hold values from 0 to 1310719
- rec_cell: int32 [512], P('shot'), parts along dimension 0, may hold values from 0 to 1310719
- observed: float32 [4, 256], P('shot'), parts along dimension 0, may hold values from -6 to 6
Outputs:
- image: float32 [128, 160, 128], P(('shot', 'tile')), parts along dimension 0
- adj_state: float32 [8, 64, 160, 128], P(('shot', 'real'), 'tile'), parts along dimension 0
The draws below stay inside these ranges and needn't reach their ends.
There are 2 independent parts, one for each index of `shot`. The reference program is written for one: setup_inputs(seed, part) draws one part's arguments, and reference() takes and returns one part's arrays. A program takes and returns all parts, laid end to end along the dimension named above; an argument that names none is the same for every part. Nothing has to cross between parts.
Inputs may be any that keep to these rules, and one draw needn't show every extreme that they name: `src_cell`: A flattened cell index x * 160 * 128 + y * 128 + z. `rec_cell`: flattened cell indices x * 160 * 128 + y * 128 + z; several receivers may share a cell.
All inputs are finite; a program needn't handle non-finite values.
Results may differ from the reference program's by a relative error of at most 0.00002.
Values sent between devices are 32-bit elements; how exact they have to be, the bound alone decides.
No kernel may reach another device: no remote copies, remote signals or barrier semaphores. Data moves between devices by JAX's collectives and lax.ppermute only.
A program may use at most 128 MiB of HBM per device.

```python
import math
import jax
import jax.numpy as jnp
from jax import lax

NY = 160
NZ = 128
NREC = 256
STEPS = 2
REALS = 4
NX = 64


def plant(drawn, own_key, smallest, high):
    longest = drawn.shape.index(max(drawn.shape))
    spots = []
    for shift in (0, 1):
        where = [jax.random.randint(jax.random.fold_in(own_key, axis), (), 0, length) for axis, length in enumerate(drawn.shape)]
        where[longest] = (where[longest] + shift) % drawn.shape[longest]
        spots.append(tuple(where))
    return drawn.at[spots[0]].set(smallest).at[spots[1]].set(high)


def level_of(rng, shape, pieces, low, top_value):
    level, own = 1.0, jax.random.fold_in(rng, 6)
    for dim, shards_of in pieces:
        steps = jnp.exp(jax.random.uniform(jax.random.fold_in(own, dim), (shards_of,), jnp.float32, low / len(pieces), top_value / len(pieces)))
        level = level * jnp.repeat(steps, shape[dim] // shards_of).reshape([-1 if axis == dim else 1 for axis in range(len(shape))])
    return level


def centred(stream_key, shape, deviation, most, cuts=(), kind=jnp.bfloat16):
    factor_of = level_of(stream_key, shape, cuts, -0.22, 0.18) if cuts else 1.0
    values = jax.random.normal(stream_key, shape, jnp.float32) * deviation * factor_of
    return jnp.minimum(jnp.maximum(values, -most), most).astype(kind)


def setup_inputs(seed: int = 0, part: int = 0) -> dict:
    splits = jax.random.split(jax.random.key(seed), 11)
    part_keys = jax.random.split(jax.random.fold_in(splits[10], part), 11)
    return {
        "courant": jnp.clip(jnp.exp(math.log(0.05) - 1.609438 * jax.random.uniform(splits[0], (REALS, NX, NY, NZ), jnp.float32) ** level_of(splits[0], (REALS, NX, NY, NZ), ((0, 4), (1, 4)), -0.2, 0.2)), 0.01, 0.05),
        "prev_field": centred(part_keys[1], (REALS, NX, NY, NZ), 1.0, 6.0, ((0, 4), (1, 4)), jnp.float32),
        "cur_field": centred(part_keys[2], (REALS, NX, NY, NZ), 1.0, 6.0, ((0, 4), (1, 4)), jnp.float32),
        "adj_prev": centred(part_keys[3], (REALS, NX, NY, NZ), 1.0, 6.0, ((0, 4), (1, 4)), jnp.float32),
        "adj_cur": centred(part_keys[4], (REALS, NX, NY, NZ), 1.0, 6.0, ((0, 4), (1, 4)), jnp.float32),
        "buoyancy": jnp.clip(jnp.exp(math.log(2.5) - 1.8325814 * jax.random.uniform(splits[5], (NX, NY, NZ), jnp.float32) ** level_of(splits[5], (NX, NY, NZ), ((0, 4),), -0.2, 0.2)), 0.4, 2.5),
        "wavelet": centred(part_keys[6], (STEPS,), 4.0, 16.0, (), jnp.float32),
        "src_cell": jax.random.randint(part_keys[7], (1,), 0, NX * NY * NZ).astype(jnp.int32),
        "rec_cell": plant(jax.random.randint(part_keys[8], (NREC,), 0, NX * NY * NZ), jax.random.fold_in(part_keys[8], 1), 0, (NX * NY * NZ) - 1).astype(jnp.int32),
        "observed": centred(part_keys[9], (STEPS, NREC), 1.0, 6.0, (), jnp.float32),
    }


SECOND = (-205.0 / 72.0, 8.0 / 5.0, -1.0 / 5.0, 8.0 / 315.0, -1.0 / 560.0)
FIRST = (4.0 / 5.0, -1.0 / 5.0, 4.0 / 105.0, -1.0 / 280.0)


def window(padded, axis, shift):
    starts = [4, 4, 4]
    starts[axis] = starts[axis] + shift
    dims = [padded.shape[0] - 8, padded.shape[1] - 8, padded.shape[2] - 8]
    return lax.slice(padded, starts, [starts[0] + dims[0], starts[1] + dims[1], starts[2] + dims[2]])


def stencil(padded):
    centre = window(padded, 0, 0)
    lap = 3.0 * SECOND[0] * centre
    grads = []
    for axis in range(3):
        for k in range(1, 5):
            lap = lap + SECOND[k] * (window(padded, axis, k) + window(padded, axis, -k))
        slope = FIRST[0] * (window(padded, axis, 1) - window(padded, axis, -1))
        for k in range(2, 5):
            slope = slope + FIRST[k - 1] * (window(padded, axis, k) - window(padded, axis, -k))
        grads.append(slope)
    return lap, grads


def operate(padded, buoyancy, grad_b):
    lap, grads = stencil(padded)
    return buoyancy * lap + (grad_b[0] * grads[0] + grad_b[1] * grads[1] + grad_b[2] * grads[2])


def inject(field, cells, values):
    return field.reshape(-1).at[cells].add(values).reshape(field.shape)


def reference(courant, prev_field, cur_field, adj_prev, adj_cur, buoyancy, wavelet, src_cell, rec_cell, observed):
    _, grad_b = stencil(jnp.pad(buoyancy, 4))
    total = jnp.zeros(buoyancy.shape, jnp.float32)
    finals = []
    for r in range(REALS):
        speed = courant[r]
        older, now = prev_field[r], cur_field[r]
        forces = []
        samples = []
        for k in range(STEPS):
            force = operate(jnp.pad(now, 4), buoyancy, grad_b)
            newer = 2.0 * now - older + speed * force
            newer = inject(newer, src_cell, jnp.full((1,), wavelet[k], jnp.float32))
            samples.append(newer.reshape(-1)[rec_cell])
            forces.append(force)
            older, now = now, newer
        residual = jnp.stack(samples) - observed
        older, now = adj_prev[r], adj_cur[r]
        image_r = jnp.zeros(buoyancy.shape, jnp.float32)
        for j in range(STEPS):
            force = operate(jnp.pad(now, 4), buoyancy, grad_b)
            newer = 2.0 * now - older + speed * force
            newer = inject(newer, rec_cell, residual[STEPS - 1 - j])
            image_r = image_r + newer * forces[STEPS - 1 - j]
            older, now = now, newer
        total = total + image_r
        finals.append(now)
    return total / REALS, jnp.stack(finals)
```

```python
import jax
import jax.numpy as jnp
from jax import lax
from jax.sharding import PartitionSpec as P

SECOND = (-205.0 / 72.0, 8.0 / 5.0, -1.0 / 5.0, 8.0 / 315.0, -1.0 / 560.0)
FIRST = (4.0 / 5.0, -1.0 / 5.0, 4.0 / 105.0, -1.0 / 280.0)


def extended(block, sides, width):
    for axis, dim in sides:
        count = lax.axis_size(axis)
        forward = [(i, i + 1) for i in range(count - 1)]
        backward = [(target, source) for source, target in forward]
        low = lax.ppermute(
            lax.slice_in_dim(block, block.shape[dim] - width, None, axis=dim), axis, forward
        )
        high = lax.ppermute(lax.slice_in_dim(block, 0, width, axis=dim), axis, backward)
        block = jnp.concatenate([low, block, high], axis=dim)
    return block


def window(padded, axis, shift):
    starts = [4, 4, 4]
    starts[axis] = starts[axis] + shift
    dims = [padded.shape[0] - 8, padded.shape[1] - 8, padded.shape[2] - 8]
    return lax.slice(
        padded, starts, [starts[0] + dims[0], starts[1] + dims[1], starts[2] + dims[2]]
    )


def stencil(padded):
    centre = window(padded, 0, 0)
    lap = 3.0 * SECOND[0] * centre
    grads = []
    for axis in range(3):
        for k in range(1, 5):
            lap = lap + SECOND[k] * (window(padded, axis, k) + window(padded, axis, -k))
        slope = FIRST[0] * (window(padded, axis, 1) - window(padded, axis, -1))
        for k in range(2, 5):
            slope = slope + FIRST[k - 1] * (window(padded, axis, k) - window(padded, axis, -k))
        grads.append(slope)
    return (lap, grads)


def side_pad(slab):
    return jnp.pad(slab, ((0, 0), (4, 4), (4, 4)))


def operate_slab(field, buoyancy, grad_b):
    padded = side_pad(extended(field, (("tile", 0),), 4))
    lap, grads = stencil(padded)
    return buoyancy * lap + (grad_b[0] * grads[0] + grad_b[1] * grads[1] + grad_b[2] * grads[2])


def inject(field, where, valid, values):
    flat = field.reshape(-1).at[where].add(jnp.where(valid, values, 0.0))
    return flat.reshape(field.shape)


def reduce_members(part, axis):
    members = lax.axis_size(axis)
    if members & (members - 1) or part.size % (members * 1024):
        return lax.psum(part, axis) / members
    me = lax.axis_index(axis)
    rows = part.reshape(-1, 128)
    bits = members.bit_length() - 1
    for b in range(bits):
        mask = 1 << b
        half = rows.shape[0] // 2
        upper = (me // mask) % 2
        keep = lax.dynamic_slice_in_dim(rows, upper * half, half, 0)
        give = lax.dynamic_slice_in_dim(rows, (1 - upper) * half, half, 0)
        pairs = [(i, i ^ mask) for i in range(members)]
        rows = keep + lax.ppermute(give, axis, pairs)
    rows = rows / members
    for b in reversed(range(bits)):
        mask = 1 << b
        upper = (me // mask) % 2
        pairs = [(i, i ^ mask) for i in range(members)]
        other = lax.ppermute(rows, axis, pairs)
        rows = jnp.where(upper == 1, jnp.concatenate([other, rows]), jnp.concatenate([rows, other]))
    return rows.reshape(part.shape)


def shards(
    courant,
    prev_field,
    cur_field,
    adj_prev,
    adj_cur,
    buoyancy,
    wavelet,
    src_cell,
    rec_cell,
    observed,
):
    speed = courant[0]
    planes, height, depth = buoyancy.shape
    volume = planes * height * depth
    offset = lax.axis_index("tile") * volume
    steps = wavelet.shape[0]

    def locate(cells):
        local = cells - offset
        valid = (local >= 0) & (local < volume)
        return (jnp.clip(local, 0, volume - 1), valid)

    src_local, src_valid = locate(src_cell)
    rec_local, rec_valid = locate(rec_cell)
    b_padded = side_pad(extended(buoyancy, (("tile", 0),), 4))
    _, grad_b = stencil(b_padded)
    older, now = (prev_field[0], cur_field[0])
    forces = []
    samples = []
    for k in range(steps):
        force = operate_slab(now, buoyancy, grad_b)
        newer = 2.0 * now - older + speed * force
        newer = inject(newer, src_local, src_valid, jnp.full((1,), wavelet[k], jnp.float32))
        samples.append(jnp.where(rec_valid, newer.reshape(-1)[rec_local], 0.0))
        forces.append(force)
        older, now = (now, newer)
    residual = jnp.where(rec_valid, jnp.stack(samples) - observed, 0.0)
    older, now = (adj_prev[0], adj_cur[0])
    image_part = jnp.zeros(buoyancy.shape, jnp.float32)
    for j in range(steps):
        force = operate_slab(now, buoyancy, grad_b)
        newer = 2.0 * now - older + speed * force
        newer = inject(newer, rec_local, rec_valid, residual[steps - 1 - j])
        image_part = image_part + newer * forces[steps - 1 - j]
        older, now = (now, newer)
    image = reduce_members(image_part, "real")
    return (image, now[None])


def solution(mesh):
    in_specs = (
        P("real", "tile", None, None),
        P(("shot", "real"), "tile", None, None),
        P(("shot", "real"), "tile", None, None),
        P(("shot", "real"), "tile", None, None),
        P(("shot", "real"), "tile", None, None),
        P("tile", None, None),
        P("shot"),
        P("shot"),
        P("shot"),
        P("shot", None),
    )
    out_specs = (P(("shot", "tile"), None, None), P(("shot", "real"), "tile", None, None))
    return jax.shard_map(shards, mesh=mesh, in_specs=in_specs, out_specs=out_specs, check_vma=False)
```

```python
import functools
import jax
import jax.numpy as jnp
from jax import lax
from jax.experimental import pallas as pl
from jax.experimental.pallas import tpu as pltpu
from jax.sharding import PartitionSpec as P

SECOND = (-205.0 / 72.0, 8.0 / 5.0, -1.0 / 5.0, 8.0 / 315.0, -1.0 / 560.0)
FIRST = (4.0 / 5.0, -1.0 / 5.0, 4.0 / 105.0, -1.0 / 280.0)
HALO = 4
PADY = 8


def lane_shift(v, k, lane):
    width = v.shape[-1]
    if k > 0:
        rolled = pltpu.roll(v, width - k, 1)
        return jnp.where(lane < width - k, rolled, 0.0)
    rolled = pltpu.roll(v, -k, 1)
    return jnp.where(lane >= -k, rolled, 0.0)


def fill_padded(pad_ref, lo_ref, mid_ref, hi_ref):
    planes, height, depth = mid_ref.shape
    pad_ref[...] = jnp.zeros(pad_ref.shape, jnp.float32)
    pad_ref[0:HALO, PADY:PADY + height, :] = lo_ref[...]
    pad_ref[HALO:HALO + planes, PADY:PADY + height, :] = mid_ref[...]
    pad_ref[HALO + planes:, PADY:PADY + height, :] = hi_ref[...]


def taps(pad_ref, plane, y0, rows, lane):
    def at(dx, dy):
        return pad_ref[plane + dx, pl.ds(PADY + y0 + dy, rows), :]
    centre = at(0, 0)
    lap = 3.0 * SECOND[0] * centre
    grads = []
    for axis in range(3):
        if axis == 0:
            get = lambda k: at(k, 0)
        elif axis == 1:
            get = lambda k: at(0, k)
        else:
            get = lambda k: lane_shift(centre, k, lane)
        vals = {k: get(k) for k in (1, 2, 3, 4, -1, -2, -3, -4)}
        for k in range(1, 5):
            lap = lap + SECOND[k] * (vals[k] + vals[-k])
        slope = FIRST[0] * (vals[1] - vals[-1])
        for k in range(2, 5):
            slope = slope + FIRST[k - 1] * (vals[k] - vals[-k])
        grads.append(slope)
    return centre, lap, grads


def step_kernel(lo_ref, mid_ref, hi_ref, b_ref, g0_ref, g1_ref, g2_ref, c_ref, old_ref,
                force_ref, new_ref, pad_ref, *, block, rows):
    i = pl.program_id(0)

    @pl.when(i == 0)
    def _():
        fill_padded(pad_ref, lo_ref, mid_ref, hi_ref)

    height = b_ref.shape[1]
    lane = lax.broadcasted_iota(jnp.int32, (rows, b_ref.shape[2]), 1)
    for p in range(block):
        plane = i * block + p + HALO
        for y0 in range(0, height, rows):
            sl = (p, pl.ds(y0, rows), slice(None))
            centre, lap, grads = taps(pad_ref, plane, y0, rows, lane)
            force = b_ref[sl] * lap + (g0_ref[sl] * grads[0] + g1_ref[sl] * grads[1] + g2_ref[sl] * grads[2])
            force_ref[sl] = force
            new_ref[sl] = 2.0 * centre - old_ref[sl] + c_ref[sl] * force


def grad_kernel(lo_ref, mid_ref, hi_ref, g0_ref, g1_ref, g2_ref, pad_ref, *, block, rows):
    i = pl.program_id(0)

    @pl.when(i == 0)
    def _():
        fill_padded(pad_ref, lo_ref, mid_ref, hi_ref)

    height = mid_ref.shape[1]
    lane = lax.broadcasted_iota(jnp.int32, (rows, mid_ref.shape[2]), 1)
    for p in range(block):
        plane = i * block + p + HALO
        for y0 in range(0, height, rows):
            sl = (p, pl.ds(y0, rows), slice(None))
            _, _, grads = taps(pad_ref, plane, y0, rows, lane)
            g0_ref[sl] = grads[0]
            g1_ref[sl] = grads[1]
            g2_ref[sl] = grads[2]


def pick_block(planes):
    for b in (4, 2, 1):
        if planes % b == 0:
            return b


def specs(shape, block):
    planes, height, depth = shape
    full = lambda s: pl.BlockSpec(s, lambda i: (0, 0, 0))
    blk = pl.BlockSpec((block, height, depth), lambda i: (i, 0, 0))
    return full, blk


def apply_step(lo, mid, hi, b, g, c, old, rows=40):
    planes, height, depth = mid.shape
    block = pick_block(planes)
    full, blk = specs(mid.shape, block)
    out = jax.ShapeDtypeStruct(mid.shape, jnp.float32)
    return pl.pallas_call(
        functools.partial(step_kernel, block=block, rows=rows),
        grid=(planes // block,),
        in_specs=[full(lo.shape), full(mid.shape), full(hi.shape)] + [blk] * 6,
        out_specs=[blk, blk],
        out_shape=[out, out],
        scratch_shapes=[pltpu.VMEM((planes + 2 * HALO, height + 2 * PADY, depth), jnp.float32)],
        compiler_params=pltpu.CompilerParams(dimension_semantics=("arbitrary",)),
    )(lo, mid, hi, b, g[0], g[1], g[2], c, old)


def apply_grad(lo, mid, hi, rows=40):
    planes, height, depth = mid.shape
    block = pick_block(planes)
    full, blk = specs(mid.shape, block)
    out = jax.ShapeDtypeStruct(mid.shape, jnp.float32)
    return pl.pallas_call(
        functools.partial(grad_kernel, block=block, rows=rows),
        grid=(planes // block,),
        in_specs=[full(lo.shape), full(mid.shape), full(hi.shape)],
        out_specs=[blk, blk, blk],
        out_shape=[out, out, out],
        scratch_shapes=[pltpu.VMEM((planes + 2 * HALO, height + 2 * PADY, depth), jnp.float32)],
        compiler_params=pltpu.CompilerParams(dimension_semantics=("arbitrary",)),
    )(lo, mid, hi)


def reduce_members(part, axis):
    members = lax.axis_size(axis)
    if members & (members - 1) or part.size % (members * 1024):
        return lax.psum(part, axis) / members
    me = lax.axis_index(axis)
    rows = part.reshape(-1, 128)
    bits = members.bit_length() - 1
    for b in range(bits):
        mask = 1 << b
        half = rows.shape[0] // 2
        upper = (me // mask) % 2
        keep = lax.dynamic_slice_in_dim(rows, upper * half, half, 0)
        give = lax.dynamic_slice_in_dim(rows, (1 - upper) * half, half, 0)
        pairs = [(i, i ^ mask) for i in range(members)]
        rows = keep + lax.ppermute(give, axis, pairs)
    rows = rows / members
    for b in reversed(range(bits)):
        mask = 1 << b
        upper = (me // mask) % 2
        pairs = [(i, i ^ mask) for i in range(members)]
        other = lax.ppermute(rows, axis, pairs)
        rows = jnp.where(upper == 1, jnp.concatenate([other, rows]), jnp.concatenate([rows, other]))
    return rows.reshape(part.shape)


def halos(block, axis):
    count = lax.axis_size(axis)
    forward = [(i, i + 1) for i in range(count - 1)]
    backward = [(target, source) for source, target in forward]
    planes = block.shape[0]
    low = lax.ppermute(block[planes - HALO:], axis, forward)
    high = lax.ppermute(block[:HALO], axis, backward)
    return low, high


def inject(field, where, valid, values):
    flat = field.reshape(-1).at[where].add(jnp.where(valid, values, 0.0))
    return flat.reshape(field.shape)


def shards(
    courant,
    prev_field,
    cur_field,
    adj_prev,
    adj_cur,
    buoyancy,
    wavelet,
    src_cell,
    rec_cell,
    observed,
):
    speed = courant[0]
    planes, height, depth = buoyancy.shape
    volume = planes * height * depth
    offset = lax.axis_index("tile") * volume
    steps = wavelet.shape[0]

    def locate(cells):
        local = cells - offset
        valid = (local >= 0) & (local < volume)
        return (jnp.clip(local, 0, volume - 1), valid)

    src_local, src_valid = locate(src_cell)
    rec_local, rec_valid = locate(rec_cell)
    b_lo, b_hi = halos(buoyancy, "tile")
    grad_b = apply_grad(b_lo, buoyancy, b_hi)
    older, now = (prev_field[0], cur_field[0])
    forces = []
    samples = []
    for k in range(steps):
        lo, hi = halos(now, "tile")
        force, newer = apply_step(lo, now, hi, buoyancy, grad_b, speed, older)
        newer = inject(newer, src_local, src_valid, jnp.full((1,), wavelet[k], jnp.float32))
        samples.append(jnp.where(rec_valid, newer.reshape(-1)[rec_local], 0.0))
        forces.append(force)
        older, now = (now, newer)
    residual = jnp.where(rec_valid, jnp.stack(samples) - observed, 0.0)
    older, now = (adj_prev[0], adj_cur[0])
    image_part = jnp.zeros(buoyancy.shape, jnp.float32)
    for j in range(steps):
        lo, hi = halos(now, "tile")
        _, newer = apply_step(lo, now, hi, buoyancy, grad_b, speed, older)
        newer = inject(newer, rec_local, rec_valid, residual[steps - 1 - j])
        image_part = image_part + newer * forces[steps - 1 - j]
        older, now = (now, newer)
    image = reduce_members(image_part, "real")
    return (image, now[None])


def solution(mesh):
    in_specs = (
        P("real", "tile", None, None),
        P(("shot", "real"), "tile", None, None),
        P(("shot", "real"), "tile", None, None),
        P(("shot", "real"), "tile", None, None),
        P(("shot", "real"), "tile", None, None),
        P("tile", None, None),
        P("shot"),
        P("shot"),
        P("shot"),
        P("shot", None),
    )
    out_specs = (P(("shot", "tile"), None, None), P(("shot", "real"), "tile", None, None))
    return jax.shard_map(shards, mesh=mesh, in_specs=in_specs, out_specs=out_specs, check_vma=False)
```

```python
import functools
import jax
import jax.numpy as jnp
from jax import lax
from jax.experimental import pallas as pl
from jax.experimental.pallas import tpu as pltpu
from jax.sharding import PartitionSpec as P

SECOND = (-205.0 / 72.0, 8.0 / 5.0, -1.0 / 5.0, 8.0 / 315.0, -1.0 / 560.0)
FIRST = (4.0 / 5.0, -1.0 / 5.0, 4.0 / 105.0, -1.0 / 280.0)
HALO = 4
PADY = 8


def lane_shift(v, k, lane):
    width = v.shape[-1]
    if k > 0:
        rolled = pltpu.roll(v, width - k, 1)
        return jnp.where(lane < width - k, rolled, 0.0)
    rolled = pltpu.roll(v, -k, 1)
    return jnp.where(lane >= -k, rolled, 0.0)


def fill_padded(pad_ref, lo_ref, mid_ref, hi_ref):
    planes, height, depth = mid_ref.shape
    pad_ref[...] = jnp.zeros(pad_ref.shape, jnp.float32)
    pad_ref[0:HALO, PADY:PADY + height, :] = lo_ref[...]
    pad_ref[HALO:HALO + planes, PADY:PADY + height, :] = mid_ref[...]
    pad_ref[HALO + planes:, PADY:PADY + height, :] = hi_ref[...]


def taps(pad_ref, plane, y0, rows, lane):
    def at(dx, dy):
        return pad_ref[plane + dx, pl.ds(PADY + y0 + dy, rows), :]
    centre = at(0, 0)
    lap = 3.0 * SECOND[0] * centre
    grads = []
    for axis in range(3):
        if axis == 0:
            get = lambda k: at(k, 0)
        elif axis == 1:
            get = lambda k: at(0, k)
        else:
            get = lambda k: lane_shift(centre, k, lane)
        vals = {k: get(k) for k in (1, 2, 3, 4, -1, -2, -3, -4)}
        for k in range(1, 5):
            lap = lap + SECOND[k] * (vals[k] + vals[-k])
        slope = FIRST[0] * (vals[1] - vals[-1])
        for k in range(2, 5):
            slope = slope + FIRST[k - 1] * (vals[k] - vals[-k])
        grads.append(slope)
    return centre, lap, grads


def step_kernel(*refs, block, rows, inject, edges):
    lo_ref, mid_ref, hi_ref, b_ref, g0_ref, g1_ref, g2_ref, c_ref, old_ref = refs[:9]
    refs = refs[9:]
    if inject:
        where_ref, amount_ref = refs[:2]
        refs = refs[2:]
    force_ref, new_ref = refs[:2]
    refs = refs[2:]
    if edges:
        edge_lo_ref, edge_hi_ref = refs[:2]
        refs = refs[2:]
    (pad_ref,) = refs
    i = pl.program_id(0)

    @pl.when(i == 0)
    def _():
        fill_padded(pad_ref, lo_ref, mid_ref, hi_ref)

    planes = mid_ref.shape[0]
    height = b_ref.shape[1]
    lane = lax.broadcasted_iota(jnp.int32, (rows, b_ref.shape[2]), 1)
    row = lax.broadcasted_iota(jnp.int32, (rows, b_ref.shape[2]), 0)
    for p in range(block):
        plane = i * block + p + HALO
        for y0 in range(0, height, rows):
            sl = (p, pl.ds(y0, rows), slice(None))
            centre, lap, grads = taps(pad_ref, plane, y0, rows, lane)
            force = b_ref[sl] * lap + (g0_ref[sl] * grads[0] + g1_ref[sl] * grads[1] + g2_ref[sl] * grads[2])
            force_ref[sl] = force
            newer = 2.0 * centre - old_ref[sl] + c_ref[sl] * force
            if inject:
                hit = (where_ref[3] == 1) & (where_ref[0] == plane - HALO)
                mask = hit & (row == where_ref[1] - y0) & (lane == where_ref[2])
                newer = jnp.where(mask, newer + amount_ref[0], newer)
            new_ref[sl] = newer
            if edges:
                g = plane - HALO

                @pl.when(g < HALO)
                def _():
                    edge_lo_ref[pl.ds(g, 1), pl.ds(y0, rows), :] = newer[None]

                @pl.when(g >= planes - HALO)
                def _():
                    edge_hi_ref[pl.ds(g - (planes - HALO), 1), pl.ds(y0, rows), :] = newer[None]


def grad_kernel(lo_ref, mid_ref, hi_ref, g0_ref, g1_ref, g2_ref, pad_ref, *, block, rows):
    i = pl.program_id(0)

    @pl.when(i == 0)
    def _():
        fill_padded(pad_ref, lo_ref, mid_ref, hi_ref)

    height = mid_ref.shape[1]
    lane = lax.broadcasted_iota(jnp.int32, (rows, mid_ref.shape[2]), 1)
    for p in range(block):
        plane = i * block + p + HALO
        for y0 in range(0, height, rows):
            sl = (p, pl.ds(y0, rows), slice(None))
            _, _, grads = taps(pad_ref, plane, y0, rows, lane)
            g0_ref[sl] = grads[0]
            g1_ref[sl] = grads[1]
            g2_ref[sl] = grads[2]


def pick_block(planes):
    for b in (4, 2, 1):
        if planes % b == 0:
            return b


def specs(shape, block):
    planes, height, depth = shape
    full = lambda s: pl.BlockSpec(s, lambda i: (0, 0, 0))
    blk = pl.BlockSpec((block, height, depth), lambda i: (i, 0, 0))
    return full, blk


def apply_step(lo, lo_at, mid, hi, hi_at, b, g, c, old, source=None, edges=False, rows=40):
    planes, height, depth = mid.shape
    block = pick_block(planes)
    full, blk = specs(mid.shape, block)
    halo = lambda at: pl.BlockSpec((HALO, height, depth), lambda i: (at, 0, 0))
    out = jax.ShapeDtypeStruct(mid.shape, jnp.float32)
    in_specs = [halo(lo_at), full(mid.shape), halo(hi_at)] + [blk] * 6
    args = [lo, mid, hi, b, g[0], g[1], g[2], c, old]
    if source is not None:
        smem = pl.BlockSpec(memory_space=pltpu.SMEM)
        in_specs += [smem, smem]
        args += list(source)
    out_specs = [blk, blk]
    out_shape = [out, out]
    if edges:
        edge = jax.ShapeDtypeStruct((HALO, height, depth), jnp.float32)
        out_specs += [full(edge.shape), full(edge.shape)]
        out_shape += [edge, edge]
    return pl.pallas_call(
        functools.partial(step_kernel, block=block, rows=rows, inject=source is not None, edges=edges),
        grid=(planes // block,),
        in_specs=in_specs,
        out_specs=out_specs,
        out_shape=out_shape,
        scratch_shapes=[pltpu.VMEM((planes + 2 * HALO, height + 2 * PADY, depth), jnp.float32)],
        compiler_params=pltpu.CompilerParams(dimension_semantics=("arbitrary",)),
    )(*args)


def apply_grad(lo, lo_at, mid, hi, hi_at, rows=40):
    planes, height, depth = mid.shape
    block = pick_block(planes)
    full, blk = specs(mid.shape, block)
    halo = lambda at: pl.BlockSpec((HALO, height, depth), lambda i: (at, 0, 0))
    out = jax.ShapeDtypeStruct(mid.shape, jnp.float32)
    return pl.pallas_call(
        functools.partial(grad_kernel, block=block, rows=rows),
        grid=(planes // block,),
        in_specs=[halo(lo_at), full(mid.shape), halo(hi_at)],
        out_specs=[blk, blk, blk],
        out_shape=[out, out, out],
        scratch_shapes=[pltpu.VMEM((planes + 2 * HALO, height + 2 * PADY, depth), jnp.float32)],
        compiler_params=pltpu.CompilerParams(dimension_semantics=("arbitrary",)),
    )(lo, mid, hi)


def reduce_members(part, axis):
    members = lax.axis_size(axis)
    if members & (members - 1) or part.size % (members * 1024):
        return lax.psum(part, axis) / members
    me = lax.axis_index(axis)
    rows = part.reshape(-1, 128)
    bits = members.bit_length() - 1
    for b in range(bits):
        mask = 1 << b
        half = rows.shape[0] // 2
        upper = (me // mask) % 2
        keep = lax.dynamic_slice_in_dim(rows, upper * half, half, 0)
        give = lax.dynamic_slice_in_dim(rows, (1 - upper) * half, half, 0)
        pairs = [(i, i ^ mask) for i in range(members)]
        rows = keep + lax.ppermute(give, axis, pairs)
    rows = rows / members
    for b in reversed(range(bits)):
        mask = 1 << b
        upper = (me // mask) % 2
        pairs = [(i, i ^ mask) for i in range(members)]
        other = lax.ppermute(rows, axis, pairs)
        rows = jnp.where(upper == 1, jnp.concatenate([other, rows]), jnp.concatenate([rows, other]))
    return rows.reshape(part.shape)


def halos(blocks, axis):
    count = lax.axis_size(axis)
    forward = [(i, i + 1) for i in range(count - 1)]
    backward = [(target, source) for source, target in forward]
    planes = blocks[0].shape[0]
    tops = jnp.concatenate([block[planes - HALO:] for block in blocks])
    bottoms = jnp.concatenate([block[:HALO] for block in blocks])
    return lax.ppermute(tops, axis, forward), lax.ppermute(bottoms, axis, backward)


def edge_halos(low_edge, high_edge, axis):
    count = lax.axis_size(axis)
    forward = [(i, i + 1) for i in range(count - 1)]
    backward = [(target, source) for source, target in forward]
    return lax.ppermute(high_edge, axis, forward), lax.ppermute(low_edge, axis, backward)


def inject(field, where, valid, values):
    flat = field.reshape(-1).at[where].add(jnp.where(valid, values, 0.0))
    return flat.reshape(field.shape)


def shards(
    courant,
    prev_field,
    cur_field,
    adj_prev,
    adj_cur,
    buoyancy,
    wavelet,
    src_cell,
    rec_cell,
    observed,
):
    speed = courant[0]
    planes, height, depth = buoyancy.shape
    volume = planes * height * depth
    offset = lax.axis_index("tile") * volume
    steps = wavelet.shape[0]

    def locate(cells):
        local = cells - offset
        valid = (local >= 0) & (local < volume)
        return (jnp.clip(local, 0, volume - 1), valid)

    src_local, src_valid = locate(src_cell)
    rec_local, rec_valid = locate(rec_cell)
    first_lo, first_hi = halos([buoyancy, cur_field[0], adj_cur[0]], "tile")
    grad_b = apply_grad(first_lo, 0, buoyancy, first_hi, 0)
    sx = src_local // (height * depth)
    sy = (src_local // depth) % height
    sz = src_local % depth
    where = jnp.concatenate([sx, sy, sz, src_valid.astype(jnp.int32)])
    older, now = (prev_field[0], cur_field[0])
    lo, lo_at, hi, hi_at = first_lo, 1, first_hi, 1
    forces = []
    samples = []
    for k in range(steps):
        source = (where, wavelet[k:k + 1])
        outs = apply_step(lo, lo_at, now, hi, hi_at, buoyancy, grad_b, speed, older, source, edges=k + 1 < steps)
        force, newer = outs[:2]
        if k + 1 < steps:
            lo, hi = edge_halos(outs[2], outs[3], "tile")
            lo_at, hi_at = 0, 0
        samples.append(jnp.where(rec_valid, newer.reshape(-1)[rec_local], 0.0))
        forces.append(force)
        older, now = (now, newer)
    residual = jnp.where(rec_valid, jnp.stack(samples) - observed, 0.0)
    older, now = (adj_prev[0], adj_cur[0])
    lo, lo_at, hi, hi_at = first_lo, 2, first_hi, 2
    image_part = jnp.zeros(buoyancy.shape, jnp.float32)
    for j in range(steps):
        if j > 0:
            (lo, hi), lo_at, hi_at = halos([now], "tile"), 0, 0
        _, newer = apply_step(lo, lo_at, now, hi, hi_at, buoyancy, grad_b, speed, older)
        newer = inject(newer, rec_local, rec_valid, residual[steps - 1 - j])
        image_part = image_part + newer * forces[steps - 1 - j]
        older, now = (now, newer)
    image = reduce_members(image_part, "real")
    return (image, now[None])


def solution(mesh):
    in_specs = (
        P("real", "tile", None, None),
        P(("shot", "real"), "tile", None, None),
        P(("shot", "real"), "tile", None, None),
        P(("shot", "real"), "tile", None, None),
        P(("shot", "real"), "tile", None, None),
        P("tile", None, None),
        P("shot"),
        P("shot"),
        P("shot"),
        P("shot", None),
    )
    out_specs = (P(("shot", "tile"), None, None), P(("shot", "real"), "tile", None, None))
    return jax.shard_map(shards, mesh=mesh, in_specs=in_specs, out_specs=out_specs, check_vma=False)
```

```python
import functools
import jax
import jax.numpy as jnp
from jax import lax
from jax.experimental import pallas as pl
from jax.experimental.pallas import tpu as pltpu
from jax.sharding import PartitionSpec as P

SECOND = (-205.0 / 72.0, 8.0 / 5.0, -1.0 / 5.0, 8.0 / 315.0, -1.0 / 560.0)
FIRST = (4.0 / 5.0, -1.0 / 5.0, 4.0 / 105.0, -1.0 / 280.0)
HALO = 4
PADY = 8


def lane_shift(v, k, lane):
    width = v.shape[-1]
    if k > 0:
        rolled = pltpu.roll(v, width - k, 1)
        return jnp.where(lane < width - k, rolled, 0.0)
    rolled = pltpu.roll(v, -k, 1)
    return jnp.where(lane >= -k, rolled, 0.0)


def fill_padded(pad_ref, lo_ref, mid_ref, hi_ref):
    planes, height, depth = mid_ref.shape
    pad_ref[...] = jnp.zeros(pad_ref.shape, jnp.float32)
    pad_ref[0:HALO, PADY:PADY + height, :] = lo_ref[...]
    pad_ref[HALO:HALO + planes, PADY:PADY + height, :] = mid_ref[...]
    pad_ref[HALO + planes:, PADY:PADY + height, :] = hi_ref[...]


def taps(pad_ref, plane, y0, rows, lane):
    def at(dx, dy):
        return pad_ref[plane + dx, pl.ds(PADY + y0 + dy, rows), :]
    centre = at(0, 0)
    lap = 3.0 * SECOND[0] * centre
    grads = []
    for axis in range(3):
        if axis == 0:
            get = lambda k: at(k, 0)
        elif axis == 1:
            get = lambda k: at(0, k)
        else:
            get = lambda k: lane_shift(centre, k, lane)
        vals = {k: get(k) for k in (1, 2, 3, 4, -1, -2, -3, -4)}
        for k in range(1, 5):
            lap = lap + SECOND[k] * (vals[k] + vals[-k])
        slope = FIRST[0] * (vals[1] - vals[-1])
        for k in range(2, 5):
            slope = slope + FIRST[k - 1] * (vals[k] - vals[-k])
        grads.append(slope)
    return centre, lap, grads


def step_kernel(*refs, block, rows, track):
    lo_ref, mid_ref, hi_ref, b_ref, g0_ref, g1_ref, g2_ref, c_ref, old_ref = refs[:9]
    if track:
        where_ref, amount_ref, rec_ref = refs[9:12]
        force_ref, new_ref, edge_lo_ref, edge_hi_ref, sample_ref, pad_ref, keep_ref = refs[12:]
    else:
        force_ref, new_ref, pad_ref = refs[9:]
    i = pl.program_id(0)

    @pl.when(i == 0)
    def _():
        fill_padded(pad_ref, lo_ref, mid_ref, hi_ref)

    planes = mid_ref.shape[0]
    height = b_ref.shape[1]
    depth = b_ref.shape[2]
    lane = lax.broadcasted_iota(jnp.int32, (rows, depth), 1)
    row = lax.broadcasted_iota(jnp.int32, (rows, depth), 0)
    for p in range(block):
        plane = i * block + p + HALO
        for y0 in range(0, height, rows):
            sl = (p, pl.ds(y0, rows), slice(None))
            centre, lap, grads = taps(pad_ref, plane, y0, rows, lane)
            force = b_ref[sl] * lap + (g0_ref[sl] * grads[0] + g1_ref[sl] * grads[1] + g2_ref[sl] * grads[2])
            force_ref[sl] = force
            newer = 2.0 * centre - old_ref[sl] + c_ref[sl] * force
            if track:
                hit = (where_ref[3] == 1) & (where_ref[0] == plane - HALO)
                mask = hit & (row == where_ref[1] - y0) & (lane == where_ref[2])
                newer = jnp.where(mask, newer + amount_ref[0], newer)
                keep_ref[plane - HALO, pl.ds(y0, rows), :] = newer
            new_ref[sl] = newer

    if track:
        @pl.when(i == pl.num_programs(0) - 1)
        def _():
            edge_lo_ref[...] = keep_ref[0:HALO]
            edge_hi_ref[...] = keep_ref[planes - HALO:planes]
            one_lane = lax.broadcasted_iota(jnp.int32, (1, depth), 1)

            def sample(r, carry):
                x = rec_ref[0, r]
                y = rec_ref[1, r]
                z = rec_ref[2, r]
                line = keep_ref[x, pl.ds(y, 1), :]
                sample_ref[pl.ds(r, 1), :] = jnp.where(one_lane == z, line, 0.0)
                return carry

            lax.fori_loop(0, sample_ref.shape[0], sample, 0, unroll=8)


def grad_kernel(lo_ref, mid_ref, hi_ref, g0_ref, g1_ref, g2_ref, pad_ref, *, block, rows):
    i = pl.program_id(0)

    @pl.when(i == 0)
    def _():
        fill_padded(pad_ref, lo_ref, mid_ref, hi_ref)

    height = mid_ref.shape[1]
    lane = lax.broadcasted_iota(jnp.int32, (rows, mid_ref.shape[2]), 1)
    for p in range(block):
        plane = i * block + p + HALO
        for y0 in range(0, height, rows):
            sl = (p, pl.ds(y0, rows), slice(None))
            _, _, grads = taps(pad_ref, plane, y0, rows, lane)
            g0_ref[sl] = grads[0]
            g1_ref[sl] = grads[1]
            g2_ref[sl] = grads[2]


def pick_block(planes):
    for b in (4, 2, 1):
        if planes % b == 0:
            return b


def specs(shape, block):
    planes, height, depth = shape
    full = lambda s: pl.BlockSpec(s, lambda i: (0, 0, 0))
    blk = pl.BlockSpec((block, height, depth), lambda i: (i, 0, 0))
    return full, blk


def apply_step(lo, mid, hi, b, g, c, old, track=None, rows=40):
    planes, height, depth = mid.shape
    block = pick_block(planes)
    full, blk = specs(mid.shape, block)
    out = jax.ShapeDtypeStruct(mid.shape, jnp.float32)
    in_specs = [full(lo.shape), full(mid.shape), full(hi.shape)] + [blk] * 6
    args = [lo, mid, hi, b, g[0], g[1], g[2], c, old]
    out_specs = [blk, blk]
    out_shape = [out, out]
    scratch = [pltpu.VMEM((planes + 2 * HALO, height + 2 * PADY, depth), jnp.float32)]
    if track is not None:
        smem = pl.BlockSpec(memory_space=pltpu.SMEM)
        in_specs += [smem, smem, smem]
        args += list(track)
        count = track[2].shape[1]
        edge = jax.ShapeDtypeStruct((HALO, height, depth), jnp.float32)
        lines = jax.ShapeDtypeStruct((count, depth), jnp.float32)
        out_specs += [full(edge.shape), full(edge.shape), pl.BlockSpec((count, depth), lambda i: (0, 0))]
        out_shape += [edge, edge, lines]
        scratch.append(pltpu.VMEM(mid.shape, jnp.float32))
    return pl.pallas_call(
        functools.partial(step_kernel, block=block, rows=rows, track=track is not None),
        grid=(planes // block,),
        in_specs=in_specs,
        out_specs=out_specs,
        out_shape=out_shape,
        scratch_shapes=scratch,
        compiler_params=pltpu.CompilerParams(dimension_semantics=("arbitrary",)),
    )(*args)


def apply_grad(lo, mid, hi, rows=40):
    planes, height, depth = mid.shape
    block = pick_block(planes)
    full, blk = specs(mid.shape, block)
    out = jax.ShapeDtypeStruct(mid.shape, jnp.float32)
    return pl.pallas_call(
        functools.partial(grad_kernel, block=block, rows=rows),
        grid=(planes // block,),
        in_specs=[full(lo.shape), full(mid.shape), full(hi.shape)],
        out_specs=[blk, blk, blk],
        out_shape=[out, out, out],
        scratch_shapes=[pltpu.VMEM((planes + 2 * HALO, height + 2 * PADY, depth), jnp.float32)],
        compiler_params=pltpu.CompilerParams(dimension_semantics=("arbitrary",)),
    )(lo, mid, hi)


def reduce_members(part, axis):
    members = lax.axis_size(axis)
    if members & (members - 1) or part.size % (members * 1024):
        return lax.psum(part, axis) / members
    me = lax.axis_index(axis)
    rows = part.reshape(-1, 128)
    bits = members.bit_length() - 1
    for b in range(bits):
        mask = 1 << b
        half = rows.shape[0] // 2
        upper = (me // mask) % 2
        keep = lax.dynamic_slice_in_dim(rows, upper * half, half, 0)
        give = lax.dynamic_slice_in_dim(rows, (1 - upper) * half, half, 0)
        pairs = [(i, i ^ mask) for i in range(members)]
        rows = keep + lax.ppermute(give, axis, pairs)
    rows = rows / members
    for b in reversed(range(bits)):
        mask = 1 << b
        upper = (me // mask) % 2
        pairs = [(i, i ^ mask) for i in range(members)]
        other = lax.ppermute(rows, axis, pairs)
        rows = jnp.where(upper == 1, jnp.concatenate([other, rows]), jnp.concatenate([rows, other]))
    return rows.reshape(part.shape)


def halos(block, axis):
    count = lax.axis_size(axis)
    forward = [(i, i + 1) for i in range(count - 1)]
    backward = [(target, source) for source, target in forward]
    planes = block.shape[0]
    low = lax.ppermute(block[planes - HALO:], axis, forward)
    high = lax.ppermute(block[:HALO], axis, backward)
    return low, high


def edge_halos(low_edge, high_edge, axis):
    count = lax.axis_size(axis)
    forward = [(i, i + 1) for i in range(count - 1)]
    backward = [(target, source) for source, target in forward]
    return lax.ppermute(high_edge, axis, forward), lax.ppermute(low_edge, axis, backward)


def inject(field, where, valid, values):
    flat = field.reshape(-1).at[where].add(jnp.where(valid, values, 0.0))
    return flat.reshape(field.shape)


def shards(
    courant,
    prev_field,
    cur_field,
    adj_prev,
    adj_cur,
    buoyancy,
    wavelet,
    src_cell,
    rec_cell,
    observed,
):
    speed = courant[0]
    planes, height, depth = buoyancy.shape
    volume = planes * height * depth
    offset = lax.axis_index("tile") * volume
    steps = wavelet.shape[0]

    def locate(cells):
        local = cells - offset
        valid = (local >= 0) & (local < volume)
        return (jnp.clip(local, 0, volume - 1), valid)

    src_local, src_valid = locate(src_cell)
    rec_local, rec_valid = locate(rec_cell)
    b_lo, b_hi = halos(buoyancy, "tile")
    grad_b = apply_grad(b_lo, buoyancy, b_hi)

    def spread(cells):
        return jnp.stack([cells // (height * depth), (cells // depth) % height, cells % depth])

    where = jnp.concatenate([spread(src_local)[:, 0], src_valid.astype(jnp.int32)])
    receivers = spread(rec_local)
    older, now = (prev_field[0], cur_field[0])
    lo, hi = halos(now, "tile")
    forces = []
    samples = []
    for k in range(steps):
        track = (where, wavelet[k:k + 1], receivers)
        force, newer, edge_lo, edge_hi, lines = apply_step(lo, now, hi, buoyancy, grad_b, speed, older, track)
        if k + 1 < steps:
            lo, hi = edge_halos(edge_lo, edge_hi, "tile")
        samples.append(jnp.sum(lines, axis=1))
        forces.append(force)
        older, now = (now, newer)
    residual = jnp.where(rec_valid, jnp.stack(samples) - observed, 0.0)
    older, now = (adj_prev[0], adj_cur[0])
    image_part = jnp.zeros(buoyancy.shape, jnp.float32)
    for j in range(steps):
        lo, hi = halos(now, "tile")
        _, newer = apply_step(lo, now, hi, buoyancy, grad_b, speed, older)
        newer = inject(newer, rec_local, rec_valid, residual[steps - 1 - j])
        image_part = image_part + newer * forces[steps - 1 - j]
        older, now = (now, newer)
    image = reduce_members(image_part, "real")
    return (image, now[None])


def solution(mesh):
    in_specs = (
        P("real", "tile", None, None),
        P(("shot", "real"), "tile", None, None),
        P(("shot", "real"), "tile", None, None),
        P(("shot", "real"), "tile", None, None),
        P(("shot", "real"), "tile", None, None),
        P("tile", None, None),
        P("shot"),
        P("shot"),
        P("shot"),
        P("shot", None),
    )
    out_specs = (P(("shot", "tile"), None, None), P(("shot", "real"), "tile", None, None))
    return jax.shard_map(shards, mesh=mesh, in_specs=in_specs, out_specs=out_specs, check_vma=False)
```

```python
import functools
import jax
import jax.numpy as jnp
from jax import lax
from jax.experimental import pallas as pl
from jax.experimental.pallas import tpu as pltpu
from jax.sharding import PartitionSpec as P

SECOND = (-205.0 / 72.0, 8.0 / 5.0, -1.0 / 5.0, 8.0 / 315.0, -1.0 / 560.0)
FIRST = (4.0 / 5.0, -1.0 / 5.0, 4.0 / 105.0, -1.0 / 280.0)
HALO = 4
PADY = 8


def lane_shift(v, k, lane):
    width = v.shape[-1]
    if k > 0:
        rolled = pltpu.roll(v, width - k, 1)
        return jnp.where(lane < width - k, rolled, 0.0)
    rolled = pltpu.roll(v, -k, 1)
    return jnp.where(lane >= -k, rolled, 0.0)


def fill_padded(pad_ref, lo_ref, mid_ref, hi_ref):
    planes, height, depth = mid_ref.shape
    pad_ref[...] = jnp.zeros(pad_ref.shape, jnp.float32)
    pad_ref[0:HALO, PADY:PADY + height, :] = lo_ref[...]
    pad_ref[HALO:HALO + planes, PADY:PADY + height, :] = mid_ref[...]
    pad_ref[HALO + planes:, PADY:PADY + height, :] = hi_ref[...]


def taps(pad_ref, plane, y0, rows, lane):
    def at(dx, dy):
        return pad_ref[plane + dx, pl.ds(PADY + y0 + dy, rows), :]
    centre = at(0, 0)
    lap = 3.0 * SECOND[0] * centre
    grads = []
    for axis in range(3):
        if axis == 0:
            get = lambda k: at(k, 0)
        elif axis == 1:
            get = lambda k: at(0, k)
        else:
            get = lambda k: lane_shift(centre, k, lane)
        vals = {k: get(k) for k in (1, 2, 3, 4, -1, -2, -3, -4)}
        for k in range(1, 5):
            lap = lap + SECOND[k] * (vals[k] + vals[-k])
        slope = FIRST[0] * (vals[1] - vals[-1])
        for k in range(2, 5):
            slope = slope + FIRST[k - 1] * (vals[k] - vals[-k])
        grads.append(slope)
    return centre, lap, grads


def step_kernel(*refs, block, rows, track, own_grad, want_force):
    refs = list(refs)
    take = lambda n: [refs.pop(0) for _ in range(n)]
    lo_ref, mid_ref, hi_ref = take(3)
    if own_grad:
        b_lo_ref, b_mid_ref, b_hi_ref = take(3)
    else:
        b_ref, g0_ref, g1_ref, g2_ref = take(4)
    c_ref, old_ref = take(2)
    if track:
        where_ref, amount_ref, rec_ref = take(3)
    force_ref = take(1)[0] if want_force else None
    (new_ref,) = take(1)
    if own_grad:
        g_out = take(3)
    if track:
        edge_lo_ref, edge_hi_ref, sample_ref = take(3)
    (pad_ref,) = take(1)
    if own_grad:
        (b_pad_ref,) = take(1)
    if track:
        (keep_ref,) = take(1)
    i = pl.program_id(0)

    @pl.when(i == 0)
    def _():
        fill_padded(pad_ref, lo_ref, mid_ref, hi_ref)
        if own_grad:
            fill_padded(b_pad_ref, b_lo_ref, b_mid_ref, b_hi_ref)

    planes = mid_ref.shape[0]
    height = c_ref.shape[1]
    depth = c_ref.shape[2]
    lane = lax.broadcasted_iota(jnp.int32, (rows, depth), 1)
    row = lax.broadcasted_iota(jnp.int32, (rows, depth), 0)
    for p in range(block):
        plane = i * block + p + HALO
        for y0 in range(0, height, rows):
            sl = (p, pl.ds(y0, rows), slice(None))
            centre, lap, grads = taps(pad_ref, plane, y0, rows, lane)
            if own_grad:
                bvals, _, gb = taps(b_pad_ref, plane, y0, rows, lane)
                for out_ref, value in zip(g_out, gb):
                    out_ref[sl] = value
            else:
                bvals = b_ref[sl]
                gb = [g0_ref[sl], g1_ref[sl], g2_ref[sl]]
            force = bvals * lap + (gb[0] * grads[0] + gb[1] * grads[1] + gb[2] * grads[2])
            if want_force:
                force_ref[sl] = force
            newer = 2.0 * centre - old_ref[sl] + c_ref[sl] * force
            if track:
                hit = (where_ref[3] == 1) & (where_ref[0] == plane - HALO)
                mask = hit & (row == where_ref[1] - y0) & (lane == where_ref[2])
                newer = jnp.where(mask, newer + amount_ref[0], newer)
                keep_ref[plane - HALO, pl.ds(y0, rows), :] = newer
            new_ref[sl] = newer

    if track:
        @pl.when(i == pl.num_programs(0) - 1)
        def _():
            edge_lo_ref[...] = keep_ref[0:HALO]
            edge_hi_ref[...] = keep_ref[planes - HALO:planes]
            one_lane = lax.broadcasted_iota(jnp.int32, (1, depth), 1)

            def sample(r, carry):
                x = rec_ref[0, r]
                y = rec_ref[1, r]
                z = rec_ref[2, r]
                line = keep_ref[x, pl.ds(y, 1), :]
                sample_ref[pl.ds(r, 1), :] = jnp.where(one_lane == z, line, 0.0)
                return carry

            lax.fori_loop(0, sample_ref.shape[0], sample, 0, unroll=8)


def grad_kernel(lo_ref, mid_ref, hi_ref, g0_ref, g1_ref, g2_ref, pad_ref, *, block, rows):
    i = pl.program_id(0)

    @pl.when(i == 0)
    def _():
        fill_padded(pad_ref, lo_ref, mid_ref, hi_ref)

    height = mid_ref.shape[1]
    lane = lax.broadcasted_iota(jnp.int32, (rows, mid_ref.shape[2]), 1)
    for p in range(block):
        plane = i * block + p + HALO
        for y0 in range(0, height, rows):
            sl = (p, pl.ds(y0, rows), slice(None))
            _, _, grads = taps(pad_ref, plane, y0, rows, lane)
            g0_ref[sl] = grads[0]
            g1_ref[sl] = grads[1]
            g2_ref[sl] = grads[2]


def pick_block(planes):
    for b in (4, 2, 1):
        if planes % b == 0:
            return b


def specs(shape, block):
    planes, height, depth = shape
    full = lambda s: pl.BlockSpec(s, lambda i: (0, 0, 0))
    blk = pl.BlockSpec((block, height, depth), lambda i: (i, 0, 0))
    return full, blk


def apply_step(lo, mid, hi, b, g, c, old, track=None, rows=40, want_force=True):
    planes, height, depth = mid.shape
    block = pick_block(planes)
    full, blk = specs(mid.shape, block)
    out = jax.ShapeDtypeStruct(mid.shape, jnp.float32)
    own_grad = g is None
    in_specs = [full(lo.shape), full(mid.shape), full(hi.shape)]
    args = [lo, mid, hi]
    if own_grad:
        in_specs += [full(b[0].shape), full(b[1].shape), full(b[2].shape)]
        args += list(b)
    else:
        in_specs += [blk] * 4
        args += [b, g[0], g[1], g[2]]
    in_specs += [blk, blk]
    args += [c, old]
    out_specs = [blk] if want_force else []
    out_shape = [out] if want_force else []
    out_specs.append(blk)
    out_shape.append(out)
    if own_grad:
        out_specs += [blk] * 3
        out_shape += [out] * 3
    scratch = [pltpu.VMEM((planes + 2 * HALO, height + 2 * PADY, depth), jnp.float32)]
    if own_grad:
        scratch.append(pltpu.VMEM((planes + 2 * HALO, height + 2 * PADY, depth), jnp.float32))
    if track is not None:
        smem = pl.BlockSpec(memory_space=pltpu.SMEM)
        in_specs += [smem, smem, smem]
        args += list(track)
        count = track[2].shape[1]
        edge = jax.ShapeDtypeStruct((HALO, height, depth), jnp.float32)
        lines = jax.ShapeDtypeStruct((count, depth), jnp.float32)
        out_specs += [full(edge.shape), full(edge.shape), pl.BlockSpec((count, depth), lambda i: (0, 0))]
        out_shape += [edge, edge, lines]
        scratch.append(pltpu.VMEM(mid.shape, jnp.float32))
    kernel = functools.partial(
        step_kernel, block=block, rows=rows, track=track is not None, own_grad=own_grad, want_force=want_force
    )
    return pl.pallas_call(
        kernel,
        grid=(planes // block,),
        in_specs=in_specs,
        out_specs=out_specs,
        out_shape=out_shape,
        scratch_shapes=scratch,
        compiler_params=pltpu.CompilerParams(dimension_semantics=("arbitrary",)),
    )(*args)


def apply_grad(lo, mid, hi, rows=40):
    planes, height, depth = mid.shape
    block = pick_block(planes)
    full, blk = specs(mid.shape, block)
    out = jax.ShapeDtypeStruct(mid.shape, jnp.float32)
    return pl.pallas_call(
        functools.partial(grad_kernel, block=block, rows=rows),
        grid=(planes // block,),
        in_specs=[full(lo.shape), full(mid.shape), full(hi.shape)],
        out_specs=[blk, blk, blk],
        out_shape=[out, out, out],
        scratch_shapes=[pltpu.VMEM((planes + 2 * HALO, height + 2 * PADY, depth), jnp.float32)],
        compiler_params=pltpu.CompilerParams(dimension_semantics=("arbitrary",)),
    )(lo, mid, hi)


def reduce_members(part, axis):
    members = lax.axis_size(axis)
    if members & (members - 1) or part.size % (members * 1024):
        return lax.psum(part, axis) / members
    me = lax.axis_index(axis)
    rows = part.reshape(-1, 128)
    bits = members.bit_length() - 1
    for b in range(bits):
        mask = 1 << b
        half = rows.shape[0] // 2
        upper = (me // mask) % 2
        keep = lax.dynamic_slice_in_dim(rows, upper * half, half, 0)
        give = lax.dynamic_slice_in_dim(rows, (1 - upper) * half, half, 0)
        pairs = [(i, i ^ mask) for i in range(members)]
        rows = keep + lax.ppermute(give, axis, pairs)
    rows = rows / members
    for b in reversed(range(bits)):
        mask = 1 << b
        upper = (me // mask) % 2
        pairs = [(i, i ^ mask) for i in range(members)]
        other = lax.ppermute(rows, axis, pairs)
        rows = jnp.where(upper == 1, jnp.concatenate([other, rows]), jnp.concatenate([rows, other]))
    return rows.reshape(part.shape)


def halos(block, axis):
    count = lax.axis_size(axis)
    forward = [(i, i + 1) for i in range(count - 1)]
    backward = [(target, source) for source, target in forward]
    planes = block.shape[0]
    low = lax.ppermute(block[planes - HALO:], axis, forward)
    high = lax.ppermute(block[:HALO], axis, backward)
    return low, high


def edge_halos(low_edge, high_edge, axis):
    count = lax.axis_size(axis)
    forward = [(i, i + 1) for i in range(count - 1)]
    backward = [(target, source) for source, target in forward]
    return lax.ppermute(high_edge, axis, forward), lax.ppermute(low_edge, axis, backward)


def inject(field, where, valid, values):
    flat = field.reshape(-1).at[where].add(jnp.where(valid, values, 0.0))
    return flat.reshape(field.shape)


def shards(
    courant,
    prev_field,
    cur_field,
    adj_prev,
    adj_cur,
    buoyancy,
    wavelet,
    src_cell,
    rec_cell,
    observed,
):
    speed = courant[0]
    planes, height, depth = buoyancy.shape
    volume = planes * height * depth
    offset = lax.axis_index("tile") * volume
    steps = wavelet.shape[0]

    def locate(cells):
        local = cells - offset
        valid = (local >= 0) & (local < volume)
        return (jnp.clip(local, 0, volume - 1), valid)

    src_local, src_valid = locate(src_cell)
    rec_local, rec_valid = locate(rec_cell)
    b_lo, b_hi = halos(buoyancy, "tile")

    def spread(cells):
        return jnp.stack([cells // (height * depth), (cells // depth) % height, cells % depth])

    where = jnp.concatenate([spread(src_local)[:, 0], src_valid.astype(jnp.int32)])
    receivers = spread(rec_local)
    older, now = (prev_field[0], cur_field[0])
    lo, hi = halos(now, "tile")
    forces = []
    samples = []
    grad_b = None
    for k in range(steps):
        track = (where, wavelet[k:k + 1], receivers)
        if grad_b is None:
            outs = apply_step(lo, now, hi, (b_lo, buoyancy, b_hi), None, speed, older, track)
            force, newer = outs[:2]
            grad_b = outs[2:5]
            edge_lo, edge_hi, lines = outs[5:]
        else:
            force, newer, edge_lo, edge_hi, lines = apply_step(lo, now, hi, buoyancy, grad_b, speed, older, track)
        if k + 1 < steps:
            lo, hi = edge_halos(edge_lo, edge_hi, "tile")
        samples.append(jnp.sum(lines, axis=1))
        forces.append(force)
        older, now = (now, newer)
    residual = jnp.where(rec_valid, jnp.stack(samples) - observed, 0.0)
    older, now = (adj_prev[0], adj_cur[0])
    image_part = jnp.zeros(buoyancy.shape, jnp.float32)
    for j in range(steps):
        lo, hi = halos(now, "tile")
        (newer,) = apply_step(lo, now, hi, buoyancy, grad_b, speed, older, want_force=False)
        newer = inject(newer, rec_local, rec_valid, residual[steps - 1 - j])
        image_part = image_part + newer * forces[steps - 1 - j]
        older, now = (now, newer)
    image = reduce_members(image_part, "real")
    return (image, now[None])


def solution(mesh):
    in_specs = (
        P("real", "tile", None, None),
        P(("shot", "real"), "tile", None, None),
        P(("shot", "real"), "tile", None, None),
        P(("shot", "real"), "tile", None, None),
        P(("shot", "real"), "tile", None, None),
        P("tile", None, None),
        P("shot"),
        P("shot"),
        P("shot"),
        P("shot", None),
    )
    out_specs = (P(("shot", "tile"), None, None), P(("shot", "real"), "tile", None, None))
    return jax.shard_map(shards, mesh=mesh, in_specs=in_specs, out_specs=out_specs, check_vma=False)
```

```python
import functools
import jax
import jax.numpy as jnp
from jax import lax
from jax.experimental import pallas as pl
from jax.experimental.pallas import tpu as pltpu
from jax.sharding import PartitionSpec as P

SECOND = (-205.0 / 72.0, 8.0 / 5.0, -1.0 / 5.0, 8.0 / 315.0, -1.0 / 560.0)
FIRST = (4.0 / 5.0, -1.0 / 5.0, 4.0 / 105.0, -1.0 / 280.0)
HALO = 4
PADY = 8


def lane_shift(v, k, lane):
    width = v.shape[-1]
    if k > 0:
        rolled = pltpu.roll(v, width - k, 1)
        return jnp.where(lane < width - k, rolled, 0.0)
    rolled = pltpu.roll(v, -k, 1)
    return jnp.where(lane >= -k, rolled, 0.0)


def fill_padded(pad_ref, lo_ref, mid_ref, hi_ref):
    planes, height, depth = mid_ref.shape
    pad_ref[...] = jnp.zeros(pad_ref.shape, jnp.float32)
    pad_ref[0:HALO, PADY:PADY + height, :] = lo_ref[...]
    pad_ref[HALO:HALO + planes, PADY:PADY + height, :] = mid_ref[...]
    pad_ref[HALO + planes:, PADY:PADY + height, :] = hi_ref[...]


def taps(pad_ref, plane, y0, rows, lane):
    def at(dx, dy):
        return pad_ref[plane + dx, pl.ds(PADY + y0 + dy, rows), :]
    centre = at(0, 0)
    lap = 3.0 * SECOND[0] * centre
    grads = []
    for axis in range(3):
        if axis == 0:
            get = lambda k: at(k, 0)
        elif axis == 1:
            get = lambda k: at(0, k)
        else:
            get = lambda k: lane_shift(centre, k, lane)
        vals = {k: get(k) for k in (1, 2, 3, 4, -1, -2, -3, -4)}
        for k in range(1, 5):
            lap = lap + SECOND[k] * (vals[k] + vals[-k])
        slope = FIRST[0] * (vals[1] - vals[-1])
        for k in range(2, 5):
            slope = slope + FIRST[k - 1] * (vals[k] - vals[-k])
        grads.append(slope)
    return centre, lap, grads


def step_kernel(*refs, block, rows, track, own_grad, want_force):
    refs = list(refs)
    take = lambda n: [refs.pop(0) for _ in range(n)]
    lo_ref, mid_ref, hi_ref = take(3)
    if own_grad:
        b_lo_ref, b_mid_ref, b_hi_ref = take(3)
    else:
        b_ref, g0_ref, g1_ref, g2_ref = take(4)
    c_ref, old_ref = take(2)
    if track:
        where_ref, amount_ref, rec_ref = take(3)
    force_ref = take(1)[0] if want_force else None
    (new_ref,) = take(1)
    if own_grad:
        g_out = take(3)
    if track:
        edge_lo_ref, edge_hi_ref, sample_ref = take(3)
    (pad_ref,) = take(1)
    if own_grad:
        (b_pad_ref,) = take(1)
    if track:
        (keep_ref,) = take(1)
    i = pl.program_id(0)

    @pl.when(i == 0)
    def _():
        fill_padded(pad_ref, lo_ref, mid_ref, hi_ref)
        if own_grad:
            fill_padded(b_pad_ref, b_lo_ref, b_mid_ref, b_hi_ref)

    planes = mid_ref.shape[0]
    height = c_ref.shape[1]
    depth = c_ref.shape[2]
    lane = lax.broadcasted_iota(jnp.int32, (rows, depth), 1)
    row = lax.broadcasted_iota(jnp.int32, (rows, depth), 0)
    for p in range(block):
        plane = i * block + p + HALO
        for y0 in range(0, height, rows):
            sl = (p, pl.ds(y0, rows), slice(None))
            centre, lap, grads = taps(pad_ref, plane, y0, rows, lane)
            if own_grad:
                bvals, _, gb = taps(b_pad_ref, plane, y0, rows, lane)
                for out_ref, value in zip(g_out, gb):
                    out_ref[sl] = value
            else:
                bvals = b_ref[sl]
                gb = [g0_ref[sl], g1_ref[sl], g2_ref[sl]]
            force = bvals * lap + (gb[0] * grads[0] + gb[1] * grads[1] + gb[2] * grads[2])
            if want_force:
                force_ref[sl] = force
            newer = 2.0 * centre - old_ref[sl] + c_ref[sl] * force
            if track:
                hit = (where_ref[3] == 1) & (where_ref[0] == plane - HALO)
                mask = hit & (row == where_ref[1] - y0) & (lane == where_ref[2])
                newer = jnp.where(mask, newer + amount_ref[0], newer)
                keep_ref[plane - HALO, pl.ds(y0, rows), :] = newer
            new_ref[sl] = newer

    if track:
        @pl.when(i == pl.num_programs(0) - 1)
        def _():
            edge_lo_ref[...] = keep_ref[0:HALO]
            edge_hi_ref[...] = keep_ref[planes - HALO:planes]
            one_lane = lax.broadcasted_iota(jnp.int32, (1, depth), 1)

            def sample(r, carry):
                x = rec_ref[0, r]
                y = rec_ref[1, r]
                z = rec_ref[2, r]
                line = keep_ref[x, pl.ds(y, 1), :]
                sample_ref[pl.ds(r, 1), :] = jnp.where(one_lane == z, line, 0.0)
                return carry

            lax.fori_loop(0, sample_ref.shape[0], sample, 0, unroll=8)


def grad_kernel(lo_ref, mid_ref, hi_ref, g0_ref, g1_ref, g2_ref, pad_ref, *, block, rows):
    i = pl.program_id(0)

    @pl.when(i == 0)
    def _():
        fill_padded(pad_ref, lo_ref, mid_ref, hi_ref)

    height = mid_ref.shape[1]
    lane = lax.broadcasted_iota(jnp.int32, (rows, mid_ref.shape[2]), 1)
    for p in range(block):
        plane = i * block + p + HALO
        for y0 in range(0, height, rows):
            sl = (p, pl.ds(y0, rows), slice(None))
            _, _, grads = taps(pad_ref, plane, y0, rows, lane)
            g0_ref[sl] = grads[0]
            g1_ref[sl] = grads[1]
            g2_ref[sl] = grads[2]


def pick_block(planes):
    for b in (4, 2, 1):
        if planes % b == 0:
            return b


def specs(shape, block):
    planes, height, depth = shape
    full = lambda s: pl.BlockSpec(s, lambda i: (0, 0, 0))
    blk = pl.BlockSpec((block, height, depth), lambda i: (i, 0, 0))
    return full, blk


def apply_step(lo, mid, hi, b, g, c, old, track=None, rows=40, want_force=True):
    planes, height, depth = mid.shape
    block = pick_block(planes)
    full, blk = specs(mid.shape, block)
    out = jax.ShapeDtypeStruct(mid.shape, jnp.float32)
    own_grad = g is None

    def halo(pair):
        array, at = pair if isinstance(pair, tuple) else (pair, 0)
        return array, pl.BlockSpec((HALO, height, depth), lambda i: (at, 0, 0))

    (lo, lo_spec), (hi, hi_spec) = halo(lo), halo(hi)
    in_specs = [lo_spec, full(mid.shape), hi_spec]
    args = [lo, mid, hi]
    if own_grad:
        (b_lo, b_lo_spec), (b_hi, b_hi_spec) = halo(b[0]), halo(b[2])
        in_specs += [b_lo_spec, full(b[1].shape), b_hi_spec]
        args += [b_lo, b[1], b_hi]
    else:
        in_specs += [blk] * 4
        args += [b, g[0], g[1], g[2]]
    in_specs += [blk, blk]
    args += [c, old]
    out_specs = [blk] if want_force else []
    out_shape = [out] if want_force else []
    out_specs.append(blk)
    out_shape.append(out)
    if own_grad:
        out_specs += [blk] * 3
        out_shape += [out] * 3
    scratch = [pltpu.VMEM((planes + 2 * HALO, height + 2 * PADY, depth), jnp.float32)]
    if own_grad:
        scratch.append(pltpu.VMEM((planes + 2 * HALO, height + 2 * PADY, depth), jnp.float32))
    if track is not None:
        smem = pl.BlockSpec(memory_space=pltpu.SMEM)
        in_specs += [smem, smem, smem]
        args += list(track)
        count = track[2].shape[1]
        edge = jax.ShapeDtypeStruct((HALO, height, depth), jnp.float32)
        lines = jax.ShapeDtypeStruct((count, depth), jnp.float32)
        out_specs += [full(edge.shape), full(edge.shape), pl.BlockSpec((count, depth), lambda i: (0, 0))]
        out_shape += [edge, edge, lines]
        scratch.append(pltpu.VMEM(mid.shape, jnp.float32))
    kernel = functools.partial(
        step_kernel, block=block, rows=rows, track=track is not None, own_grad=own_grad, want_force=want_force
    )
    return pl.pallas_call(
        kernel,
        grid=(planes // block,),
        in_specs=in_specs,
        out_specs=out_specs,
        out_shape=out_shape,
        scratch_shapes=scratch,
        compiler_params=pltpu.CompilerParams(dimension_semantics=("arbitrary",)),
    )(*args)


def apply_grad(lo, mid, hi, rows=40):
    planes, height, depth = mid.shape
    block = pick_block(planes)
    full, blk = specs(mid.shape, block)
    out = jax.ShapeDtypeStruct(mid.shape, jnp.float32)
    return pl.pallas_call(
        functools.partial(grad_kernel, block=block, rows=rows),
        grid=(planes // block,),
        in_specs=[full(lo.shape), full(mid.shape), full(hi.shape)],
        out_specs=[blk, blk, blk],
        out_shape=[out, out, out],
        scratch_shapes=[pltpu.VMEM((planes + 2 * HALO, height + 2 * PADY, depth), jnp.float32)],
        compiler_params=pltpu.CompilerParams(dimension_semantics=("arbitrary",)),
    )(lo, mid, hi)


def reduce_members(part, axis):
    members = lax.axis_size(axis)
    if members & (members - 1) or part.size % (members * 1024):
        return lax.psum(part, axis) / members
    me = lax.axis_index(axis)
    rows = part.reshape(-1, 128)
    bits = members.bit_length() - 1
    for b in range(bits):
        mask = 1 << b
        half = rows.shape[0] // 2
        upper = (me // mask) % 2
        keep = lax.dynamic_slice_in_dim(rows, upper * half, half, 0)
        give = lax.dynamic_slice_in_dim(rows, (1 - upper) * half, half, 0)
        pairs = [(i, i ^ mask) for i in range(members)]
        rows = keep + lax.ppermute(give, axis, pairs)
    rows = rows / members
    for b in reversed(range(bits)):
        mask = 1 << b
        upper = (me // mask) % 2
        pairs = [(i, i ^ mask) for i in range(members)]
        other = lax.ppermute(rows, axis, pairs)
        rows = jnp.where(upper == 1, jnp.concatenate([other, rows]), jnp.concatenate([rows, other]))
    return rows.reshape(part.shape)


def halos(blocks, axis):
    count = lax.axis_size(axis)
    forward = [(i, i + 1) for i in range(count - 1)]
    backward = [(target, source) for source, target in forward]
    planes = blocks[0].shape[0]
    tops = jnp.concatenate([block[planes - HALO:] for block in blocks])
    bottoms = jnp.concatenate([block[:HALO] for block in blocks])
    return lax.ppermute(tops, axis, forward), lax.ppermute(bottoms, axis, backward)


def edge_halos(low_edge, high_edge, axis):
    count = lax.axis_size(axis)
    forward = [(i, i + 1) for i in range(count - 1)]
    backward = [(target, source) for source, target in forward]
    return lax.ppermute(high_edge, axis, forward), lax.ppermute(low_edge, axis, backward)


def inject(field, where, valid, values):
    flat = field.reshape(-1).at[where].add(jnp.where(valid, values, 0.0))
    return flat.reshape(field.shape)


def shards(
    courant,
    prev_field,
    cur_field,
    adj_prev,
    adj_cur,
    buoyancy,
    wavelet,
    src_cell,
    rec_cell,
    observed,
):
    speed = courant[0]
    planes, height, depth = buoyancy.shape
    volume = planes * height * depth
    offset = lax.axis_index("tile") * volume
    steps = wavelet.shape[0]

    def locate(cells):
        local = cells - offset
        valid = (local >= 0) & (local < volume)
        return (jnp.clip(local, 0, volume - 1), valid)

    src_local, src_valid = locate(src_cell)
    rec_local, rec_valid = locate(rec_cell)
    first_lo, first_hi = halos([buoyancy, cur_field[0]], "tile")

    def spread(cells):
        return jnp.stack([cells // (height * depth), (cells // depth) % height, cells % depth])

    where = jnp.concatenate([spread(src_local)[:, 0], src_valid.astype(jnp.int32)])
    receivers = spread(rec_local)
    older, now = (prev_field[0], cur_field[0])
    lo, hi = (first_lo, 1), (first_hi, 1)
    forces = []
    samples = []
    grad_b = None
    for k in range(steps):
        track = (where, wavelet[k:k + 1], receivers)
        if grad_b is None:
            outs = apply_step(lo, now, hi, ((first_lo, 0), buoyancy, (first_hi, 0)), None, speed, older, track)
            force, newer = outs[:2]
            grad_b = outs[2:5]
            edge_lo, edge_hi, lines = outs[5:]
        else:
            force, newer, edge_lo, edge_hi, lines = apply_step(lo, now, hi, buoyancy, grad_b, speed, older, track)
        if k + 1 < steps:
            lo, hi = edge_halos(edge_lo, edge_hi, "tile")
        samples.append(jnp.sum(lines, axis=1))
        forces.append(force)
        older, now = (now, newer)
    residual = jnp.where(rec_valid, jnp.stack(samples) - observed, 0.0)
    older, now = (adj_prev[0], adj_cur[0])
    image_part = jnp.zeros(buoyancy.shape, jnp.float32)
    for j in range(steps):
        lo, hi = halos([now], "tile")
        (newer,) = apply_step(lo, now, hi, buoyancy, grad_b, speed, older, want_force=False)
        newer = inject(newer, rec_local, rec_valid, residual[steps - 1 - j])
        image_part = image_part + newer * forces[steps - 1 - j]
        older, now = (now, newer)
    image = reduce_members(image_part, "real")
    return (image, now[None])


def solution(mesh):
    in_specs = (
        P("real", "tile", None, None),
        P(("shot", "real"), "tile", None, None),
        P(("shot", "real"), "tile", None, None),
        P(("shot", "real"), "tile", None, None),
        P(("shot", "real"), "tile", None, None),
        P("tile", None, None),
        P("shot"),
        P("shot"),
        P("shot"),
        P("shot", None),
    )
    out_specs = (P(("shot", "tile"), None, None), P(("shot", "real"), "tile", None, None))
    return jax.shard_map(shards, mesh=mesh, in_specs=in_specs, out_specs=out_specs, check_vma=False)
```

```python
import functools
import jax
import jax.numpy as jnp
from jax import lax
from jax.experimental import pallas as pl
from jax.experimental.pallas import tpu as pltpu
from jax.sharding import PartitionSpec as P

SECOND = (-205.0 / 72.0, 8.0 / 5.0, -1.0 / 5.0, 8.0 / 315.0, -1.0 / 560.0)
FIRST = (4.0 / 5.0, -1.0 / 5.0, 4.0 / 105.0, -1.0 / 280.0)
HALO = 4
PADY = 8


def lane_shift(v, k, lane):
    width = v.shape[-1]
    if k > 0:
        rolled = pltpu.roll(v, width - k, 1)
        return jnp.where(lane < width - k, rolled, 0.0)
    rolled = pltpu.roll(v, -k, 1)
    return jnp.where(lane >= -k, rolled, 0.0)


def fill_padded(pad_ref, lo_ref, mid_ref, hi_ref, sem):
    planes, height, depth = mid_ref.shape
    rows = pl.ds(PADY, height)
    copies = [
        pltpu.make_async_copy(lo_ref, pad_ref.at[pl.ds(0, HALO), rows, :], sem.at[0]),
        pltpu.make_async_copy(mid_ref, pad_ref.at[pl.ds(HALO, planes), rows, :], sem.at[1]),
        pltpu.make_async_copy(hi_ref, pad_ref.at[pl.ds(HALO + planes, HALO), rows, :], sem.at[2]),
    ]
    for copy in copies:
        copy.start()
    pad_ref[:, 0:PADY, :] = jnp.zeros((planes + 2 * HALO, PADY, depth), jnp.float32)
    pad_ref[:, PADY + height:, :] = jnp.zeros((planes + 2 * HALO, PADY, depth), jnp.float32)
    for copy in copies:
        copy.wait()


def taps(pad_ref, plane, y0, rows, lane):
    def at(dx, dy):
        return pad_ref[plane + dx, pl.ds(PADY + y0 + dy, rows), :]
    centre = at(0, 0)
    lap = 3.0 * SECOND[0] * centre
    grads = []
    for axis in range(3):
        if axis == 0:
            get = lambda k: at(k, 0)
        elif axis == 1:
            get = lambda k: at(0, k)
        else:
            get = lambda k: lane_shift(centre, k, lane)
        vals = {k: get(k) for k in (1, 2, 3, 4, -1, -2, -3, -4)}
        for k in range(1, 5):
            lap = lap + SECOND[k] * (vals[k] + vals[-k])
        slope = FIRST[0] * (vals[1] - vals[-1])
        for k in range(2, 5):
            slope = slope + FIRST[k - 1] * (vals[k] - vals[-k])
        grads.append(slope)
    return centre, lap, grads


def step_kernel(*refs, block, rows, track, own_grad, want_force):
    refs = list(refs)
    take = lambda n: [refs.pop(0) for _ in range(n)]
    lo_ref, mid_ref, hi_ref = take(3)
    if own_grad:
        b_lo_ref, b_mid_ref, b_hi_ref = take(3)
    else:
        b_ref, g0_ref, g1_ref, g2_ref = take(4)
    c_ref, old_ref = take(2)
    if track:
        where_ref, amount_ref, rec_ref = take(3)
    force_ref = take(1)[0] if want_force else None
    (new_ref,) = take(1)
    if own_grad:
        g_out = take(3)
    if track:
        edge_lo_ref, edge_hi_ref, sample_ref = take(3)
    pad_ref, sem = take(2)
    if own_grad:
        b_pad_ref, b_sem = take(2)
    if track:
        (keep_ref,) = take(1)
    i = pl.program_id(0)

    @pl.when(i == 0)
    def _():
        fill_padded(pad_ref, lo_ref, mid_ref, hi_ref, sem)
        if own_grad:
            fill_padded(b_pad_ref, b_lo_ref, b_mid_ref, b_hi_ref, b_sem)

    planes = mid_ref.shape[0]
    height = c_ref.shape[1]
    depth = c_ref.shape[2]
    lane = lax.broadcasted_iota(jnp.int32, (rows, depth), 1)
    row = lax.broadcasted_iota(jnp.int32, (rows, depth), 0)
    for p in range(block):
        plane = i * block + p + HALO
        for y0 in range(0, height, rows):
            sl = (p, pl.ds(y0, rows), slice(None))
            centre, lap, grads = taps(pad_ref, plane, y0, rows, lane)
            if own_grad:
                bvals, _, gb = taps(b_pad_ref, plane, y0, rows, lane)
                for out_ref, value in zip(g_out, gb):
                    out_ref[sl] = value
            else:
                bvals = b_ref[sl]
                gb = [g0_ref[sl], g1_ref[sl], g2_ref[sl]]
            force = bvals * lap + (gb[0] * grads[0] + gb[1] * grads[1] + gb[2] * grads[2])
            if want_force:
                force_ref[sl] = force
            newer = 2.0 * centre - old_ref[sl] + c_ref[sl] * force
            if track:
                hit = (where_ref[3] == 1) & (where_ref[0] == plane - HALO)
                mask = hit & (row == where_ref[1] - y0) & (lane == where_ref[2])
                newer = jnp.where(mask, newer + amount_ref[0], newer)
                keep_ref[plane - HALO, pl.ds(y0, rows), :] = newer
            new_ref[sl] = newer

    if track:
        @pl.when(i == pl.num_programs(0) - 1)
        def _():
            edge_lo_ref[...] = keep_ref[0:HALO]
            edge_hi_ref[...] = keep_ref[planes - HALO:planes]
            one_lane = lax.broadcasted_iota(jnp.int32, (1, depth), 1)

            def sample(r, carry):
                x = rec_ref[0, r]
                y = rec_ref[1, r]
                z = rec_ref[2, r]
                line = keep_ref[x, pl.ds(y, 1), :]
                sample_ref[pl.ds(r, 1), :] = jnp.where(one_lane == z, line, 0.0)
                return carry

            lax.fori_loop(0, sample_ref.shape[0], sample, 0, unroll=8)


def pick_block(planes):
    for b in (4, 2, 1):
        if planes % b == 0:
            return b


def specs(shape, block):
    planes, height, depth = shape
    full = lambda s: pl.BlockSpec(s, lambda i: (0, 0, 0))
    blk = pl.BlockSpec((block, height, depth), lambda i: (i, 0, 0))
    return full, blk


def apply_step(lo, mid, hi, b, g, c, old, track=None, rows=40, want_force=True):
    planes, height, depth = mid.shape
    block = pick_block(planes)
    full, blk = specs(mid.shape, block)
    out = jax.ShapeDtypeStruct(mid.shape, jnp.float32)
    own_grad = g is None
    anywhere = pl.BlockSpec(memory_space=pl.ANY)
    in_specs = [anywhere] * 3
    args = [lo, mid, hi]
    if own_grad:
        in_specs += [anywhere] * 3
        args += list(b)
    else:
        in_specs += [blk] * 4
        args += [b, g[0], g[1], g[2]]
    in_specs += [blk, blk]
    args += [c, old]
    out_specs = [blk] if want_force else []
    out_shape = [out] if want_force else []
    out_specs.append(blk)
    out_shape.append(out)
    if own_grad:
        out_specs += [blk] * 3
        out_shape += [out] * 3
    padded = pltpu.VMEM((planes + 2 * HALO, height + 2 * PADY, depth), jnp.float32)
    scratch = [padded, pltpu.SemaphoreType.DMA((3,))]
    if own_grad:
        scratch += [padded, pltpu.SemaphoreType.DMA((3,))]
    if track is not None:
        smem = pl.BlockSpec(memory_space=pltpu.SMEM)
        in_specs += [smem, smem, smem]
        args += list(track)
        count = track[2].shape[1]
        edge = jax.ShapeDtypeStruct((HALO, height, depth), jnp.float32)
        lines = jax.ShapeDtypeStruct((count, depth), jnp.float32)
        out_specs += [full(edge.shape), full(edge.shape), pl.BlockSpec((count, depth), lambda i: (0, 0))]
        out_shape += [edge, edge, lines]
        scratch.append(pltpu.VMEM(mid.shape, jnp.float32))
    kernel = functools.partial(
        step_kernel, block=block, rows=rows, track=track is not None, own_grad=own_grad, want_force=want_force
    )
    return pl.pallas_call(
        kernel,
        grid=(planes // block,),
        in_specs=in_specs,
        out_specs=out_specs,
        out_shape=out_shape,
        scratch_shapes=scratch,
        compiler_params=pltpu.CompilerParams(dimension_semantics=("arbitrary",)),
    )(*args)


def reduce_members(part, axis):
    members = lax.axis_size(axis)
    if members & (members - 1) or part.size % (members * 1024):
        return lax.psum(part, axis) / members
    me = lax.axis_index(axis)
    rows = part.reshape(-1, 128)
    bits = members.bit_length() - 1
    for b in range(bits):
        mask = 1 << b
        half = rows.shape[0] // 2
        upper = (me // mask) % 2
        keep = lax.dynamic_slice_in_dim(rows, upper * half, half, 0)
        give = lax.dynamic_slice_in_dim(rows, (1 - upper) * half, half, 0)
        pairs = [(i, i ^ mask) for i in range(members)]
        rows = keep + lax.ppermute(give, axis, pairs)
    rows = rows / members
    for b in reversed(range(bits)):
        mask = 1 << b
        upper = (me // mask) % 2
        pairs = [(i, i ^ mask) for i in range(members)]
        other = lax.ppermute(rows, axis, pairs)
        rows = jnp.where(upper == 1, jnp.concatenate([other, rows]), jnp.concatenate([rows, other]))
    return rows.reshape(part.shape)


def halos(block, axis):
    count = lax.axis_size(axis)
    forward = [(i, i + 1) for i in range(count - 1)]
    backward = [(target, source) for source, target in forward]
    planes = block.shape[0]
    low = lax.ppermute(block[planes - HALO:], axis, forward)
    high = lax.ppermute(block[:HALO], axis, backward)
    return low, high


def edge_halos(low_edge, high_edge, axis):
    count = lax.axis_size(axis)
    forward = [(i, i + 1) for i in range(count - 1)]
    backward = [(target, source) for source, target in forward]
    return lax.ppermute(high_edge, axis, forward), lax.ppermute(low_edge, axis, backward)


def inject(field, where, valid, values):
    flat = field.reshape(-1).at[where].add(jnp.where(valid, values, 0.0))
    return flat.reshape(field.shape)


def shards(
    courant,
    prev_field,
    cur_field,
    adj_prev,
    adj_cur,
    buoyancy,
    wavelet,
    src_cell,
    rec_cell,
    observed,
):
    speed = courant[0]
    planes, height, depth = buoyancy.shape
    volume = planes * height * depth
    offset = lax.axis_index("tile") * volume
    steps = wavelet.shape[0]

    def locate(cells):
        local = cells - offset
        valid = (local >= 0) & (local < volume)
        return (jnp.clip(local, 0, volume - 1), valid)

    src_local, src_valid = locate(src_cell)
    rec_local, rec_valid = locate(rec_cell)
    b_lo, b_hi = halos(buoyancy, "tile")

    def spread(cells):
        return jnp.stack([cells // (height * depth), (cells // depth) % height, cells % depth])

    where = jnp.concatenate([spread(src_local)[:, 0], src_valid.astype(jnp.int32)])
    receivers = spread(rec_local)
    older, now = (prev_field[0], cur_field[0])
    lo, hi = halos(now, "tile")
    forces = []
    samples = []
    grad_b = None
    for k in range(steps):
        track = (where, wavelet[k:k + 1], receivers)
        if grad_b is None:
            outs = apply_step(lo, now, hi, (b_lo, buoyancy, b_hi), None, speed, older, track)
            force, newer = outs[:2]
            grad_b = outs[2:5]
            edge_lo, edge_hi, lines = outs[5:]
        else:
            force, newer, edge_lo, edge_hi, lines = apply_step(lo, now, hi, buoyancy, grad_b, speed, older, track)
        if k + 1 < steps:
            lo, hi = edge_halos(edge_lo, edge_hi, "tile")
        samples.append(jnp.sum(lines, axis=1))
        forces.append(force)
        older, now = (now, newer)
    residual = jnp.where(rec_valid, jnp.stack(samples) - observed, 0.0)
    older, now = (adj_prev[0], adj_cur[0])
    image_part = jnp.zeros(buoyancy.shape, jnp.float32)
    for j in range(steps):
        lo, hi = halos(now, "tile")
        (newer,) = apply_step(lo, now, hi, buoyancy, grad_b, speed, older, want_force=False)
        newer = inject(newer, rec_local, rec_valid, residual[steps - 1 - j])
        image_part = image_part + newer * forces[steps - 1 - j]
        older, now = (now, newer)
    image = reduce_members(image_part, "real")
    return (image, now[None])


def solution(mesh):
    in_specs = (
        P("real", "tile", None, None),
        P(("shot", "real"), "tile", None, None),
        P(("shot", "real"), "tile", None, None),
        P(("shot", "real"), "tile", None, None),
        P(("shot", "real"), "tile", None, None),
        P("tile", None, None),
        P("shot"),
        P("shot"),
        P("shot"),
        P("shot", None),
    )
    out_specs = (P(("shot", "tile"), None, None), P(("shot", "real"), "tile", None, None))
    return jax.shard_map(shards, mesh=mesh, in_specs=in_specs, out_specs=out_specs, check_vma=False)
```

```python
import functools
import jax
import jax.numpy as jnp
from jax import lax
from jax.experimental import pallas as pl
from jax.experimental.pallas import tpu as pltpu
from jax.sharding import PartitionSpec as P

SECOND = (-205.0 / 72.0, 8.0 / 5.0, -1.0 / 5.0, 8.0 / 315.0, -1.0 / 560.0)
FIRST = (4.0 / 5.0, -1.0 / 5.0, 4.0 / 105.0, -1.0 / 280.0)
HALO = 4
PADY = 8


def lane_shift(v, k, lane):
    width = v.shape[-1]
    if k > 0:
        rolled = pltpu.roll(v, width - k, 1)
        return jnp.where(lane < width - k, rolled, 0.0)
    rolled = pltpu.roll(v, -k, 1)
    return jnp.where(lane >= -k, rolled, 0.0)


def fill_padded(pad_ref, lo_ref, mid_ref, hi_ref):
    planes, height, depth = mid_ref.shape
    pad_ref[...] = jnp.zeros(pad_ref.shape, jnp.float32)
    pad_ref[0:HALO, PADY:PADY + height, :] = lo_ref[...]
    pad_ref[HALO:HALO + planes, PADY:PADY + height, :] = mid_ref[...]
    pad_ref[HALO + planes:, PADY:PADY + height, :] = hi_ref[...]


def taps(pad_ref, plane, y0, rows, lane):
    def at(dx, dy):
        return pad_ref[plane + dx, pl.ds(PADY + y0 + dy, rows), :]
    centre = at(0, 0)
    lap = 3.0 * SECOND[0] * centre
    grads = []
    for axis in range(3):
        if axis == 0:
            get = lambda k: at(k, 0)
        elif axis == 1:
            get = lambda k: at(0, k)
        else:
            get = lambda k: lane_shift(centre, k, lane)
        vals = {k: get(k) for k in (1, 2, 3, 4, -1, -2, -3, -4)}
        for k in range(1, 5):
            lap = lap + SECOND[k] * (vals[k] + vals[-k])
        slope = FIRST[0] * (vals[1] - vals[-1])
        for k in range(2, 5):
            slope = slope + FIRST[k - 1] * (vals[k] - vals[-k])
        grads.append(slope)
    return centre, lap, grads


def step_kernel(*refs, block, rows, track, own_grad, want_force):
    refs = list(refs)
    take = lambda n: [refs.pop(0) for _ in range(n)]
    lo_ref, mid_ref, hi_ref = take(3)
    if own_grad:
        b_lo_ref, b_mid_ref, b_hi_ref = take(3)
    else:
        b_ref, g0_ref, g1_ref, g2_ref = take(4)
    c_ref, old_ref = take(2)
    if track:
        where_ref, amount_ref, rec_ref = take(3)
    force_ref = take(1)[0] if want_force else None
    (new_ref,) = take(1)
    if own_grad:
        g_out = take(3)
    if track:
        edge_lo_ref, edge_hi_ref, sample_ref = take(3)
    (pad_ref,) = take(1)
    if own_grad:
        (b_pad_ref,) = take(1)
    if track:
        (keep_ref,) = take(1)
    i = pl.program_id(0)

    @pl.when(i == 0)
    def _():
        fill_padded(pad_ref, lo_ref, mid_ref, hi_ref)
        if own_grad:
            fill_padded(b_pad_ref, b_lo_ref, b_mid_ref, b_hi_ref)

    planes = mid_ref.shape[0]
    height = c_ref.shape[1]
    depth = c_ref.shape[2]
    lane = lax.broadcasted_iota(jnp.int32, (rows, depth), 1)
    row = lax.broadcasted_iota(jnp.int32, (rows, depth), 0)
    for p in range(block):
        plane = i * block + p + HALO
        for y0 in range(0, height, rows):
            sl = (p, pl.ds(y0, rows), slice(None))
            centre, lap, grads = taps(pad_ref, plane, y0, rows, lane)
            if own_grad:
                bvals, _, gb = taps(b_pad_ref, plane, y0, rows, lane)
                for out_ref, value in zip(g_out, gb):
                    out_ref[sl] = value
            else:
                bvals = b_ref[sl]
                gb = [g0_ref[sl], g1_ref[sl], g2_ref[sl]]
            force = bvals * lap + (gb[0] * grads[0] + gb[1] * grads[1] + gb[2] * grads[2])
            if want_force:
                force_ref[sl] = force
            newer = 2.0 * centre - old_ref[sl] + c_ref[sl] * force
            if track:
                hit = (where_ref[3] == 1) & (where_ref[0] == plane - HALO)
                mask = hit & (row == where_ref[1] - y0) & (lane == where_ref[2])
                newer = jnp.where(mask, newer + amount_ref[0], newer)
                keep_ref[plane - HALO, pl.ds(y0, rows), :] = newer
            new_ref[sl] = newer

    if track:
        @pl.when(i == pl.num_programs(0) - 1)
        def _():
            edge_lo_ref[...] = keep_ref[0:HALO]
            edge_hi_ref[...] = keep_ref[planes - HALO:planes]
            one_lane = lax.broadcasted_iota(jnp.int32, (1, depth), 1)

            def sample(r, carry):
                x = rec_ref[0, r]
                y = rec_ref[1, r]
                z = rec_ref[2, r]
                line = keep_ref[x, pl.ds(y, 1), :]
                sample_ref[pl.ds(r, 1), :] = jnp.where(one_lane == z, line, 0.0)
                return carry

            lax.fori_loop(0, sample_ref.shape[0], sample, 0, unroll=8)


def grad_kernel(lo_ref, mid_ref, hi_ref, g0_ref, g1_ref, g2_ref, pad_ref, *, block, rows):
    i = pl.program_id(0)

    @pl.when(i == 0)
    def _():
        fill_padded(pad_ref, lo_ref, mid_ref, hi_ref)

    height = mid_ref.shape[1]
    lane = lax.broadcasted_iota(jnp.int32, (rows, mid_ref.shape[2]), 1)
    for p in range(block):
        plane = i * block + p + HALO
        for y0 in range(0, height, rows):
            sl = (p, pl.ds(y0, rows), slice(None))
            _, _, grads = taps(pad_ref, plane, y0, rows, lane)
            g0_ref[sl] = grads[0]
            g1_ref[sl] = grads[1]
            g2_ref[sl] = grads[2]


def pick_block(planes):
    for b in (4, 2, 1):
        if planes % b == 0:
            return b


def specs(shape, block):
    planes, height, depth = shape
    full = lambda s: pl.BlockSpec(s, lambda i: (0, 0, 0))
    blk = pl.BlockSpec((block, height, depth), lambda i: (i, 0, 0))
    return full, blk


def apply_step(lo, mid, hi, b, g, c, old, track=None, rows=40, want_force=True):
    planes, height, depth = mid.shape
    block = pick_block(planes)
    full, blk = specs(mid.shape, block)
    out = jax.ShapeDtypeStruct(mid.shape, jnp.float32)
    own_grad = g is None
    in_specs = [full(lo.shape), full(mid.shape), full(hi.shape)]
    args = [lo, mid, hi]
    if own_grad:
        in_specs += [full(b[0].shape), full(b[1].shape), full(b[2].shape)]
        args += list(b)
    else:
        in_specs += [blk] * 4
        args += [b, g[0], g[1], g[2]]
    in_specs += [blk, blk]
    args += [c, old]
    out_specs = [blk] if want_force else []
    out_shape = [out] if want_force else []
    out_specs.append(blk)
    out_shape.append(out)
    if own_grad:
        out_specs += [blk] * 3
        out_shape += [out] * 3
    scratch = [pltpu.VMEM((planes + 2 * HALO, height + 2 * PADY, depth), jnp.float32)]
    if own_grad:
        scratch.append(pltpu.VMEM((planes + 2 * HALO, height + 2 * PADY, depth), jnp.float32))
    if track is not None:
        smem = pl.BlockSpec(memory_space=pltpu.SMEM)
        in_specs += [smem, smem, smem]
        args += list(track)
        count = track[2].shape[1]
        edge = jax.ShapeDtypeStruct((HALO, height, depth), jnp.float32)
        lines = jax.ShapeDtypeStruct((count, depth), jnp.float32)
        out_specs += [full(edge.shape), full(edge.shape), pl.BlockSpec((count, depth), lambda i: (0, 0))]
        out_shape += [edge, edge, lines]
        scratch.append(pltpu.VMEM(mid.shape, jnp.float32))
    kernel = functools.partial(
        step_kernel, block=block, rows=rows, track=track is not None, own_grad=own_grad, want_force=want_force
    )
    return pl.pallas_call(
        kernel,
        grid=(planes // block,),
        in_specs=in_specs,
        out_specs=out_specs,
        out_shape=out_shape,
        scratch_shapes=scratch,
        compiler_params=pltpu.CompilerParams(dimension_semantics=("arbitrary",)),
    )(*args)


def apply_grad(lo, mid, hi, rows=40):
    planes, height, depth = mid.shape
    block = pick_block(planes)
    full, blk = specs(mid.shape, block)
    out = jax.ShapeDtypeStruct(mid.shape, jnp.float32)
    return pl.pallas_call(
        functools.partial(grad_kernel, block=block, rows=rows),
        grid=(planes // block,),
        in_specs=[full(lo.shape), full(mid.shape), full(hi.shape)],
        out_specs=[blk, blk, blk],
        out_shape=[out, out, out],
        scratch_shapes=[pltpu.VMEM((planes + 2 * HALO, height + 2 * PADY, depth), jnp.float32)],
        compiler_params=pltpu.CompilerParams(dimension_semantics=("arbitrary",)),
    )(lo, mid, hi)


def reduce_members(part, axis):
    members = lax.axis_size(axis)
    if members & (members - 1) or part.size % (members * 1024):
        return lax.psum(part, axis) / members
    me = lax.axis_index(axis)
    rows = part.reshape(-1, 128)
    bits = members.bit_length() - 1
    for b in range(bits):
        mask = 1 << b
        half = rows.shape[0] // 2
        upper = (me // mask) % 2
        keep = lax.dynamic_slice_in_dim(rows, upper * half, half, 0)
        give = lax.dynamic_slice_in_dim(rows, (1 - upper) * half, half, 0)
        pairs = [(i, i ^ mask) for i in range(members)]
        rows = keep + lax.ppermute(give, axis, pairs)
    rows = rows / members
    for b in reversed(range(bits)):
        mask = 1 << b
        upper = (me // mask) % 2
        pairs = [(i, i ^ mask) for i in range(members)]
        other = lax.ppermute(rows, axis, pairs)
        rows = jnp.where(upper == 1, jnp.concatenate([other, rows]), jnp.concatenate([rows, other]))
    return rows.reshape(part.shape)


def halos(block, axis):
    count = lax.axis_size(axis)
    forward = [(i, i + 1) for i in range(count - 1)]
    backward = [(target, source) for source, target in forward]
    planes = block.shape[0]
    low = lax.ppermute(block[planes - HALO:], axis, forward)
    high = lax.ppermute(block[:HALO], axis, backward)
    return low, high


def edge_halos(low_edge, high_edge, axis):
    count = lax.axis_size(axis)
    forward = [(i, i + 1) for i in range(count - 1)]
    backward = [(target, source) for source, target in forward]
    return lax.ppermute(high_edge, axis, forward), lax.ppermute(low_edge, axis, backward)


def inject(field, where, valid, values):
    flat = field.reshape(-1).at[where].add(jnp.where(valid, values, 0.0))
    return flat.reshape(field.shape)


def shards(
    courant,
    prev_field,
    cur_field,
    adj_prev,
    adj_cur,
    buoyancy,
    wavelet,
    src_cell,
    rec_cell,
    observed,
):
    speed = courant[0]
    planes, height, depth = buoyancy.shape
    volume = planes * height * depth
    offset = lax.axis_index("tile") * volume
    steps = wavelet.shape[0]

    def locate(cells):
        local = cells - offset
        valid = (local >= 0) & (local < volume)
        return (jnp.clip(local, 0, volume - 1), valid)

    src_local, src_valid = locate(src_cell)
    rec_local, rec_valid = locate(rec_cell)
    b_lo, b_hi = halos(buoyancy, "tile")

    def spread(cells):
        return jnp.stack([cells // (height * depth), (cells // depth) % height, cells % depth])

    where = jnp.concatenate([spread(src_local)[:, 0], src_valid.astype(jnp.int32)])
    receivers = spread(rec_local)
    older, now = (prev_field[0], cur_field[0])
    lo, hi = halos(now, "tile")
    forces = []
    samples = []
    grad_b = None
    for k in range(steps):
        track = (where, wavelet[k:k + 1], receivers)
        if grad_b is None:
            outs = apply_step(lo, now, hi, (b_lo, buoyancy, b_hi), None, speed, older, track)
            force, newer = outs[:2]
            grad_b = outs[2:5]
            edge_lo, edge_hi, lines = outs[5:]
        else:
            force, newer, edge_lo, edge_hi, lines = apply_step(lo, now, hi, buoyancy, grad_b, speed, older, track)
        if k + 1 < steps:
            lo, hi = edge_halos(edge_lo, edge_hi, "tile")
        samples.append(jnp.sum(lines, axis=1))
        forces.append(force)
        older, now = (now, newer)
    residual = jnp.where(rec_valid, jnp.stack(samples) - observed, 0.0)
    older, now = (adj_prev[0], adj_cur[0])
    image_part = jnp.zeros(buoyancy.shape, jnp.float32)
    edge = HALO * height * depth
    count = lax.axis_size("tile")
    forward = [(i, i + 1) for i in range(count - 1)]
    backward = [(target, source) for source, target in forward]

    def near(start):
        local = rec_cell - start
        valid = (local >= 0) & (local < edge)
        return jnp.clip(local, 0, edge - 1), valid

    below_local, below_valid = near(offset - edge)
    above_local, above_valid = near(offset + volume)
    lo, hi = halos(now, "tile")
    for j in range(steps):
        (newer,) = apply_step(lo, now, hi, buoyancy, grad_b, speed, older, want_force=False)
        values = residual[steps - 1 - j]
        if j + 1 < steps:
            lo, hi = edge_halos(newer[:HALO], newer[planes - HALO:], "tile")
            lo = inject(lo, below_local, below_valid, lax.ppermute(values, "tile", forward))
            hi = inject(hi, above_local, above_valid, lax.ppermute(values, "tile", backward))
        newer = inject(newer, rec_local, rec_valid, values)
        image_part = image_part + newer * forces[steps - 1 - j]
        older, now = (now, newer)
    image = reduce_members(image_part, "real")
    return (image, now[None])


def solution(mesh):
    in_specs = (
        P("real", "tile", None, None),
        P(("shot", "real"), "tile", None, None),
        P(("shot", "real"), "tile", None, None),
        P(("shot", "real"), "tile", None, None),
        P(("shot", "real"), "tile", None, None),
        P("tile", None, None),
        P("shot"),
        P("shot"),
        P("shot"),
        P("shot", None),
    )
    out_specs = (P(("shot", "tile"), None, None), P(("shot", "real"), "tile", None, None))
    return jax.shard_map(shards, mesh=mesh, in_specs=in_specs, out_specs=out_specs, check_vma=False)
```

```python
import functools
import jax
import jax.numpy as jnp
from jax import lax
from jax.experimental import pallas as pl
from jax.experimental.pallas import tpu as pltpu
from jax.sharding import PartitionSpec as P

SECOND = (-205.0 / 72.0, 8.0 / 5.0, -1.0 / 5.0, 8.0 / 315.0, -1.0 / 560.0)
FIRST = (4.0 / 5.0, -1.0 / 5.0, 4.0 / 105.0, -1.0 / 280.0)
HALO = 4
PADY = 8


def lane_shift(v, k, lane):
    width = v.shape[-1]
    if k > 0:
        rolled = pltpu.roll(v, width - k, 1)
        return jnp.where(lane < width - k, rolled, 0.0)
    rolled = pltpu.roll(v, -k, 1)
    return jnp.where(lane >= -k, rolled, 0.0)


def fill_padded(pad_ref, lo_ref, mid_ref, hi_ref):
    planes, height, depth = mid_ref.shape
    pad_ref[...] = jnp.zeros(pad_ref.shape, jnp.float32)
    pad_ref[0:HALO, PADY:PADY + height, :] = lo_ref[...]
    pad_ref[HALO:HALO + planes, PADY:PADY + height, :] = mid_ref[...]
    pad_ref[HALO + planes:, PADY:PADY + height, :] = hi_ref[...]


def taps(pad_ref, plane, y0, rows, lane):
    def at(dx, dy):
        return pad_ref[plane + dx, pl.ds(PADY + y0 + dy, rows), :]
    centre = at(0, 0)
    lap = 3.0 * SECOND[0] * centre
    grads = []
    for axis in range(3):
        if axis == 0:
            get = lambda k: at(k, 0)
        elif axis == 1:
            get = lambda k: at(0, k)
        else:
            get = lambda k: lane_shift(centre, k, lane)
        vals = {k: get(k) for k in (1, 2, 3, 4, -1, -2, -3, -4)}
        for k in range(1, 5):
            lap = lap + SECOND[k] * (vals[k] + vals[-k])
        slope = FIRST[0] * (vals[1] - vals[-1])
        for k in range(2, 5):
            slope = slope + FIRST[k - 1] * (vals[k] - vals[-k])
        grads.append(slope)
    return centre, lap, grads


def step_kernel(*refs, block, rows, track, own_grad, want_force):
    refs = list(refs)
    take = lambda n: [refs.pop(0) for _ in range(n)]
    lo_ref, mid_ref, hi_ref = take(3)
    if own_grad:
        b_lo_ref, b_mid_ref, b_hi_ref = take(3)
    else:
        b_ref, g0_ref, g1_ref, g2_ref = take(4)
    c_ref, old_ref = take(2)
    if track:
        where_ref, amount_ref, rec_ref = take(3)
    force_ref = take(1)[0] if want_force else None
    (new_ref,) = take(1)
    if own_grad:
        g_out = take(3)
    if track:
        edge_lo_ref, edge_hi_ref, sample_ref = take(3)
    (pad_ref,) = take(1)
    if own_grad:
        (b_pad_ref,) = take(1)
    if track:
        (keep_ref,) = take(1)
    i = pl.program_id(0)

    @pl.when(i == 0)
    def _():
        fill_padded(pad_ref, lo_ref, mid_ref, hi_ref)
        if own_grad:
            fill_padded(b_pad_ref, b_lo_ref, b_mid_ref, b_hi_ref)

    planes = mid_ref.shape[0]
    height = c_ref.shape[1]
    depth = c_ref.shape[2]
    lane = lax.broadcasted_iota(jnp.int32, (rows, depth), 1)
    row = lax.broadcasted_iota(jnp.int32, (rows, depth), 0)
    for p in range(block):
        plane = i * block + p + HALO
        for y0 in range(0, height, rows):
            sl = (p, pl.ds(y0, rows), slice(None))
            centre, lap, grads = taps(pad_ref, plane, y0, rows, lane)
            if own_grad:
                bvals, _, gb = taps(b_pad_ref, plane, y0, rows, lane)
                for out_ref, value in zip(g_out, gb):
                    out_ref[sl] = value
            else:
                bvals = b_ref[sl]
                gb = [g0_ref[sl], g1_ref[sl], g2_ref[sl]]
            force = bvals * lap + (gb[0] * grads[0] + gb[1] * grads[1] + gb[2] * grads[2])
            if want_force:
                force_ref[sl] = force
            newer = 2.0 * centre - old_ref[sl] + c_ref[sl] * force
            if track:
                hit = (where_ref[3] == 1) & (where_ref[0] == plane - HALO)
                mask = hit & (row == where_ref[1] - y0) & (lane == where_ref[2])
                newer = jnp.where(mask, newer + amount_ref[0], newer)
                keep_ref[plane - HALO, pl.ds(y0, rows), :] = newer
            new_ref[sl] = newer

    if track:
        @pl.when(i == pl.num_programs(0) - 1)
        def _():
            edge_lo_ref[...] = keep_ref[0:HALO]
            edge_hi_ref[...] = keep_ref[planes - HALO:planes]
            one_lane = lax.broadcasted_iota(jnp.int32, (1, depth), 1)

            def sample(r, carry):
                x = rec_ref[0, r]
                y = rec_ref[1, r]
                z = rec_ref[2, r]
                line = keep_ref[x, pl.ds(y, 1), :]
                sample_ref[pl.ds(r, 1), :] = jnp.where(one_lane == z, line, 0.0)
                return carry

            lax.fori_loop(0, sample_ref.shape[0], sample, 0, unroll=8)


def grad_kernel(lo_ref, mid_ref, hi_ref, g0_ref, g1_ref, g2_ref, pad_ref, *, block, rows):
    i = pl.program_id(0)

    @pl.when(i == 0)
    def _():
        fill_padded(pad_ref, lo_ref, mid_ref, hi_ref)

    height = mid_ref.shape[1]
    lane = lax.broadcasted_iota(jnp.int32, (rows, mid_ref.shape[2]), 1)
    for p in range(block):
        plane = i * block + p + HALO
        for y0 in range(0, height, rows):
            sl = (p, pl.ds(y0, rows), slice(None))
            _, _, grads = taps(pad_ref, plane, y0, rows, lane)
            g0_ref[sl] = grads[0]
            g1_ref[sl] = grads[1]
            g2_ref[sl] = grads[2]


def pick_block(planes):
    for b in (4, 2, 1):
        if planes % b == 0:
            return b


def specs(shape, block):
    planes, height, depth = shape
    full = lambda s: pl.BlockSpec(s, lambda i: (0, 0, 0))
    blk = pl.BlockSpec((block, height, depth), lambda i: (i, 0, 0))
    return full, blk


def apply_step(lo, mid, hi, b, g, c, old, track=None, rows=40, want_force=True):
    planes, height, depth = mid.shape
    block = pick_block(planes)
    full, blk = specs(mid.shape, block)
    out = jax.ShapeDtypeStruct(mid.shape, jnp.float32)
    own_grad = g is None
    in_specs = [full(lo.shape), full(mid.shape), full(hi.shape)]
    args = [lo, mid, hi]
    if own_grad:
        in_specs += [full(b[0].shape), full(b[1].shape), full(b[2].shape)]
        args += list(b)
    else:
        in_specs += [blk] * 4
        args += [b, g[0], g[1], g[2]]
    in_specs += [blk, blk]
    args += [c, old]
    out_specs = [blk] if want_force else []
    out_shape = [out] if want_force else []
    out_specs.append(blk)
    out_shape.append(out)
    if own_grad:
        out_specs += [blk] * 3
        out_shape += [out] * 3
    scratch = [pltpu.VMEM((planes + 2 * HALO, height + 2 * PADY, depth), jnp.float32)]
    if own_grad:
        scratch.append(pltpu.VMEM((planes + 2 * HALO, height + 2 * PADY, depth), jnp.float32))
    if track is not None:
        smem = pl.BlockSpec(memory_space=pltpu.SMEM)
        in_specs += [smem, smem, smem]
        args += list(track)
        count = track[2].shape[1]
        edge = jax.ShapeDtypeStruct((HALO, height, depth), jnp.float32)
        lines = jax.ShapeDtypeStruct((count, depth), jnp.float32)
        out_specs += [full(edge.shape), full(edge.shape), pl.BlockSpec((count, depth), lambda i: (0, 0))]
        out_shape += [edge, edge, lines]
        scratch.append(pltpu.VMEM(mid.shape, jnp.float32))
    kernel = functools.partial(
        step_kernel, block=block, rows=rows, track=track is not None, own_grad=own_grad, want_force=want_force
    )
    return pl.pallas_call(
        kernel,
        grid=(planes // block,),
        in_specs=in_specs,
        out_specs=out_specs,
        out_shape=out_shape,
        scratch_shapes=scratch,
        compiler_params=pltpu.CompilerParams(dimension_semantics=("arbitrary",)),
    )(*args)


def apply_grad(lo, mid, hi, rows=40):
    planes, height, depth = mid.shape
    block = pick_block(planes)
    full, blk = specs(mid.shape, block)
    out = jax.ShapeDtypeStruct(mid.shape, jnp.float32)
    return pl.pallas_call(
        functools.partial(grad_kernel, block=block, rows=rows),
        grid=(planes // block,),
        in_specs=[full(lo.shape), full(mid.shape), full(hi.shape)],
        out_specs=[blk, blk, blk],
        out_shape=[out, out, out],
        scratch_shapes=[pltpu.VMEM((planes + 2 * HALO, height + 2 * PADY, depth), jnp.float32)],
        compiler_params=pltpu.CompilerParams(dimension_semantics=("arbitrary",)),
    )(lo, mid, hi)


def reduce_members(part, axis):
    members = lax.axis_size(axis)
    if members & (members - 1) or part.size % (members * 1024):
        return lax.psum(part, axis) / members
    me = lax.axis_index(axis)
    rows = part.reshape(-1, 128)
    bits = members.bit_length() - 1
    for b in range(bits):
        mask = 1 << b
        half = rows.shape[0] // 2
        upper = (me // mask) % 2
        keep = lax.dynamic_slice_in_dim(rows, upper * half, half, 0)
        give = lax.dynamic_slice_in_dim(rows, (1 - upper) * half, half, 0)
        pairs = [(i, i ^ mask) for i in range(members)]
        rows = keep + lax.ppermute(give, axis, pairs)
    rows = rows / members
    for b in reversed(range(bits)):
        mask = 1 << b
        upper = (me // mask) % 2
        pairs = [(i, i ^ mask) for i in range(members)]
        other = lax.ppermute(rows, axis, pairs)
        rows = jnp.where(upper == 1, jnp.concatenate([other, rows]), jnp.concatenate([rows, other]))
    return rows.reshape(part.shape)


def swap_halos(bottom, top, axis):
    count = lax.axis_size(axis)
    odd = lax.axis_index(axis) % 2 == 1
    first = [(i, i ^ 1) for i in range(count) if i ^ 1 < count]
    second = [(i, i + 1) for i in range(1, count - 1, 2)] + [(i + 1, i) for i in range(1, count - 1, 2)]
    got_first = lax.ppermute(jnp.where(odd, bottom, top), axis, first)
    got_second = lax.ppermute(jnp.where(odd, top, bottom), axis, second)
    return jnp.where(odd, got_first, got_second), jnp.where(odd, got_second, got_first)


def halos(block, axis):
    planes = block.shape[0]
    return swap_halos(block[:HALO], block[planes - HALO:], axis)


def edge_halos(low_edge, high_edge, axis):
    return swap_halos(low_edge, high_edge, axis)


def inject(field, where, valid, values):
    flat = field.reshape(-1).at[where].add(jnp.where(valid, values, 0.0))
    return flat.reshape(field.shape)


def shards(
    courant,
    prev_field,
    cur_field,
    adj_prev,
    adj_cur,
    buoyancy,
    wavelet,
    src_cell,
    rec_cell,
    observed,
):
    speed = courant[0]
    planes, height, depth = buoyancy.shape
    volume = planes * height * depth
    offset = lax.axis_index("tile") * volume
    steps = wavelet.shape[0]

    def locate(cells):
        local = cells - offset
        valid = (local >= 0) & (local < volume)
        return (jnp.clip(local, 0, volume - 1), valid)

    src_local, src_valid = locate(src_cell)
    rec_local, rec_valid = locate(rec_cell)
    b_lo, b_hi = halos(buoyancy, "tile")

    def spread(cells):
        return jnp.stack([cells // (height * depth), (cells // depth) % height, cells % depth])

    where = jnp.concatenate([spread(src_local)[:, 0], src_valid.astype(jnp.int32)])
    receivers = spread(rec_local)
    older, now = (prev_field[0], cur_field[0])
    lo, hi = halos(now, "tile")
    forces = []
    samples = []
    grad_b = None
    for k in range(steps):
        track = (where, wavelet[k:k + 1], receivers)
        if grad_b is None:
            outs = apply_step(lo, now, hi, (b_lo, buoyancy, b_hi), None, speed, older, track)
            force, newer = outs[:2]
            grad_b = outs[2:5]
            edge_lo, edge_hi, lines = outs[5:]
        else:
            force, newer, edge_lo, edge_hi, lines = apply_step(lo, now, hi, buoyancy, grad_b, speed, older, track)
        if k + 1 < steps:
            lo, hi = edge_halos(edge_lo, edge_hi, "tile")
        samples.append(jnp.sum(lines, axis=1))
        forces.append(force)
        older, now = (now, newer)
    residual = jnp.where(rec_valid, jnp.stack(samples) - observed, 0.0)
    older, now = (adj_prev[0], adj_cur[0])
    image_part = jnp.zeros(buoyancy.shape, jnp.float32)
    for j in range(steps):
        lo, hi = halos(now, "tile")
        (newer,) = apply_step(lo, now, hi, buoyancy, grad_b, speed, older, want_force=False)
        newer = inject(newer, rec_local, rec_valid, residual[steps - 1 - j])
        image_part = image_part + newer * forces[steps - 1 - j]
        older, now = (now, newer)
    image = reduce_members(image_part, "real")
    return (image, now[None])


def solution(mesh):
    in_specs = (
        P("real", "tile", None, None),
        P(("shot", "real"), "tile", None, None),
        P(("shot", "real"), "tile", None, None),
        P(("shot", "real"), "tile", None, None),
        P(("shot", "real"), "tile", None, None),
        P("tile", None, None),
        P("shot"),
        P("shot"),
        P("shot"),
        P("shot", None),
    )
    out_specs = (P(("shot", "tile"), None, None), P(("shot", "real"), "tile", None, None))
    return jax.shard_map(shards, mesh=mesh, in_specs=in_specs, out_specs=out_specs, check_vma=False)
```

```python
import functools
import jax
import jax.numpy as jnp
from jax import lax
from jax.experimental import pallas as pl
from jax.experimental.pallas import tpu as pltpu
from jax.sharding import PartitionSpec as P

SECOND = (-205.0 / 72.0, 8.0 / 5.0, -1.0 / 5.0, 8.0 / 315.0, -1.0 / 560.0)
FIRST = (4.0 / 5.0, -1.0 / 5.0, 4.0 / 105.0, -1.0 / 280.0)
HALO = 4
PADY = 8


def lane_shift(v, k, lane):
    width = v.shape[-1]
    if k > 0:
        rolled = pltpu.roll(v, width - k, 1)
        return jnp.where(lane < width - k, rolled, 0.0)
    rolled = pltpu.roll(v, -k, 1)
    return jnp.where(lane >= -k, rolled, 0.0)


def fill_padded(pad_ref, first_ref, mid_ref, second_ref, odd):
    planes, height, depth = mid_ref.shape
    pad_ref[...] = jnp.zeros(pad_ref.shape, jnp.float32)
    first = first_ref[...]
    second = second_ref[...]
    pad_ref[0:HALO, PADY:PADY + height, :] = jnp.where(odd, first, second)
    pad_ref[HALO:HALO + planes, PADY:PADY + height, :] = mid_ref[...]
    pad_ref[HALO + planes:, PADY:PADY + height, :] = jnp.where(odd, second, first)


def taps(pad_ref, plane, y0, rows, lane):
    def at(dx, dy):
        return pad_ref[plane + dx, pl.ds(PADY + y0 + dy, rows), :]
    centre = at(0, 0)
    lap = 3.0 * SECOND[0] * centre
    grads = []
    for axis in range(3):
        if axis == 0:
            get = lambda k: at(k, 0)
        elif axis == 1:
            get = lambda k: at(0, k)
        else:
            get = lambda k: lane_shift(centre, k, lane)
        vals = {k: get(k) for k in (1, 2, 3, 4, -1, -2, -3, -4)}
        for k in range(1, 5):
            lap = lap + SECOND[k] * (vals[k] + vals[-k])
        slope = FIRST[0] * (vals[1] - vals[-1])
        for k in range(2, 5):
            slope = slope + FIRST[k - 1] * (vals[k] - vals[-k])
        grads.append(slope)
    return centre, lap, grads


def step_kernel(*refs, block, rows, track, own_grad, want_force):
    refs = list(refs)
    take = lambda n: [refs.pop(0) for _ in range(n)]
    (parity_ref,) = take(1)
    lo_ref, mid_ref, hi_ref = take(3)
    if own_grad:
        b_lo_ref, b_mid_ref, b_hi_ref = take(3)
    else:
        b_ref, g0_ref, g1_ref, g2_ref = take(4)
    c_ref, old_ref = take(2)
    if track:
        where_ref, amount_ref, rec_ref = take(3)
    force_ref = take(1)[0] if want_force else None
    (new_ref,) = take(1)
    if own_grad:
        g_out = take(3)
    if track:
        edge_lo_ref, edge_hi_ref, sample_ref = take(3)
    (pad_ref,) = take(1)
    if own_grad:
        (b_pad_ref,) = take(1)
    if track:
        (keep_ref,) = take(1)
    i = pl.program_id(0)

    odd = parity_ref[0] == 1

    @pl.when(i == 0)
    def _():
        fill_padded(pad_ref, lo_ref, mid_ref, hi_ref, odd)
        if own_grad:
            fill_padded(b_pad_ref, b_lo_ref, b_mid_ref, b_hi_ref, odd)

    planes = mid_ref.shape[0]
    height = c_ref.shape[1]
    depth = c_ref.shape[2]
    lane = lax.broadcasted_iota(jnp.int32, (rows, depth), 1)
    row = lax.broadcasted_iota(jnp.int32, (rows, depth), 0)
    for p in range(block):
        plane = i * block + p + HALO
        for y0 in range(0, height, rows):
            sl = (p, pl.ds(y0, rows), slice(None))
            centre, lap, grads = taps(pad_ref, plane, y0, rows, lane)
            if own_grad:
                bvals, _, gb = taps(b_pad_ref, plane, y0, rows, lane)
                for out_ref, value in zip(g_out, gb):
                    out_ref[sl] = value
            else:
                bvals = b_ref[sl]
                gb = [g0_ref[sl], g1_ref[sl], g2_ref[sl]]
            force = bvals * lap + (gb[0] * grads[0] + gb[1] * grads[1] + gb[2] * grads[2])
            if want_force:
                force_ref[sl] = force
            newer = 2.0 * centre - old_ref[sl] + c_ref[sl] * force
            if track:
                hit = (where_ref[3] == 1) & (where_ref[0] == plane - HALO)
                mask = hit & (row == where_ref[1] - y0) & (lane == where_ref[2])
                newer = jnp.where(mask, newer + amount_ref[0], newer)
                keep_ref[plane - HALO, pl.ds(y0, rows), :] = newer
            new_ref[sl] = newer

    if track:
        @pl.when(i == pl.num_programs(0) - 1)
        def _():
            bottom = keep_ref[0:HALO]
            top = keep_ref[planes - HALO:planes]
            edge_lo_ref[...] = jnp.where(odd, bottom, top)
            edge_hi_ref[...] = jnp.where(odd, top, bottom)
            one_lane = lax.broadcasted_iota(jnp.int32, (1, depth), 1)

            def sample(r, carry):
                x = rec_ref[0, r]
                y = rec_ref[1, r]
                z = rec_ref[2, r]
                line = keep_ref[x, pl.ds(y, 1), :]
                sample_ref[pl.ds(r, 1), :] = jnp.where(one_lane == z, line, 0.0)
                return carry

            lax.fori_loop(0, sample_ref.shape[0], sample, 0, unroll=8)


def grad_kernel(lo_ref, mid_ref, hi_ref, g0_ref, g1_ref, g2_ref, pad_ref, *, block, rows):
    i = pl.program_id(0)

    @pl.when(i == 0)
    def _():
        fill_padded(pad_ref, lo_ref, mid_ref, hi_ref)

    height = mid_ref.shape[1]
    lane = lax.broadcasted_iota(jnp.int32, (rows, mid_ref.shape[2]), 1)
    for p in range(block):
        plane = i * block + p + HALO
        for y0 in range(0, height, rows):
            sl = (p, pl.ds(y0, rows), slice(None))
            _, _, grads = taps(pad_ref, plane, y0, rows, lane)
            g0_ref[sl] = grads[0]
            g1_ref[sl] = grads[1]
            g2_ref[sl] = grads[2]


def pick_block(planes):
    for b in (4, 2, 1):
        if planes % b == 0:
            return b


def specs(shape, block):
    planes, height, depth = shape
    full = lambda s: pl.BlockSpec(s, lambda i: (0, 0, 0))
    blk = pl.BlockSpec((block, height, depth), lambda i: (i, 0, 0))
    return full, blk


def apply_step(parity, lo, mid, hi, b, g, c, old, track=None, rows=40, want_force=True):
    planes, height, depth = mid.shape
    block = pick_block(planes)
    full, blk = specs(mid.shape, block)
    out = jax.ShapeDtypeStruct(mid.shape, jnp.float32)
    own_grad = g is None
    in_specs = [pl.BlockSpec(memory_space=pltpu.SMEM), full(lo.shape), full(mid.shape), full(hi.shape)]
    args = [parity, lo, mid, hi]
    if own_grad:
        in_specs += [full(b[0].shape), full(b[1].shape), full(b[2].shape)]
        args += list(b)
    else:
        in_specs += [blk] * 4
        args += [b, g[0], g[1], g[2]]
    in_specs += [blk, blk]
    args += [c, old]
    out_specs = [blk] if want_force else []
    out_shape = [out] if want_force else []
    out_specs.append(blk)
    out_shape.append(out)
    if own_grad:
        out_specs += [blk] * 3
        out_shape += [out] * 3
    scratch = [pltpu.VMEM((planes + 2 * HALO, height + 2 * PADY, depth), jnp.float32)]
    if own_grad:
        scratch.append(pltpu.VMEM((planes + 2 * HALO, height + 2 * PADY, depth), jnp.float32))
    if track is not None:
        smem = pl.BlockSpec(memory_space=pltpu.SMEM)
        in_specs += [smem, smem, smem]
        args += list(track)
        count = track[2].shape[1]
        edge = jax.ShapeDtypeStruct((HALO, height, depth), jnp.float32)
        lines = jax.ShapeDtypeStruct((count, depth), jnp.float32)
        out_specs += [full(edge.shape), full(edge.shape), pl.BlockSpec((count, depth), lambda i: (0, 0))]
        out_shape += [edge, edge, lines]
        scratch.append(pltpu.VMEM(mid.shape, jnp.float32))
    kernel = functools.partial(
        step_kernel, block=block, rows=rows, track=track is not None, own_grad=own_grad, want_force=want_force
    )
    return pl.pallas_call(
        kernel,
        grid=(planes // block,),
        in_specs=in_specs,
        out_specs=out_specs,
        out_shape=out_shape,
        scratch_shapes=scratch,
        compiler_params=pltpu.CompilerParams(dimension_semantics=("arbitrary",)),
    )(*args)


def apply_grad(lo, mid, hi, rows=40):
    planes, height, depth = mid.shape
    block = pick_block(planes)
    full, blk = specs(mid.shape, block)
    out = jax.ShapeDtypeStruct(mid.shape, jnp.float32)
    return pl.pallas_call(
        functools.partial(grad_kernel, block=block, rows=rows),
        grid=(planes // block,),
        in_specs=[full(lo.shape), full(mid.shape), full(hi.shape)],
        out_specs=[blk, blk, blk],
        out_shape=[out, out, out],
        scratch_shapes=[pltpu.VMEM((planes + 2 * HALO, height + 2 * PADY, depth), jnp.float32)],
        compiler_params=pltpu.CompilerParams(dimension_semantics=("arbitrary",)),
    )(lo, mid, hi)


def reduce_members(part, axis):
    members = lax.axis_size(axis)
    if members & (members - 1) or part.size % (members * 1024):
        return lax.psum(part, axis) / members
    me = lax.axis_index(axis)
    rows = part.reshape(-1, 128)
    bits = members.bit_length() - 1
    for b in range(bits):
        mask = 1 << b
        half = rows.shape[0] // 2
        upper = (me // mask) % 2
        keep = lax.dynamic_slice_in_dim(rows, upper * half, half, 0)
        give = lax.dynamic_slice_in_dim(rows, (1 - upper) * half, half, 0)
        pairs = [(i, i ^ mask) for i in range(members)]
        rows = keep + lax.ppermute(give, axis, pairs)
    rows = rows / members
    for b in reversed(range(bits)):
        mask = 1 << b
        upper = (me // mask) % 2
        pairs = [(i, i ^ mask) for i in range(members)]
        other = lax.ppermute(rows, axis, pairs)
        rows = jnp.where(upper == 1, jnp.concatenate([other, rows]), jnp.concatenate([rows, other]))
    return rows.reshape(part.shape)


def swap_halos(sends, axis):
    count = lax.axis_size(axis)
    first = [(i, i ^ 1) for i in range(count) if i ^ 1 < count]
    second = [(i, i + 1) for i in range(1, count - 1, 2)] + [(i + 1, i) for i in range(1, count - 1, 2)]
    return lax.ppermute(sends[0], axis, first), lax.ppermute(sends[1], axis, second)


def halos(block, axis):
    planes = block.shape[0]
    odd = lax.axis_index(axis) % 2
    near = lax.dynamic_slice_in_dim(block, (1 - odd) * (planes - HALO), HALO, 0)
    far = lax.dynamic_slice_in_dim(block, odd * (planes - HALO), HALO, 0)
    return swap_halos((near, far), axis)


def inject(field, where, valid, values):
    flat = field.reshape(-1).at[where].add(jnp.where(valid, values, 0.0))
    return flat.reshape(field.shape)


def shards(
    courant,
    prev_field,
    cur_field,
    adj_prev,
    adj_cur,
    buoyancy,
    wavelet,
    src_cell,
    rec_cell,
    observed,
):
    speed = courant[0]
    planes, height, depth = buoyancy.shape
    volume = planes * height * depth
    offset = lax.axis_index("tile") * volume
    steps = wavelet.shape[0]

    def locate(cells):
        local = cells - offset
        valid = (local >= 0) & (local < volume)
        return (jnp.clip(local, 0, volume - 1), valid)

    src_local, src_valid = locate(src_cell)
    rec_local, rec_valid = locate(rec_cell)
    parity = (lax.axis_index("tile") % 2).astype(jnp.int32).reshape(1)
    b_lo, b_hi = halos(buoyancy, "tile")

    def spread(cells):
        return jnp.stack([cells // (height * depth), (cells // depth) % height, cells % depth])

    where = jnp.concatenate([spread(src_local)[:, 0], src_valid.astype(jnp.int32)])
    receivers = spread(rec_local)
    older, now = (prev_field[0], cur_field[0])
    lo, hi = halos(now, "tile")
    forces = []
    samples = []
    grad_b = None
    for k in range(steps):
        track = (where, wavelet[k:k + 1], receivers)
        if grad_b is None:
            outs = apply_step(parity, lo, now, hi, (b_lo, buoyancy, b_hi), None, speed, older, track)
            force, newer = outs[:2]
            grad_b = outs[2:5]
            edge_lo, edge_hi, lines = outs[5:]
        else:
            force, newer, edge_lo, edge_hi, lines = apply_step(parity, lo, now, hi, buoyancy, grad_b, speed, older, track)
        if k + 1 < steps:
            lo, hi = swap_halos((edge_lo, edge_hi), "tile")
        samples.append(jnp.sum(lines, axis=1))
        forces.append(force)
        older, now = (now, newer)
    residual = jnp.where(rec_valid, jnp.stack(samples) - observed, 0.0)
    older, now = (adj_prev[0], adj_cur[0])
    image_part = jnp.zeros(buoyancy.shape, jnp.float32)
    for j in range(steps):
        lo, hi = halos(now, "tile")
        (newer,) = apply_step(parity, lo, now, hi, buoyancy, grad_b, speed, older, want_force=False)
        newer = inject(newer, rec_local, rec_valid, residual[steps - 1 - j])
        image_part = image_part + newer * forces[steps - 1 - j]
        older, now = (now, newer)
    image = reduce_members(image_part, "real")
    return (image, now[None])


def solution(mesh):
    in_specs = (
        P("real", "tile", None, None),
        P(("shot", "real"), "tile", None, None),
        P(("shot", "real"), "tile", None, None),
        P(("shot", "real"), "tile", None, None),
        P(("shot", "real"), "tile", None, None),
        P("tile", None, None),
        P("shot"),
        P("shot"),
        P("shot"),
        P("shot", None),
    )
    out_specs = (P(("shot", "tile"), None, None), P(("shot", "real"), "tile", None, None))
    return jax.shard_map(shards, mesh=mesh, in_specs=in_specs, out_specs=out_specs, check_vma=False)
```

```python
import functools
import jax
import jax.numpy as jnp
from jax import lax
from jax.experimental import pallas as pl
from jax.experimental.pallas import tpu as pltpu
from jax.sharding import PartitionSpec as P

SECOND = (-205.0 / 72.0, 8.0 / 5.0, -1.0 / 5.0, 8.0 / 315.0, -1.0 / 560.0)
FIRST = (4.0 / 5.0, -1.0 / 5.0, 4.0 / 105.0, -1.0 / 280.0)
HALO = 4
PADY = 8


def lane_shift(v, k, lane):
    width = v.shape[-1]
    if k > 0:
        rolled = pltpu.roll(v, width - k, 1)
        return jnp.where(lane < width - k, rolled, 0.0)
    rolled = pltpu.roll(v, -k, 1)
    return jnp.where(lane >= -k, rolled, 0.0)


def fill_padded(pad_ref, first_ref, mid_ref, second_ref, odd):
    planes, height, depth = mid_ref.shape
    pad_ref[...] = jnp.zeros(pad_ref.shape, jnp.float32)
    first = first_ref[...]
    second = second_ref[...]
    pad_ref[0:HALO, PADY:PADY + height, :] = jnp.where(odd, first, second)
    pad_ref[HALO:HALO + planes, PADY:PADY + height, :] = mid_ref[...]
    pad_ref[HALO + planes:, PADY:PADY + height, :] = jnp.where(odd, second, first)


def taps(pad_ref, plane, y0, rows, lane):
    def at(dx, dy):
        return pad_ref[plane + dx, pl.ds(PADY + y0 + dy, rows), :]
    centre = at(0, 0)
    lap = 3.0 * SECOND[0] * centre
    grads = []
    for axis in range(3):
        if axis == 0:
            get = lambda k: at(k, 0)
        elif axis == 1:
            get = lambda k: at(0, k)
        else:
            get = lambda k: lane_shift(centre, k, lane)
        vals = {k: get(k) for k in (1, 2, 3, 4, -1, -2, -3, -4)}
        for k in range(1, 5):
            lap = lap + SECOND[k] * (vals[k] + vals[-k])
        slope = FIRST[0] * (vals[1] - vals[-1])
        for k in range(2, 5):
            slope = slope + FIRST[k - 1] * (vals[k] - vals[-k])
        grads.append(slope)
    return centre, lap, grads


def step_kernel(*refs, block, rows, track, own_grad, want_force):
    refs = list(refs)
    take = lambda n: [refs.pop(0) for _ in range(n)]
    (parity_ref,) = take(1)
    lo_ref, mid_ref, hi_ref = take(3)
    if own_grad:
        b_lo_ref, b_mid_ref, b_hi_ref = take(3)
    else:
        b_ref, g0_ref, g1_ref, g2_ref = take(4)
    c_ref, old_ref = take(2)
    if track:
        where_ref, amount_ref, rec_ref = take(3)
    force_ref = take(1)[0] if want_force else None
    (new_ref,) = take(1)
    if own_grad:
        g_out = take(3)
    if track:
        edge_lo_ref, edge_hi_ref, sample_ref = take(3)
    (pad_ref,) = take(1)
    if own_grad:
        (b_pad_ref,) = take(1)
    if track:
        (keep_ref,) = take(1)
    i = pl.program_id(0)

    odd = parity_ref[0] == 1

    @pl.when(i == 0)
    def _():
        fill_padded(pad_ref, lo_ref, mid_ref, hi_ref, odd)
        if own_grad:
            fill_padded(b_pad_ref, b_lo_ref, b_mid_ref, b_hi_ref, odd)

    planes = mid_ref.shape[0]
    height = c_ref.shape[1]
    depth = c_ref.shape[2]
    lane = lax.broadcasted_iota(jnp.int32, (rows, depth), 1)
    row = lax.broadcasted_iota(jnp.int32, (rows, depth), 0)
    for p in range(block):
        plane = i * block + p + HALO
        for y0 in range(0, height, rows):
            sl = (p, pl.ds(y0, rows), slice(None))
            centre, lap, grads = taps(pad_ref, plane, y0, rows, lane)
            if own_grad:
                bvals, _, gb = taps(b_pad_ref, plane, y0, rows, lane)
                for out_ref, value in zip(g_out, gb):
                    out_ref[sl] = value
            else:
                bvals = b_ref[sl]
                gb = [g0_ref[sl], g1_ref[sl], g2_ref[sl]]
            force = bvals * lap + (gb[0] * grads[0] + gb[1] * grads[1] + gb[2] * grads[2])
            if want_force:
                force_ref[sl] = force
            newer = 2.0 * centre - old_ref[sl] + c_ref[sl] * force
            if track:
                hit = (where_ref[3] == 1) & (where_ref[0] == plane - HALO)
                mask = hit & (row == where_ref[1] - y0) & (lane == where_ref[2])
                newer = jnp.where(mask, newer + amount_ref[0], newer)
                keep_ref[plane - HALO, pl.ds(y0, rows), :] = newer
            new_ref[sl] = newer

    if track:
        @pl.when(i == pl.num_programs(0) - 1)
        def _():
            bottom = keep_ref[0:HALO]
            top = keep_ref[planes - HALO:planes]
            edge_lo_ref[...] = jnp.where(odd, bottom, top)
            edge_hi_ref[...] = jnp.where(odd, top, bottom)
            one_lane = lax.broadcasted_iota(jnp.int32, (1, depth), 1)

            def sample(r, carry):
                x = rec_ref[0, r]
                y = rec_ref[1, r]
                z = rec_ref[2, r]
                line = keep_ref[x, pl.ds(y, 1), :]
                sample_ref[pl.ds(r, 1), :] = jnp.where(one_lane == z, line, 0.0)
                return carry

            lax.fori_loop(0, sample_ref.shape[0], sample, 0, unroll=8)


def grad_kernel(lo_ref, mid_ref, hi_ref, g0_ref, g1_ref, g2_ref, pad_ref, *, block, rows):
    i = pl.program_id(0)

    @pl.when(i == 0)
    def _():
        fill_padded(pad_ref, lo_ref, mid_ref, hi_ref)

    height = mid_ref.shape[1]
    lane = lax.broadcasted_iota(jnp.int32, (rows, mid_ref.shape[2]), 1)
    for p in range(block):
        plane = i * block + p + HALO
        for y0 in range(0, height, rows):
            sl = (p, pl.ds(y0, rows), slice(None))
            _, _, grads = taps(pad_ref, plane, y0, rows, lane)
            g0_ref[sl] = grads[0]
            g1_ref[sl] = grads[1]
            g2_ref[sl] = grads[2]


def final_kernel(parity_ref, lo_ref, mid_ref, hi_ref, b_ref, g0_ref, g1_ref, g2_ref, c_ref, old_ref,
                 rec_ref, valid_ref, amount_ref, part_ref, force_ref, new_ref, image_ref, pad_ref, *, block, rows):
    i = pl.program_id(0)
    odd = parity_ref[0] == 1

    @pl.when(i == 0)
    def _():
        fill_padded(pad_ref, lo_ref, mid_ref, hi_ref, odd)

    planes, height, depth = mid_ref.shape
    lane = lax.broadcasted_iota(jnp.int32, (rows, depth), 1)
    for p in range(block):
        plane = i * block + p + HALO
        for y0 in range(0, height, rows):
            sl = (p, pl.ds(y0, rows), slice(None))
            centre, lap, grads = taps(pad_ref, plane, y0, rows, lane)
            force = b_ref[sl] * lap + (g0_ref[sl] * grads[0] + g1_ref[sl] * grads[1] + g2_ref[sl] * grads[2])
            new_ref[plane - HALO, pl.ds(y0, rows), :] = 2.0 * centre - old_ref[sl] + c_ref[sl] * force

    @pl.when(i == pl.num_programs(0) - 1)
    def _():
        one_lane = lax.broadcasted_iota(jnp.int32, (1, depth), 1)

        def add(r, carry):
            x = rec_ref[0, r]
            y = rec_ref[1, r]
            hit = (one_lane == rec_ref[2, r]) & (valid_ref[r] == 1)
            line = new_ref[x, pl.ds(y, 1), :]
            new_ref[x, pl.ds(y, 1), :] = jnp.where(hit, line + amount_ref[r], line)
            return carry

        lax.fori_loop(0, amount_ref.shape[0], add, 0)
        for q in range(planes):
            image_ref[q] = part_ref[q] + new_ref[q] * force_ref[q]


def apply_final(parity, lo, mid, hi, b, g, c, old, receivers, valid, amount, part, force, rows=40):
    planes, height, depth = mid.shape
    block = pick_block(planes)
    full, blk = specs(mid.shape, block)
    out = jax.ShapeDtypeStruct(mid.shape, jnp.float32)
    smem = pl.BlockSpec(memory_space=pltpu.SMEM)
    return pl.pallas_call(
        functools.partial(final_kernel, block=block, rows=rows),
        grid=(planes // block,),
        in_specs=[smem, full(lo.shape), full(mid.shape), full(hi.shape)] + [blk] * 6
        + [smem, smem, smem, full(mid.shape), full(mid.shape)],
        out_specs=[full(mid.shape), full(mid.shape)],
        out_shape=[out, out],
        scratch_shapes=[pltpu.VMEM((planes + 2 * HALO, height + 2 * PADY, depth), jnp.float32)],
        compiler_params=pltpu.CompilerParams(dimension_semantics=("arbitrary",)),
    )(parity, lo, mid, hi, b, g[0], g[1], g[2], c, old, receivers, valid, amount, part, force)


def pick_block(planes):
    for b in (4, 2, 1):
        if planes % b == 0:
            return b


def specs(shape, block):
    planes, height, depth = shape
    full = lambda s: pl.BlockSpec(s, lambda i: (0, 0, 0))
    blk = pl.BlockSpec((block, height, depth), lambda i: (i, 0, 0))
    return full, blk


def apply_step(parity, lo, mid, hi, b, g, c, old, track=None, rows=40, want_force=True):
    planes, height, depth = mid.shape
    block = pick_block(planes)
    full, blk = specs(mid.shape, block)
    out = jax.ShapeDtypeStruct(mid.shape, jnp.float32)
    own_grad = g is None
    in_specs = [pl.BlockSpec(memory_space=pltpu.SMEM), full(lo.shape), full(mid.shape), full(hi.shape)]
    args = [parity, lo, mid, hi]
    if own_grad:
        in_specs += [full(b[0].shape), full(b[1].shape), full(b[2].shape)]
        args += list(b)
    else:
        in_specs += [blk] * 4
        args += [b, g[0], g[1], g[2]]
    in_specs += [blk, blk]
    args += [c, old]
    out_specs = [blk] if want_force else []
    out_shape = [out] if want_force else []
    out_specs.append(blk)
    out_shape.append(out)
    if own_grad:
        out_specs += [blk] * 3
        out_shape += [out] * 3
    scratch = [pltpu.VMEM((planes + 2 * HALO, height + 2 * PADY, depth), jnp.float32)]
    if own_grad:
        scratch.append(pltpu.VMEM((planes + 2 * HALO, height + 2 * PADY, depth), jnp.float32))
    if track is not None:
        smem = pl.BlockSpec(memory_space=pltpu.SMEM)
        in_specs += [smem, smem, smem]
        args += list(track)
        count = track[2].shape[1]
        edge = jax.ShapeDtypeStruct((HALO, height, depth), jnp.float32)
        lines = jax.ShapeDtypeStruct((count, depth), jnp.float32)
        out_specs += [full(edge.shape), full(edge.shape), pl.BlockSpec((count, depth), lambda i: (0, 0))]
        out_shape += [edge, edge, lines]
        scratch.append(pltpu.VMEM(mid.shape, jnp.float32))
    kernel = functools.partial(
        step_kernel, block=block, rows=rows, track=track is not None, own_grad=own_grad, want_force=want_force
    )
    return pl.pallas_call(
        kernel,
        grid=(planes // block,),
        in_specs=in_specs,
        out_specs=out_specs,
        out_shape=out_shape,
        scratch_shapes=scratch,
        compiler_params=pltpu.CompilerParams(dimension_semantics=("arbitrary",)),
    )(*args)


def apply_grad(lo, mid, hi, rows=40):
    planes, height, depth = mid.shape
    block = pick_block(planes)
    full, blk = specs(mid.shape, block)
    out = jax.ShapeDtypeStruct(mid.shape, jnp.float32)
    return pl.pallas_call(
        functools.partial(grad_kernel, block=block, rows=rows),
        grid=(planes // block,),
        in_specs=[full(lo.shape), full(mid.shape), full(hi.shape)],
        out_specs=[blk, blk, blk],
        out_shape=[out, out, out],
        scratch_shapes=[pltpu.VMEM((planes + 2 * HALO, height + 2 * PADY, depth), jnp.float32)],
        compiler_params=pltpu.CompilerParams(dimension_semantics=("arbitrary",)),
    )(lo, mid, hi)


def reduce_members(part, axis):
    members = lax.axis_size(axis)
    if members & (members - 1) or part.size % (members * 1024):
        return lax.psum(part, axis) / members
    me = lax.axis_index(axis)
    rows = part.reshape(-1, 128)
    bits = members.bit_length() - 1
    for b in range(bits):
        mask = 1 << b
        half = rows.shape[0] // 2
        upper = (me // mask) % 2
        keep = lax.dynamic_slice_in_dim(rows, upper * half, half, 0)
        give = lax.dynamic_slice_in_dim(rows, (1 - upper) * half, half, 0)
        pairs = [(i, i ^ mask) for i in range(members)]
        rows = keep + lax.ppermute(give, axis, pairs)
    rows = rows / members
    for b in reversed(range(bits)):
        mask = 1 << b
        upper = (me // mask) % 2
        pairs = [(i, i ^ mask) for i in range(members)]
        other = lax.ppermute(rows, axis, pairs)
        rows = jnp.where(upper == 1, jnp.concatenate([other, rows]), jnp.concatenate([rows, other]))
    return rows.reshape(part.shape)


def swap_halos(sends, axis):
    count = lax.axis_size(axis)
    first = [(i, i ^ 1) for i in range(count) if i ^ 1 < count]
    second = [(i, i + 1) for i in range(1, count - 1, 2)] + [(i + 1, i) for i in range(1, count - 1, 2)]
    return lax.ppermute(sends[0], axis, first), lax.ppermute(sends[1], axis, second)


def halos(block, axis):
    planes = block.shape[0]
    odd = lax.axis_index(axis) % 2
    near = lax.dynamic_slice_in_dim(block, (1 - odd) * (planes - HALO), HALO, 0)
    far = lax.dynamic_slice_in_dim(block, odd * (planes - HALO), HALO, 0)
    return swap_halos((near, far), axis)


def inject(field, where, valid, values):
    flat = field.reshape(-1).at[where].add(jnp.where(valid, values, 0.0))
    return flat.reshape(field.shape)


def shards(
    courant,
    prev_field,
    cur_field,
    adj_prev,
    adj_cur,
    buoyancy,
    wavelet,
    src_cell,
    rec_cell,
    observed,
):
    speed = courant[0]
    planes, height, depth = buoyancy.shape
    volume = planes * height * depth
    offset = lax.axis_index("tile") * volume
    steps = wavelet.shape[0]

    def locate(cells):
        local = cells - offset
        valid = (local >= 0) & (local < volume)
        return (jnp.clip(local, 0, volume - 1), valid)

    src_local, src_valid = locate(src_cell)
    rec_local, rec_valid = locate(rec_cell)
    parity = (lax.axis_index("tile") % 2).astype(jnp.int32).reshape(1)
    b_lo, b_hi = halos(buoyancy, "tile")

    def spread(cells):
        return jnp.stack([cells // (height * depth), (cells // depth) % height, cells % depth])

    where = jnp.concatenate([spread(src_local)[:, 0], src_valid.astype(jnp.int32)])
    receivers = spread(rec_local)
    older, now = (prev_field[0], cur_field[0])
    lo, hi = halos(now, "tile")
    forces = []
    samples = []
    grad_b = None
    for k in range(steps):
        track = (where, wavelet[k:k + 1], receivers)
        if grad_b is None:
            outs = apply_step(parity, lo, now, hi, (b_lo, buoyancy, b_hi), None, speed, older, track)
            force, newer = outs[:2]
            grad_b = outs[2:5]
            edge_lo, edge_hi, lines = outs[5:]
        else:
            force, newer, edge_lo, edge_hi, lines = apply_step(parity, lo, now, hi, buoyancy, grad_b, speed, older, track)
        if k + 1 < steps:
            lo, hi = swap_halos((edge_lo, edge_hi), "tile")
        samples.append(jnp.sum(lines, axis=1))
        forces.append(force)
        older, now = (now, newer)
    residual = jnp.where(rec_valid, jnp.stack(samples) - observed, 0.0)
    older, now = (adj_prev[0], adj_cur[0])
    image_part = jnp.zeros(buoyancy.shape, jnp.float32)
    for j in range(steps):
        lo, hi = halos(now, "tile")
        m = steps - 1 - j
        if j + 1 < steps:
            (newer,) = apply_step(parity, lo, now, hi, buoyancy, grad_b, speed, older, want_force=False)
            newer = inject(newer, rec_local, rec_valid, residual[m])
            image_part = image_part + newer * forces[m]
        else:
            valid = rec_valid.astype(jnp.int32)
            newer, image_part = apply_final(
                parity, lo, now, hi, buoyancy, grad_b, speed, older, receivers, valid, residual[m], image_part, forces[m]
            )
        older, now = (now, newer)
    image = reduce_members(image_part, "real")
    return (image, now[None])


def solution(mesh):
    in_specs = (
        P("real", "tile", None, None),
        P(("shot", "real"), "tile", None, None),
        P(("shot", "real"), "tile", None, None),
        P(("shot", "real"), "tile", None, None),
        P(("shot", "real"), "tile", None, None),
        P("tile", None, None),
        P("shot"),
        P("shot"),
        P("shot"),
        P("shot", None),
    )
    out_specs = (P(("shot", "tile"), None, None), P(("shot", "real"), "tile", None, None))
    return jax.shard_map(shards, mesh=mesh, in_specs=in_specs, out_specs=out_specs, check_vma=False)
```

```python
import functools
import jax
import jax.numpy as jnp
from jax import lax
from jax.experimental import pallas as pl
from jax.experimental.pallas import tpu as pltpu
from jax.sharding import PartitionSpec as P

SECOND = (-205.0 / 72.0, 8.0 / 5.0, -1.0 / 5.0, 8.0 / 315.0, -1.0 / 560.0)
FIRST = (4.0 / 5.0, -1.0 / 5.0, 4.0 / 105.0, -1.0 / 280.0)
HALO = 4
PADY = 8


def lane_shift(v, k, lane):
    width = v.shape[-1]
    if k > 0:
        rolled = pltpu.roll(v, width - k, 1)
        return jnp.where(lane < width - k, rolled, 0.0)
    rolled = pltpu.roll(v, -k, 1)
    return jnp.where(lane >= -k, rolled, 0.0)


def fill_padded(pad_ref, first_ref, mid_ref, second_ref, odd):
    planes, height, depth = mid_ref.shape
    pad_ref[...] = jnp.zeros(pad_ref.shape, jnp.float32)
    first = first_ref[...]
    second = second_ref[...]
    pad_ref[0:HALO, PADY:PADY + height, :] = jnp.where(odd, first, second)
    pad_ref[HALO:HALO + planes, PADY:PADY + height, :] = mid_ref[...]
    pad_ref[HALO + planes:, PADY:PADY + height, :] = jnp.where(odd, second, first)


def taps(pad_ref, plane, y0, rows, lane):
    def at(dx, dy):
        return pad_ref[plane + dx, pl.ds(PADY + y0 + dy, rows), :]
    centre = at(0, 0)
    lap = 3.0 * SECOND[0] * centre
    grads = []
    for axis in range(3):
        if axis == 0:
            get = lambda k: at(k, 0)
        elif axis == 1:
            get = lambda k: at(0, k)
        else:
            get = lambda k: lane_shift(centre, k, lane)
        vals = {k: get(k) for k in (1, 2, 3, 4, -1, -2, -3, -4)}
        for k in range(1, 5):
            lap = lap + SECOND[k] * (vals[k] + vals[-k])
        slope = FIRST[0] * (vals[1] - vals[-1])
        for k in range(2, 5):
            slope = slope + FIRST[k - 1] * (vals[k] - vals[-k])
        grads.append(slope)
    return centre, lap, grads


def step_kernel(*refs, block, rows, track, own_grad, want_force, edges):
    refs = list(refs)
    take = lambda n: [refs.pop(0) for _ in range(n)]
    (parity_ref,) = take(1)
    lo_ref, mid_ref, hi_ref = take(3)
    if own_grad:
        b_lo_ref, b_mid_ref, b_hi_ref = take(3)
    else:
        b_ref, g0_ref, g1_ref, g2_ref = take(4)
    c_ref, old_ref = take(2)
    if track:
        where_ref, amount_ref, rec_ref = take(3)
    force_ref = take(1)[0] if want_force else None
    (new_ref,) = take(1)
    if own_grad:
        g_out = take(3)
    if track and edges:
        edge_lo_ref, edge_hi_ref = take(2)
    if track:
        (sample_ref,) = take(1)
    (pad_ref,) = take(1)
    if own_grad:
        (b_pad_ref,) = take(1)
    if track:
        (keep_ref,) = take(1)
    i = pl.program_id(0)

    odd = parity_ref[0] == 1

    @pl.when(i == 0)
    def _():
        fill_padded(pad_ref, lo_ref, mid_ref, hi_ref, odd)
        if own_grad:
            fill_padded(b_pad_ref, b_lo_ref, b_mid_ref, b_hi_ref, odd)

    planes = mid_ref.shape[0]
    height = c_ref.shape[1]
    depth = c_ref.shape[2]
    lane = lax.broadcasted_iota(jnp.int32, (rows, depth), 1)
    row = lax.broadcasted_iota(jnp.int32, (rows, depth), 0)
    for p in range(block):
        plane = i * block + p + HALO
        for y0 in range(0, height, rows):
            sl = (p, pl.ds(y0, rows), slice(None))
            centre, lap, grads = taps(pad_ref, plane, y0, rows, lane)
            if own_grad:
                bvals, _, gb = taps(b_pad_ref, plane, y0, rows, lane)
                for out_ref, value in zip(g_out, gb):
                    out_ref[sl] = value
            else:
                bvals = b_ref[sl]
                gb = [g0_ref[sl], g1_ref[sl], g2_ref[sl]]
            force = bvals * lap + (gb[0] * grads[0] + gb[1] * grads[1] + gb[2] * grads[2])
            if want_force:
                force_ref[sl] = force
            newer = 2.0 * centre - old_ref[sl] + c_ref[sl] * force
            if track:
                hit = (where_ref[3] == 1) & (where_ref[0] == plane - HALO)
                mask = hit & (row == where_ref[1] - y0) & (lane == where_ref[2])
                newer = jnp.where(mask, newer + amount_ref[0], newer)
                keep_ref[pl.ds(pl.multiple_of((plane - HALO) * height + y0, 8), rows), :] = newer
            new_ref[sl] = newer

    if track:
        @pl.when(i == pl.num_programs(0) - 1)
        def _():
            if edges:
                for q in range(HALO):
                    bottom = keep_ref[q * height:(q + 1) * height, :]
                    top = keep_ref[(planes - HALO + q) * height:(planes - HALO + q + 1) * height, :]
                    edge_lo_ref[q] = jnp.where(odd, bottom, top)
                    edge_hi_ref[q] = jnp.where(odd, top, bottom)
            one_lane = lax.broadcasted_iota(jnp.int32, (1, depth), 1)

            def sample(r, carry):
                line = keep_ref[pl.ds(rec_ref[0, r], 1), :]
                sample_ref[pl.ds(r, 1), :] = jnp.where(one_lane == rec_ref[1, r], line, 0.0)
                return carry

            lax.fori_loop(0, sample_ref.shape[0], sample, 0, unroll=8)


def grad_kernel(lo_ref, mid_ref, hi_ref, g0_ref, g1_ref, g2_ref, pad_ref, *, block, rows):
    i = pl.program_id(0)

    @pl.when(i == 0)
    def _():
        fill_padded(pad_ref, lo_ref, mid_ref, hi_ref)

    height = mid_ref.shape[1]
    lane = lax.broadcasted_iota(jnp.int32, (rows, mid_ref.shape[2]), 1)
    for p in range(block):
        plane = i * block + p + HALO
        for y0 in range(0, height, rows):
            sl = (p, pl.ds(y0, rows), slice(None))
            _, _, grads = taps(pad_ref, plane, y0, rows, lane)
            g0_ref[sl] = grads[0]
            g1_ref[sl] = grads[1]
            g2_ref[sl] = grads[2]


def pick_block(planes):
    for b in (4, 2, 1):
        if planes % b == 0:
            return b


def specs(shape, block):
    planes, height, depth = shape
    full = lambda s: pl.BlockSpec(s, lambda i: (0, 0, 0))
    blk = pl.BlockSpec((block, height, depth), lambda i: (i, 0, 0))
    return full, blk


def apply_step(parity, lo, mid, hi, b, g, c, old, track=None, rows=40, want_force=True, edges=True):
    planes, height, depth = mid.shape
    block = pick_block(planes)
    full, blk = specs(mid.shape, block)
    out = jax.ShapeDtypeStruct(mid.shape, jnp.float32)
    own_grad = g is None
    in_specs = [pl.BlockSpec(memory_space=pltpu.SMEM), full(lo.shape), full(mid.shape), full(hi.shape)]
    args = [parity, lo, mid, hi]
    if own_grad:
        in_specs += [full(b[0].shape), full(b[1].shape), full(b[2].shape)]
        args += list(b)
    else:
        in_specs += [blk] * 4
        args += [b, g[0], g[1], g[2]]
    in_specs += [blk, blk]
    args += [c, old]
    out_specs = [blk] if want_force else []
    out_shape = [out] if want_force else []
    out_specs.append(blk)
    out_shape.append(out)
    if own_grad:
        out_specs += [blk] * 3
        out_shape += [out] * 3
    scratch = [pltpu.VMEM((planes + 2 * HALO, height + 2 * PADY, depth), jnp.float32)]
    if own_grad:
        scratch.append(pltpu.VMEM((planes + 2 * HALO, height + 2 * PADY, depth), jnp.float32))
    if track is not None:
        smem = pl.BlockSpec(memory_space=pltpu.SMEM)
        in_specs += [smem, smem, smem]
        args += list(track)
        count = track[2].shape[1]
        edge = jax.ShapeDtypeStruct((HALO, height, depth), jnp.float32)
        lines = jax.ShapeDtypeStruct((count, depth), jnp.float32)
        if edges:
            out_specs += [full(edge.shape), full(edge.shape)]
            out_shape += [edge, edge]
        out_specs.append(pl.BlockSpec((count, depth), lambda i: (0, 0)))
        out_shape.append(lines)
        scratch.append(pltpu.VMEM((planes * height, depth), jnp.float32))
    kernel = functools.partial(
        step_kernel, block=block, rows=rows, track=track is not None, own_grad=own_grad, want_force=want_force,
        edges=edges,
    )
    return pl.pallas_call(
        kernel,
        grid=(planes // block,),
        in_specs=in_specs,
        out_specs=out_specs,
        out_shape=out_shape,
        scratch_shapes=scratch,
        compiler_params=pltpu.CompilerParams(dimension_semantics=("arbitrary",)),
    )(*args)


def apply_grad(lo, mid, hi, rows=40):
    planes, height, depth = mid.shape
    block = pick_block(planes)
    full, blk = specs(mid.shape, block)
    out = jax.ShapeDtypeStruct(mid.shape, jnp.float32)
    return pl.pallas_call(
        functools.partial(grad_kernel, block=block, rows=rows),
        grid=(planes // block,),
        in_specs=[full(lo.shape), full(mid.shape), full(hi.shape)],
        out_specs=[blk, blk, blk],
        out_shape=[out, out, out],
        scratch_shapes=[pltpu.VMEM((planes + 2 * HALO, height + 2 * PADY, depth), jnp.float32)],
        compiler_params=pltpu.CompilerParams(dimension_semantics=("arbitrary",)),
    )(lo, mid, hi)


def reduce_members(part, axis):
    members = lax.axis_size(axis)
    if members & (members - 1) or part.size % (members * 1024):
        return lax.psum(part, axis) / members
    me = lax.axis_index(axis)
    rows = part.reshape(-1, 128)
    bits = members.bit_length() - 1
    for b in range(bits):
        mask = 1 << b
        half = rows.shape[0] // 2
        upper = (me // mask) % 2
        keep = lax.dynamic_slice_in_dim(rows, upper * half, half, 0)
        give = lax.dynamic_slice_in_dim(rows, (1 - upper) * half, half, 0)
        pairs = [(i, i ^ mask) for i in range(members)]
        rows = keep + lax.ppermute(give, axis, pairs)
    rows = rows / members
    for b in reversed(range(bits)):
        mask = 1 << b
        upper = (me // mask) % 2
        pairs = [(i, i ^ mask) for i in range(members)]
        other = lax.ppermute(rows, axis, pairs)
        rows = jnp.where(upper == 1, jnp.concatenate([other, rows]), jnp.concatenate([rows, other]))
    return rows.reshape(part.shape)


def swap_halos(sends, axis):
    count = lax.axis_size(axis)
    first = [(i, i ^ 1) for i in range(count) if i ^ 1 < count]
    second = [(i, i + 1) for i in range(1, count - 1, 2)] + [(i + 1, i) for i in range(1, count - 1, 2)]
    return lax.ppermute(sends[0], axis, first), lax.ppermute(sends[1], axis, second)


def halos(block, axis):
    planes = block.shape[0]
    odd = lax.axis_index(axis) % 2
    near = lax.dynamic_slice_in_dim(block, (1 - odd) * (planes - HALO), HALO, 0)
    far = lax.dynamic_slice_in_dim(block, odd * (planes - HALO), HALO, 0)
    return swap_halos((near, far), axis)


def inject(field, where, valid, values):
    flat = field.reshape(-1).at[where].add(jnp.where(valid, values, 0.0))
    return flat.reshape(field.shape)


def shards(
    courant,
    prev_field,
    cur_field,
    adj_prev,
    adj_cur,
    buoyancy,
    wavelet,
    src_cell,
    rec_cell,
    observed,
):
    speed = courant[0]
    planes, height, depth = buoyancy.shape
    volume = planes * height * depth
    offset = lax.axis_index("tile") * volume
    steps = wavelet.shape[0]

    def locate(cells):
        local = cells - offset
        valid = (local >= 0) & (local < volume)
        return (jnp.clip(local, 0, volume - 1), valid)

    src_local, src_valid = locate(src_cell)
    rec_local, rec_valid = locate(rec_cell)
    parity = (lax.axis_index("tile") % 2).astype(jnp.int32).reshape(1)
    b_lo, b_hi = halos(buoyancy, "tile")

    def spread(cells):
        return jnp.stack([cells // (height * depth), (cells // depth) % height, cells % depth])

    where = jnp.concatenate([spread(src_local)[:, 0], src_valid.astype(jnp.int32)])
    receivers = jnp.stack([rec_local // depth, rec_local % depth])
    older, now = (prev_field[0], cur_field[0])
    lo, hi = halos(now, "tile")
    forces = []
    samples = []
    grad_b = None
    for k in range(steps):
        track = (where, wavelet[k:k + 1], receivers)
        if grad_b is None:
            outs = apply_step(parity, lo, now, hi, (b_lo, buoyancy, b_hi), None, speed, older, track)
            force, newer = outs[:2]
            grad_b = outs[2:5]
            edge_lo, edge_hi, lines = outs[5:]
        else:
            outs = apply_step(parity, lo, now, hi, buoyancy, grad_b, speed, older, track, edges=k + 1 < steps)
            force, newer, lines = outs[0], outs[1], outs[-1]
            edge_lo, edge_hi = (outs[2], outs[3]) if k + 1 < steps else (None, None)
        if k + 1 < steps:
            lo, hi = swap_halos((edge_lo, edge_hi), "tile")
        samples.append(jnp.sum(lines, axis=1))
        forces.append(force)
        older, now = (now, newer)
    residual = jnp.where(rec_valid, jnp.stack(samples) - observed, 0.0)
    older, now = (adj_prev[0], adj_cur[0])
    image_part = jnp.zeros(buoyancy.shape, jnp.float32)
    for j in range(steps):
        lo, hi = halos(now, "tile")
        (newer,) = apply_step(parity, lo, now, hi, buoyancy, grad_b, speed, older, want_force=False)
        newer = inject(newer, rec_local, rec_valid, residual[steps - 1 - j])
        image_part = image_part + newer * forces[steps - 1 - j]
        older, now = (now, newer)
    image = reduce_members(image_part, "real")
    return (image, now[None])


def solution(mesh):
    in_specs = (
        P("real", "tile", None, None),
        P(("shot", "real"), "tile", None, None),
        P(("shot", "real"), "tile", None, None),
        P(("shot", "real"), "tile", None, None),
        P(("shot", "real"), "tile", None, None),
        P("tile", None, None),
        P("shot"),
        P("shot"),
        P("shot"),
        P("shot", None),
    )
    out_specs = (P(("shot", "tile"), None, None), P(("shot", "real"), "tile", None, None))
    return jax.shard_map(shards, mesh=mesh, in_specs=in_specs, out_specs=out_specs, check_vma=False)
```

```python
import functools
import jax
import jax.numpy as jnp
from jax import lax
from jax.experimental import pallas as pl
from jax.experimental.pallas import tpu as pltpu
from jax.sharding import PartitionSpec as P

SECOND = (-205.0 / 72.0, 8.0 / 5.0, -1.0 / 5.0, 8.0 / 315.0, -1.0 / 560.0)
FIRST = (4.0 / 5.0, -1.0 / 5.0, 4.0 / 105.0, -1.0 / 280.0)
HALO = 4
PADY = 8


def lane_shift(v, k, lane):
    width = v.shape[-1]
    if k > 0:
        rolled = pltpu.roll(v, width - k, 1)
        return jnp.where(lane < width - k, rolled, 0.0)
    rolled = pltpu.roll(v, -k, 1)
    return jnp.where(lane >= -k, rolled, 0.0)


def fill_padded(pad_ref, first_ref, mid_ref, second_ref, odd):
    planes, height, depth = mid_ref.shape
    pad_ref[...] = jnp.zeros(pad_ref.shape, jnp.float32)
    first = first_ref[...]
    second = second_ref[...]
    pad_ref[0:HALO, PADY:PADY + height, :] = jnp.where(odd, first, second)
    pad_ref[HALO:HALO + planes, PADY:PADY + height, :] = mid_ref[...]
    pad_ref[HALO + planes:, PADY:PADY + height, :] = jnp.where(odd, second, first)


def taps(pad_ref, plane, y0, rows, lane):
    def at(dx, dy):
        return pad_ref[plane + dx, pl.ds(PADY + y0 + dy, rows), :]
    centre = at(0, 0)
    lap = 3.0 * SECOND[0] * centre
    grads = []
    for axis in range(3):
        if axis == 0:
            get = lambda k: at(k, 0)
        elif axis == 1:
            get = lambda k: at(0, k)
        else:
            get = lambda k: lane_shift(centre, k, lane)
        vals = {k: get(k) for k in (1, 2, 3, 4, -1, -2, -3, -4)}
        for k in range(1, 5):
            lap = lap + SECOND[k] * (vals[k] + vals[-k])
        slope = FIRST[0] * (vals[1] - vals[-1])
        for k in range(2, 5):
            slope = slope + FIRST[k - 1] * (vals[k] - vals[-k])
        grads.append(slope)
    return centre, lap, grads


def step_kernel(*refs, block, rows, track, own_grad, want_force, edges):
    refs = list(refs)
    take = lambda n: [refs.pop(0) for _ in range(n)]
    (parity_ref,) = take(1)
    lo_ref, mid_ref, hi_ref = take(3)
    if own_grad:
        b_lo_ref, b_mid_ref, b_hi_ref = take(3)
    else:
        b_ref, g0_ref, g1_ref, g2_ref = take(4)
    c_ref, old_ref = take(2)
    if track:
        where_ref, amount_ref, rec_ref = take(3)
    force_ref = take(1)[0] if want_force else None
    (new_ref,) = take(1)
    if own_grad:
        g_out = take(3)
    if track and edges:
        edge_lo_ref, edge_hi_ref = take(2)
    if track:
        (sample_ref,) = take(1)
    (pad_ref,) = take(1)
    if own_grad:
        (b_pad_ref,) = take(1)
    if track:
        (keep_ref,) = take(1)
    i = pl.program_id(0)

    odd = parity_ref[0] == 1

    @pl.when(i == 0)
    def _():
        fill_padded(pad_ref, lo_ref, mid_ref, hi_ref, odd)
        if own_grad:
            fill_padded(b_pad_ref, b_lo_ref, b_mid_ref, b_hi_ref, odd)

    planes = mid_ref.shape[0]
    height = c_ref.shape[1]
    depth = c_ref.shape[2]
    lane = lax.broadcasted_iota(jnp.int32, (rows, depth), 1)
    row = lax.broadcasted_iota(jnp.int32, (rows, depth), 0)
    for p in range(block):
        plane = i * block + p + HALO
        for y0 in range(0, height, rows):
            sl = (p, pl.ds(y0, rows), slice(None))
            centre, lap, grads = taps(pad_ref, plane, y0, rows, lane)
            if own_grad:
                bvals, _, gb = taps(b_pad_ref, plane, y0, rows, lane)
                for out_ref, value in zip(g_out, gb):
                    out_ref[sl] = value
            else:
                bvals = b_ref[sl]
                gb = [g0_ref[sl], g1_ref[sl], g2_ref[sl]]
            force = bvals * lap + (gb[0] * grads[0] + gb[1] * grads[1] + gb[2] * grads[2])
            if want_force:
                force_ref[sl] = force
            newer = 2.0 * centre - old_ref[sl] + c_ref[sl] * force
            if track:
                hit = (where_ref[3] == 1) & (where_ref[0] == plane - HALO)
                mask = hit & (row == where_ref[1] - y0) & (lane == where_ref[2])
                newer = jnp.where(mask, newer + amount_ref[0], newer)
                keep_ref[pl.ds(pl.multiple_of((plane - HALO) * height + y0, 8), rows), :] = newer
            new_ref[sl] = newer

    if track:
        @pl.when(i == pl.num_programs(0) - 1)
        def _():
            if edges:
                for q in range(HALO):
                    bottom = keep_ref[q * height:(q + 1) * height, :]
                    top = keep_ref[(planes - HALO + q) * height:(planes - HALO + q + 1) * height, :]
                    edge_lo_ref[q] = jnp.where(odd, bottom, top)
                    edge_hi_ref[q] = jnp.where(odd, top, bottom)
            one_lane = lax.broadcasted_iota(jnp.int32, (1, depth), 1)

            def sample(r, carry):
                line = keep_ref[pl.ds(rec_ref[0, r], 1), :]
                sample_ref[pl.ds(r, 1), :] = jnp.where(one_lane == rec_ref[1, r], line, 0.0)
                return carry

            lax.fori_loop(0, sample_ref.shape[0], sample, 0, unroll=8)


def grad_kernel(lo_ref, mid_ref, hi_ref, g0_ref, g1_ref, g2_ref, pad_ref, *, block, rows):
    i = pl.program_id(0)

    @pl.when(i == 0)
    def _():
        fill_padded(pad_ref, lo_ref, mid_ref, hi_ref)

    height = mid_ref.shape[1]
    lane = lax.broadcasted_iota(jnp.int32, (rows, mid_ref.shape[2]), 1)
    for p in range(block):
        plane = i * block + p + HALO
        for y0 in range(0, height, rows):
            sl = (p, pl.ds(y0, rows), slice(None))
            _, _, grads = taps(pad_ref, plane, y0, rows, lane)
            g0_ref[sl] = grads[0]
            g1_ref[sl] = grads[1]
            g2_ref[sl] = grads[2]


def pick_block(planes):
    for b in (4, 2, 1):
        if planes % b == 0:
            return b


def specs(shape, block):
    planes, height, depth = shape
    full = lambda s: pl.BlockSpec(s, lambda i: (0, 0, 0))
    blk = pl.BlockSpec((block, height, depth), lambda i: (i, 0, 0))
    return full, blk


def apply_step(parity, lo, mid, hi, b, g, c, old, track=None, rows=40, want_force=True, edges=True):
    planes, height, depth = mid.shape
    block = pick_block(planes)
    full, blk = specs(mid.shape, block)
    out = jax.ShapeDtypeStruct(mid.shape, jnp.float32)
    own_grad = g is None
    in_specs = [pl.BlockSpec(memory_space=pltpu.SMEM), full(lo.shape), full(mid.shape), full(hi.shape)]
    args = [parity, lo, mid, hi]
    if own_grad:
        in_specs += [full(b[0].shape), full(b[1].shape), full(b[2].shape)]
        args += list(b)
    else:
        in_specs += [blk] * 4
        args += [b, g[0], g[1], g[2]]
    in_specs += [blk, blk]
    args += [c, old]
    out_specs = [blk] if want_force else []
    out_shape = [out] if want_force else []
    out_specs.append(blk)
    out_shape.append(out)
    if own_grad:
        out_specs += [blk] * 3
        out_shape += [out] * 3
    scratch = [pltpu.VMEM((planes + 2 * HALO, height + 2 * PADY, depth), jnp.float32)]
    if own_grad:
        scratch.append(pltpu.VMEM((planes + 2 * HALO, height + 2 * PADY, depth), jnp.float32))
    if track is not None:
        smem = pl.BlockSpec(memory_space=pltpu.SMEM)
        in_specs += [smem, smem, smem]
        args += list(track)
        count = track[2].shape[1]
        edge = jax.ShapeDtypeStruct((HALO, height, depth), jnp.float32)
        lines = jax.ShapeDtypeStruct((count, depth), jnp.float32)
        if edges:
            out_specs += [full(edge.shape), full(edge.shape)]
            out_shape += [edge, edge]
        out_specs.append(pl.BlockSpec((count, depth), lambda i: (0, 0)))
        out_shape.append(lines)
        scratch.append(pltpu.VMEM((planes * height, depth), jnp.float32))
    kernel = functools.partial(
        step_kernel, block=block, rows=rows, track=track is not None, own_grad=own_grad, want_force=want_force,
        edges=edges,
    )
    return pl.pallas_call(
        kernel,
        grid=(planes // block,),
        in_specs=in_specs,
        out_specs=out_specs,
        out_shape=out_shape,
        scratch_shapes=scratch,
        compiler_params=pltpu.CompilerParams(dimension_semantics=("arbitrary",)),
    )(*args)


def apply_grad(lo, mid, hi, rows=40):
    planes, height, depth = mid.shape
    block = pick_block(planes)
    full, blk = specs(mid.shape, block)
    out = jax.ShapeDtypeStruct(mid.shape, jnp.float32)
    return pl.pallas_call(
        functools.partial(grad_kernel, block=block, rows=rows),
        grid=(planes // block,),
        in_specs=[full(lo.shape), full(mid.shape), full(hi.shape)],
        out_specs=[blk, blk, blk],
        out_shape=[out, out, out],
        scratch_shapes=[pltpu.VMEM((planes + 2 * HALO, height + 2 * PADY, depth), jnp.float32)],
        compiler_params=pltpu.CompilerParams(dimension_semantics=("arbitrary",)),
    )(lo, mid, hi)


def split_permute(block, axis, pairs, pieces):
    size = block.shape[0] // pieces
    parts = [lax.ppermute(block[p * size:(p + 1) * size], axis, pairs) for p in range(pieces)]
    return parts[0] if pieces == 1 else jnp.concatenate(parts)


def reduce_members(part, axis):
    members = lax.axis_size(axis)
    if members & (members - 1) or part.size % (members * 2048):
        return lax.psum(part, axis) / members
    me = lax.axis_index(axis)
    rows = part.reshape(-1, 128)
    bits = members.bit_length() - 1
    for b in range(bits):
        mask = 1 << b
        half = rows.shape[0] // 2
        upper = (me // mask) % 2
        keep = lax.dynamic_slice_in_dim(rows, upper * half, half, 0)
        give = lax.dynamic_slice_in_dim(rows, (1 - upper) * half, half, 0)
        pairs = [(i, i ^ mask) for i in range(members)]
        rows = keep + split_permute(give, axis, pairs, 2 if b else 1)
    rows = rows / members
    for b in reversed(range(bits)):
        mask = 1 << b
        upper = (me // mask) % 2
        pairs = [(i, i ^ mask) for i in range(members)]
        other = split_permute(rows, axis, pairs, 2 if b else 1)
        rows = jnp.where(upper == 1, jnp.concatenate([other, rows]), jnp.concatenate([rows, other]))
    return rows.reshape(part.shape)


def swap_halos(sends, axis):
    count = lax.axis_size(axis)
    first = [(i, i ^ 1) for i in range(count) if i ^ 1 < count]
    second = [(i, i + 1) for i in range(1, count - 1, 2)] + [(i + 1, i) for i in range(1, count - 1, 2)]
    return lax.ppermute(sends[0], axis, first), lax.ppermute(sends[1], axis, second)


def halos(block, axis):
    planes = block.shape[0]
    odd = lax.axis_index(axis) % 2
    near = lax.dynamic_slice_in_dim(block, (1 - odd) * (planes - HALO), HALO, 0)
    far = lax.dynamic_slice_in_dim(block, odd * (planes - HALO), HALO, 0)
    return swap_halos((near, far), axis)


def inject(field, where, valid, values):
    flat = field.reshape(-1).at[where].add(jnp.where(valid, values, 0.0))
    return flat.reshape(field.shape)


def shards(
    courant,
    prev_field,
    cur_field,
    adj_prev,
    adj_cur,
    buoyancy,
    wavelet,
    src_cell,
    rec_cell,
    observed,
):
    speed = courant[0]
    planes, height, depth = buoyancy.shape
    volume = planes * height * depth
    offset = lax.axis_index("tile") * volume
    steps = wavelet.shape[0]

    def locate(cells):
        local = cells - offset
        valid = (local >= 0) & (local < volume)
        return (jnp.clip(local, 0, volume - 1), valid)

    src_local, src_valid = locate(src_cell)
    rec_local, rec_valid = locate(rec_cell)
    parity = (lax.axis_index("tile") % 2).astype(jnp.int32).reshape(1)
    b_lo, b_hi = halos(buoyancy, "tile")

    def spread(cells):
        return jnp.stack([cells // (height * depth), (cells // depth) % height, cells % depth])

    where = jnp.concatenate([spread(src_local)[:, 0], src_valid.astype(jnp.int32)])
    receivers = jnp.stack([rec_local // depth, rec_local % depth])
    older, now = (prev_field[0], cur_field[0])
    lo, hi = halos(now, "tile")
    forces = []
    samples = []
    grad_b = None
    for k in range(steps):
        track = (where, wavelet[k:k + 1], receivers)
        if grad_b is None:
            outs = apply_step(parity, lo, now, hi, (b_lo, buoyancy, b_hi), None, speed, older, track)
            force, newer = outs[:2]
            grad_b = outs[2:5]
            edge_lo, edge_hi, lines = outs[5:]
        else:
            outs = apply_step(parity, lo, now, hi, buoyancy, grad_b, speed, older, track, edges=k + 1 < steps)
            force, newer, lines = outs[0], outs[1], outs[-1]
            edge_lo, edge_hi = (outs[2], outs[3]) if k + 1 < steps else (None, None)
        if k + 1 < steps:
            lo, hi = swap_halos((edge_lo, edge_hi), "tile")
        samples.append(jnp.sum(lines, axis=1))
        forces.append(force)
        older, now = (now, newer)
    residual = jnp.where(rec_valid, jnp.stack(samples) - observed, 0.0)
    older, now = (adj_prev[0], adj_cur[0])
    image_part = jnp.zeros(buoyancy.shape, jnp.float32)
    for j in range(steps):
        lo, hi = halos(now, "tile")
        (newer,) = apply_step(parity, lo, now, hi, buoyancy, grad_b, speed, older, want_force=False)
        newer = inject(newer, rec_local, rec_valid, residual[steps - 1 - j])
        image_part = image_part + newer * forces[steps - 1 - j]
        older, now = (now, newer)
    image = reduce_members(image_part, "real")
    return (image, now[None])


def solution(mesh):
    in_specs = (
        P("real", "tile", None, None),
        P(("shot", "real"), "tile", None, None),
        P(("shot", "real"), "tile", None, None),
        P(("shot", "real"), "tile", None, None),
        P(("shot", "real"), "tile", None, None),
        P("tile", None, None),
        P("shot"),
        P("shot"),
        P("shot"),
        P("shot", None),
    )
    out_specs = (P(("shot", "tile"), None, None), P(("shot", "real"), "tile", None, None))
    return jax.shard_map(shards, mesh=mesh, in_specs=in_specs, out_specs=out_specs, check_vma=False)
```

```python
import functools
import jax
import jax.numpy as jnp
from jax import lax
from jax.experimental import pallas as pl
from jax.experimental.pallas import tpu as pltpu
from jax.sharding import PartitionSpec as P

SECOND = (-205.0 / 72.0, 8.0 / 5.0, -1.0 / 5.0, 8.0 / 315.0, -1.0 / 560.0)
FIRST = (4.0 / 5.0, -1.0 / 5.0, 4.0 / 105.0, -1.0 / 280.0)
HALO = 4
PADY = 8


def lane_shift(v, k, lane):
    width = v.shape[-1]
    if k > 0:
        rolled = pltpu.roll(v, width - k, 1)
        return jnp.where(lane < width - k, rolled, 0.0)
    rolled = pltpu.roll(v, -k, 1)
    return jnp.where(lane >= -k, rolled, 0.0)


def fill_padded(pad_ref, first_ref, mid_ref, second_ref, odd):
    planes, height, depth = mid_ref.shape
    pad_ref[...] = jnp.zeros(pad_ref.shape, jnp.float32)
    first = first_ref[...]
    second = second_ref[...]
    pad_ref[0:HALO, PADY:PADY + height, :] = jnp.where(odd, first, second)
    pad_ref[HALO:HALO + planes, PADY:PADY + height, :] = mid_ref[...]
    pad_ref[HALO + planes:, PADY:PADY + height, :] = jnp.where(odd, second, first)


def taps(pad_ref, plane, y0, rows, lane):
    def at(dx, dy):
        return pad_ref[plane + dx, pl.ds(PADY + y0 + dy, rows), :]
    centre = at(0, 0)
    lap = 3.0 * SECOND[0] * centre
    grads = []
    for axis in range(3):
        if axis == 0:
            get = lambda k: at(k, 0)
        elif axis == 1:
            get = lambda k: at(0, k)
        else:
            get = lambda k: lane_shift(centre, k, lane)
        vals = {k: get(k) for k in (1, 2, 3, 4, -1, -2, -3, -4)}
        for k in range(1, 5):
            lap = lap + SECOND[k] * (vals[k] + vals[-k])
        slope = FIRST[0] * (vals[1] - vals[-1])
        for k in range(2, 5):
            slope = slope + FIRST[k - 1] * (vals[k] - vals[-k])
        grads.append(slope)
    return centre, lap, grads


def step_kernel(*refs, block, rows, track, own_grad, want_force, edges):
    refs = list(refs)
    take = lambda n: [refs.pop(0) for _ in range(n)]
    (parity_ref,) = take(1)
    lo_ref, mid_ref, hi_ref = take(3)
    if own_grad:
        b_lo_ref, b_mid_ref, b_hi_ref = take(3)
    else:
        b_ref, g0_ref, g1_ref, g2_ref = take(4)
    c_ref, old_ref = take(2)
    if track:
        where_ref, amount_ref, rec_ref = take(3)
    force_ref = take(1)[0] if want_force else None
    (new_ref,) = take(1)
    if own_grad:
        g_out = take(3)
    if track and edges:
        edge_lo_ref, edge_hi_ref = take(2)
    if track:
        (sample_ref,) = take(1)
    (pad_ref,) = take(1)
    if own_grad:
        (b_pad_ref,) = take(1)
    if track:
        (keep_ref,) = take(1)
    i = pl.program_id(0)

    odd = parity_ref[0] == 1

    @pl.when(i == 0)
    def _():
        fill_padded(pad_ref, lo_ref, mid_ref, hi_ref, odd)
        if own_grad:
            fill_padded(b_pad_ref, b_lo_ref, b_mid_ref, b_hi_ref, odd)

    planes = mid_ref.shape[0]
    height = c_ref.shape[1]
    depth = c_ref.shape[2]
    lane = lax.broadcasted_iota(jnp.int32, (rows, depth), 1)
    row = lax.broadcasted_iota(jnp.int32, (rows, depth), 0)
    for p in range(block):
        plane = i * block + p + HALO
        for y0 in range(0, height, rows):
            sl = (p, pl.ds(y0, rows), slice(None))
            centre, lap, grads = taps(pad_ref, plane, y0, rows, lane)
            if own_grad:
                bvals, _, gb = taps(b_pad_ref, plane, y0, rows, lane)
                for out_ref, value in zip(g_out, gb):
                    out_ref[sl] = value
            else:
                bvals = b_ref[sl]
                gb = [g0_ref[sl], g1_ref[sl], g2_ref[sl]]
            force = bvals * lap + (gb[0] * grads[0] + gb[1] * grads[1] + gb[2] * grads[2])
            if want_force:
                force_ref[sl] = force
            newer = 2.0 * centre - old_ref[sl] + c_ref[sl] * force
            if track:
                hit = (where_ref[3] == 1) & (where_ref[0] == plane - HALO)
                mask = hit & (row == where_ref[1] - y0) & (lane == where_ref[2])
                newer = jnp.where(mask, newer + amount_ref[0], newer)
                keep_ref[pl.ds(pl.multiple_of((plane - HALO) * height + y0, 8), rows), :] = newer
            new_ref[sl] = newer

    if track:
        @pl.when(i == pl.num_programs(0) - 1)
        def _():
            if edges:
                for q in range(HALO):
                    bottom = keep_ref[q * height:(q + 1) * height, :]
                    top = keep_ref[(planes - HALO + q) * height:(planes - HALO + q + 1) * height, :]
                    edge_lo_ref[q] = jnp.where(odd, bottom, top)
                    edge_hi_ref[q] = jnp.where(odd, top, bottom)
            one_lane = lax.broadcasted_iota(jnp.int32, (1, depth), 1)

            def sample(r, carry):
                line = keep_ref[pl.ds(rec_ref[0, r], 1), :]
                sample_ref[pl.ds(r, 1), :] = jnp.where(one_lane == rec_ref[1, r], line, 0.0)
                return carry

            lax.fori_loop(0, sample_ref.shape[0], sample, 0, unroll=32)


def grad_kernel(lo_ref, mid_ref, hi_ref, g0_ref, g1_ref, g2_ref, pad_ref, *, block, rows):
    i = pl.program_id(0)

    @pl.when(i == 0)
    def _():
        fill_padded(pad_ref, lo_ref, mid_ref, hi_ref)

    height = mid_ref.shape[1]
    lane = lax.broadcasted_iota(jnp.int32, (rows, mid_ref.shape[2]), 1)
    for p in range(block):
        plane = i * block + p + HALO
        for y0 in range(0, height, rows):
            sl = (p, pl.ds(y0, rows), slice(None))
            _, _, grads = taps(pad_ref, plane, y0, rows, lane)
            g0_ref[sl] = grads[0]
            g1_ref[sl] = grads[1]
            g2_ref[sl] = grads[2]


def pick_block(planes):
    for b in (4, 2, 1):
        if planes % b == 0:
            return b


def specs(shape, block):
    planes, height, depth = shape
    full = lambda s: pl.BlockSpec(s, lambda i: (0, 0, 0))
    blk = pl.BlockSpec((block, height, depth), lambda i: (i, 0, 0))
    return full, blk


def apply_step(parity, lo, mid, hi, b, g, c, old, track=None, rows=40, want_force=True, edges=True):
    planes, height, depth = mid.shape
    block = pick_block(planes)
    full, blk = specs(mid.shape, block)
    out = jax.ShapeDtypeStruct(mid.shape, jnp.float32)
    own_grad = g is None
    in_specs = [pl.BlockSpec(memory_space=pltpu.SMEM), full(lo.shape), full(mid.shape), full(hi.shape)]
    args = [parity, lo, mid, hi]
    if own_grad:
        in_specs += [full(b[0].shape), full(b[1].shape), full(b[2].shape)]
        args += list(b)
    else:
        in_specs += [blk] * 4
        args += [b, g[0], g[1], g[2]]
    in_specs += [blk, blk]
    args += [c, old]
    out_specs = [blk] if want_force else []
    out_shape = [out] if want_force else []
    out_specs.append(blk)
    out_shape.append(out)
    if own_grad:
        out_specs += [blk] * 3
        out_shape += [out] * 3
    scratch = [pltpu.VMEM((planes + 2 * HALO, height + 2 * PADY, depth), jnp.float32)]
    if own_grad:
        scratch.append(pltpu.VMEM((planes + 2 * HALO, height + 2 * PADY, depth), jnp.float32))
    if track is not None:
        smem = pl.BlockSpec(memory_space=pltpu.SMEM)
        in_specs += [smem, smem, smem]
        args += list(track)
        count = track[2].shape[1]
        edge = jax.ShapeDtypeStruct((HALO, height, depth), jnp.float32)
        lines = jax.ShapeDtypeStruct((count, depth), jnp.float32)
        if edges:
            out_specs += [full(edge.shape), full(edge.shape)]
            out_shape += [edge, edge]
        out_specs.append(pl.BlockSpec((count, depth), lambda i: (0, 0)))
        out_shape.append(lines)
        scratch.append(pltpu.VMEM((planes * height, depth), jnp.float32))
    kernel = functools.partial(
        step_kernel, block=block, rows=rows, track=track is not None, own_grad=own_grad, want_force=want_force,
        edges=edges,
    )
    return pl.pallas_call(
        kernel,
        grid=(planes // block,),
        in_specs=in_specs,
        out_specs=out_specs,
        out_shape=out_shape,
        scratch_shapes=scratch,
        compiler_params=pltpu.CompilerParams(dimension_semantics=("arbitrary",)),
    )(*args)


def apply_grad(lo, mid, hi, rows=40):
    planes, height, depth = mid.shape
    block = pick_block(planes)
    full, blk = specs(mid.shape, block)
    out = jax.ShapeDtypeStruct(mid.shape, jnp.float32)
    return pl.pallas_call(
        functools.partial(grad_kernel, block=block, rows=rows),
        grid=(planes // block,),
        in_specs=[full(lo.shape), full(mid.shape), full(hi.shape)],
        out_specs=[blk, blk, blk],
        out_shape=[out, out, out],
        scratch_shapes=[pltpu.VMEM((planes + 2 * HALO, height + 2 * PADY, depth), jnp.float32)],
        compiler_params=pltpu.CompilerParams(dimension_semantics=("arbitrary",)),
    )(lo, mid, hi)


def reduce_members(part, axis):
    members = lax.axis_size(axis)
    if members & (members - 1) or part.size % (members * 1024):
        return lax.psum(part, axis) / members
    me = lax.axis_index(axis)
    rows = part.reshape(-1, 128)
    bits = members.bit_length() - 1
    for b in range(bits):
        mask = 1 << b
        half = rows.shape[0] // 2
        upper = (me // mask) % 2
        keep = lax.dynamic_slice_in_dim(rows, upper * half, half, 0)
        give = lax.dynamic_slice_in_dim(rows, (1 - upper) * half, half, 0)
        pairs = [(i, i ^ mask) for i in range(members)]
        rows = keep + lax.ppermute(give, axis, pairs)
    rows = rows / members
    for b in reversed(range(bits)):
        mask = 1 << b
        upper = (me // mask) % 2
        pairs = [(i, i ^ mask) for i in range(members)]
        other = lax.ppermute(rows, axis, pairs)
        rows = jnp.where(upper == 1, jnp.concatenate([other, rows]), jnp.concatenate([rows, other]))
    return rows.reshape(part.shape)


def swap_halos(sends, axis):
    count = lax.axis_size(axis)
    first = [(i, i ^ 1) for i in range(count) if i ^ 1 < count]
    second = [(i, i + 1) for i in range(1, count - 1, 2)] + [(i + 1, i) for i in range(1, count - 1, 2)]
    return lax.ppermute(sends[0], axis, first), lax.ppermute(sends[1], axis, second)


def halos(block, axis):
    planes = block.shape[0]
    odd = lax.axis_index(axis) % 2
    near = lax.dynamic_slice_in_dim(block, (1 - odd) * (planes - HALO), HALO, 0)
    far = lax.dynamic_slice_in_dim(block, odd * (planes - HALO), HALO, 0)
    return swap_halos((near, far), axis)


def inject(field, where, valid, values):
    flat = field.reshape(-1).at[where].add(jnp.where(valid, values, 0.0))
    return flat.reshape(field.shape)


def shards(
    courant,
    prev_field,
    cur_field,
    adj_prev,
    adj_cur,
    buoyancy,
    wavelet,
    src_cell,
    rec_cell,
    observed,
):
    speed = courant[0]
    planes, height, depth = buoyancy.shape
    volume = planes * height * depth
    offset = lax.axis_index("tile") * volume
    steps = wavelet.shape[0]

    def locate(cells):
        local = cells - offset
        valid = (local >= 0) & (local < volume)
        return (jnp.clip(local, 0, volume - 1), valid)

    src_local, src_valid = locate(src_cell)
    rec_local, rec_valid = locate(rec_cell)
    parity = (lax.axis_index("tile") % 2).astype(jnp.int32).reshape(1)
    b_lo, b_hi = halos(buoyancy, "tile")

    def spread(cells):
        return jnp.stack([cells // (height * depth), (cells // depth) % height, cells % depth])

    where = jnp.concatenate([spread(src_local)[:, 0], src_valid.astype(jnp.int32)])
    receivers = jnp.stack([rec_local // depth, rec_local % depth])
    older, now = (prev_field[0], cur_field[0])
    lo, hi = halos(now, "tile")
    forces = []
    samples = []
    grad_b = None
    for k in range(steps):
        track = (where, wavelet[k:k + 1], receivers)
        if grad_b is None:
            outs = apply_step(parity, lo, now, hi, (b_lo, buoyancy, b_hi), None, speed, older, track)
            force, newer = outs[:2]
            grad_b = outs[2:5]
            edge_lo, edge_hi, lines = outs[5:]
        else:
            outs = apply_step(parity, lo, now, hi, buoyancy, grad_b, speed, older, track, edges=k + 1 < steps)
            force, newer, lines = outs[0], outs[1], outs[-1]
            edge_lo, edge_hi = (outs[2], outs[3]) if k + 1 < steps else (None, None)
        if k + 1 < steps:
            lo, hi = swap_halos((edge_lo, edge_hi), "tile")
        samples.append(jnp.sum(lines, axis=1))
        forces.append(force)
        older, now = (now, newer)
    residual = jnp.where(rec_valid, jnp.stack(samples) - observed, 0.0)
    older, now = (adj_prev[0], adj_cur[0])
    image_part = jnp.zeros(buoyancy.shape, jnp.float32)
    for j in range(steps):
        lo, hi = halos(now, "tile")
        (newer,) = apply_step(parity, lo, now, hi, buoyancy, grad_b, speed, older, want_force=False)
        newer = inject(newer, rec_local, rec_valid, residual[steps - 1 - j])
        image_part = image_part + newer * forces[steps - 1 - j]
        older, now = (now, newer)
    image = reduce_members(image_part, "real")
    return (image, now[None])


def solution(mesh):
    in_specs = (
        P("real", "tile", None, None),
        P(("shot", "real"), "tile", None, None),
        P(("shot", "real"), "tile", None, None),
        P(("shot", "real"), "tile", None, None),
        P(("shot", "real"), "tile", None, None),
        P("tile", None, None),
        P("shot"),
        P("shot"),
        P("shot"),
        P("shot", None),
    )
    out_specs = (P(("shot", "tile"), None, None), P(("shot", "real"), "tile", None, None))
    return jax.shard_map(shards, mesh=mesh, in_specs=in_specs, out_specs=out_specs, check_vma=False)
```

```python
import functools
import jax
import jax.numpy as jnp
from jax import lax
from jax.experimental import pallas as pl
from jax.experimental.pallas import tpu as pltpu
from jax.sharding import PartitionSpec as P

SECOND = (-205.0 / 72.0, 8.0 / 5.0, -1.0 / 5.0, 8.0 / 315.0, -1.0 / 560.0)
FIRST = (4.0 / 5.0, -1.0 / 5.0, 4.0 / 105.0, -1.0 / 280.0)
HALO = 4
PADY = 8


def lane_shift(v, k, lane):
    width = v.shape[-1]
    if k > 0:
        rolled = pltpu.roll(v, width - k, 1)
        return jnp.where(lane < width - k, rolled, 0.0)
    rolled = pltpu.roll(v, -k, 1)
    return jnp.where(lane >= -k, rolled, 0.0)


def fill_padded(pad_ref, first_ref, mid_ref, second_ref, odd):
    planes, height, depth = mid_ref.shape
    pad_ref[...] = jnp.zeros(pad_ref.shape, jnp.float32)
    first = first_ref[...]
    second = second_ref[...]
    pad_ref[0:HALO, PADY:PADY + height, :] = jnp.where(odd, first, second)
    pad_ref[HALO:HALO + planes, PADY:PADY + height, :] = mid_ref[...]
    pad_ref[HALO + planes:, PADY:PADY + height, :] = jnp.where(odd, second, first)


def taps(pad_ref, plane, y0, rows, lane):
    def at(dx, dy):
        return pad_ref[plane + dx, pl.ds(PADY + y0 + dy, rows), :]
    centre = at(0, 0)
    lap = 3.0 * SECOND[0] * centre
    grads = []
    for axis in range(3):
        if axis == 0:
            get = lambda k: at(k, 0)
        elif axis == 1:
            get = lambda k: at(0, k)
        else:
            get = lambda k: lane_shift(centre, k, lane)
        vals = {k: get(k) for k in (1, 2, 3, 4, -1, -2, -3, -4)}
        for k in range(1, 5):
            lap = lap + SECOND[k] * (vals[k] + vals[-k])
        slope = FIRST[0] * (vals[1] - vals[-1])
        for k in range(2, 5):
            slope = slope + FIRST[k - 1] * (vals[k] - vals[-k])
        grads.append(slope)
    return centre, lap, grads


def step_kernel(*refs, block, rows, track, own_grad, want_force, edges):
    refs = list(refs)
    take = lambda n: [refs.pop(0) for _ in range(n)]
    (parity_ref,) = take(1)
    lo_ref, mid_ref, hi_ref = take(3)
    if own_grad:
        b_lo_ref, b_mid_ref, b_hi_ref = take(3)
    else:
        b_ref, g0_ref, g1_ref, g2_ref = take(4)
    c_ref, old_ref = take(2)
    if track:
        where_ref, amount_ref, rec_ref = take(3)
    force_ref = take(1)[0] if want_force else None
    (new_ref,) = take(1)
    if own_grad:
        g_out = take(3)
    if track and edges:
        edge_lo_ref, edge_hi_ref = take(2)
    if track:
        (sample_ref,) = take(1)
    (pad_ref,) = take(1)
    if own_grad:
        (b_pad_ref,) = take(1)
    if track:
        (keep_ref,) = take(1)
    i = pl.program_id(0)

    odd = parity_ref[0] == 1

    @pl.when(i == 0)
    def _():
        fill_padded(pad_ref, lo_ref, mid_ref, hi_ref, odd)
        if own_grad:
            fill_padded(b_pad_ref, b_lo_ref, b_mid_ref, b_hi_ref, odd)

    planes = mid_ref.shape[0]
    height = c_ref.shape[1]
    depth = c_ref.shape[2]
    lane = lax.broadcasted_iota(jnp.int32, (rows, depth), 1)
    row = lax.broadcasted_iota(jnp.int32, (rows, depth), 0)
    for p in range(block):
        plane = i * block + p + HALO
        for y0 in range(0, height, rows):
            sl = (p, pl.ds(y0, rows), slice(None))
            centre, lap, grads = taps(pad_ref, plane, y0, rows, lane)
            if own_grad:
                bvals, _, gb = taps(b_pad_ref, plane, y0, rows, lane)
                for out_ref, value in zip(g_out, gb):
                    out_ref[sl] = value
            else:
                bvals = b_ref[sl]
                gb = [g0_ref[sl], g1_ref[sl], g2_ref[sl]]
            force = bvals * lap + (gb[0] * grads[0] + gb[1] * grads[1] + gb[2] * grads[2])
            if want_force:
                force_ref[sl] = force
            newer = 2.0 * centre - old_ref[sl] + c_ref[sl] * force
            if track:
                hit = (where_ref[3] == 1) & (where_ref[0] == plane - HALO)
                mask = hit & (row == where_ref[1] - y0) & (lane == where_ref[2])
                newer = jnp.where(mask, newer + amount_ref[0], newer)
                keep_ref[pl.ds(pl.multiple_of((plane - HALO) * height + y0, 8), rows), :] = newer
            new_ref[sl] = newer

    if track:
        @pl.when(i == pl.num_programs(0) - 1)
        def _():
            if edges:
                for q in range(HALO):
                    bottom = keep_ref[q * height:(q + 1) * height, :]
                    top = keep_ref[(planes - HALO + q) * height:(planes - HALO + q + 1) * height, :]
                    edge_lo_ref[q] = jnp.where(odd, bottom, top)
                    edge_hi_ref[q] = jnp.where(odd, top, bottom)
            one_lane = lax.broadcasted_iota(jnp.int32, (1, depth), 1)

            def sample(r, carry):
                line = keep_ref[pl.ds(rec_ref[0, r], 1), :]
                sample_ref[pl.ds(r, 1), :] = jnp.where(one_lane == rec_ref[1, r], line, 0.0)
                return carry

            lax.fori_loop(0, sample_ref.shape[0], sample, 0, unroll=8)


def grad_kernel(lo_ref, mid_ref, hi_ref, g0_ref, g1_ref, g2_ref, pad_ref, *, block, rows):
    i = pl.program_id(0)

    @pl.when(i == 0)
    def _():
        fill_padded(pad_ref, lo_ref, mid_ref, hi_ref)

    height = mid_ref.shape[1]
    lane = lax.broadcasted_iota(jnp.int32, (rows, mid_ref.shape[2]), 1)
    for p in range(block):
        plane = i * block + p + HALO
        for y0 in range(0, height, rows):
            sl = (p, pl.ds(y0, rows), slice(None))
            _, _, grads = taps(pad_ref, plane, y0, rows, lane)
            g0_ref[sl] = grads[0]
            g1_ref[sl] = grads[1]
            g2_ref[sl] = grads[2]


def final_kernel(parity_ref, lo_ref, mid_ref, hi_ref, b_ref, g0_ref, g1_ref, g2_ref, c_ref, old_ref,
                 rec_ref, valid_ref, amount_ref, new_ref, pad_ref, *, block, rows):
    i = pl.program_id(0)
    odd = parity_ref[0] == 1

    @pl.when(i == 0)
    def _():
        fill_padded(pad_ref, lo_ref, mid_ref, hi_ref, odd)

    planes, height, depth = mid_ref.shape
    lane = lax.broadcasted_iota(jnp.int32, (rows, depth), 1)
    for p in range(block):
        plane = i * block + p + HALO
        for y0 in range(0, height, rows):
            sl = (p, pl.ds(y0, rows), slice(None))
            centre, lap, grads = taps(pad_ref, plane, y0, rows, lane)
            force = b_ref[sl] * lap + (g0_ref[sl] * grads[0] + g1_ref[sl] * grads[1] + g2_ref[sl] * grads[2])
            new_ref[plane - HALO, pl.ds(y0, rows), :] = 2.0 * centre - old_ref[sl] + c_ref[sl] * force

    @pl.when(i == pl.num_programs(0) - 1)
    def _():
        one_lane = lax.broadcasted_iota(jnp.int32, (1, depth), 1)

        def add(r, carry):
            x = rec_ref[0, r]
            y = rec_ref[1, r]
            hit = (one_lane == rec_ref[2, r]) & (valid_ref[r] == 1)
            line = new_ref[x, pl.ds(y, 1), :]
            new_ref[x, pl.ds(y, 1), :] = jnp.where(hit, line + amount_ref[r], line)
            return carry

        lax.fori_loop(0, amount_ref.shape[0], add, 0)


def apply_final(parity, lo, mid, hi, b, g, c, old, receivers, valid, amount, rows=40):
    planes, height, depth = mid.shape
    block = pick_block(planes)
    full, blk = specs(mid.shape, block)
    out = jax.ShapeDtypeStruct(mid.shape, jnp.float32)
    smem = pl.BlockSpec(memory_space=pltpu.SMEM)
    return pl.pallas_call(
        functools.partial(final_kernel, block=block, rows=rows),
        grid=(planes // block,),
        in_specs=[smem, full(lo.shape), full(mid.shape), full(hi.shape)] + [blk] * 6
        + [smem, smem, smem],
        out_specs=full(mid.shape),
        out_shape=out,
        scratch_shapes=[pltpu.VMEM((planes + 2 * HALO, height + 2 * PADY, depth), jnp.float32)],
        compiler_params=pltpu.CompilerParams(dimension_semantics=("arbitrary",)),
    )(parity, lo, mid, hi, b, g[0], g[1], g[2], c, old, receivers, valid, amount)


def pick_block(planes):
    for b in (4, 2, 1):
        if planes % b == 0:
            return b


def specs(shape, block):
    planes, height, depth = shape
    full = lambda s: pl.BlockSpec(s, lambda i: (0, 0, 0))
    blk = pl.BlockSpec((block, height, depth), lambda i: (i, 0, 0))
    return full, blk


def apply_step(parity, lo, mid, hi, b, g, c, old, track=None, rows=40, want_force=True, edges=True):
    planes, height, depth = mid.shape
    block = pick_block(planes)
    full, blk = specs(mid.shape, block)
    out = jax.ShapeDtypeStruct(mid.shape, jnp.float32)
    own_grad = g is None
    in_specs = [pl.BlockSpec(memory_space=pltpu.SMEM), full(lo.shape), full(mid.shape), full(hi.shape)]
    args = [parity, lo, mid, hi]
    if own_grad:
        in_specs += [full(b[0].shape), full(b[1].shape), full(b[2].shape)]
        args += list(b)
    else:
        in_specs += [blk] * 4
        args += [b, g[0], g[1], g[2]]
    in_specs += [blk, blk]
    args += [c, old]
    out_specs = [blk] if want_force else []
    out_shape = [out] if want_force else []
    out_specs.append(blk)
    out_shape.append(out)
    if own_grad:
        out_specs += [blk] * 3
        out_shape += [out] * 3
    scratch = [pltpu.VMEM((planes + 2 * HALO, height + 2 * PADY, depth), jnp.float32)]
    if own_grad:
        scratch.append(pltpu.VMEM((planes + 2 * HALO, height + 2 * PADY, depth), jnp.float32))
    if track is not None:
        smem = pl.BlockSpec(memory_space=pltpu.SMEM)
        in_specs += [smem, smem, smem]
        args += list(track)
        count = track[2].shape[1]
        edge = jax.ShapeDtypeStruct((HALO, height, depth), jnp.float32)
        lines = jax.ShapeDtypeStruct((count, depth), jnp.float32)
        if edges:
            out_specs += [full(edge.shape), full(edge.shape)]
            out_shape += [edge, edge]
        out_specs.append(pl.BlockSpec((count, depth), lambda i: (0, 0)))
        out_shape.append(lines)
        scratch.append(pltpu.VMEM((planes * height, depth), jnp.float32))
    kernel = functools.partial(
        step_kernel, block=block, rows=rows, track=track is not None, own_grad=own_grad, want_force=want_force,
        edges=edges,
    )
    return pl.pallas_call(
        kernel,
        grid=(planes // block,),
        in_specs=in_specs,
        out_specs=out_specs,
        out_shape=out_shape,
        scratch_shapes=scratch,
        compiler_params=pltpu.CompilerParams(dimension_semantics=("arbitrary",)),
    )(*args)


def apply_grad(lo, mid, hi, rows=40):
    planes, height, depth = mid.shape
    block = pick_block(planes)
    full, blk = specs(mid.shape, block)
    out = jax.ShapeDtypeStruct(mid.shape, jnp.float32)
    return pl.pallas_call(
        functools.partial(grad_kernel, block=block, rows=rows),
        grid=(planes // block,),
        in_specs=[full(lo.shape), full(mid.shape), full(hi.shape)],
        out_specs=[blk, blk, blk],
        out_shape=[out, out, out],
        scratch_shapes=[pltpu.VMEM((planes + 2 * HALO, height + 2 * PADY, depth), jnp.float32)],
        compiler_params=pltpu.CompilerParams(dimension_semantics=("arbitrary",)),
    )(lo, mid, hi)


def reduce_members(part, axis):
    members = lax.axis_size(axis)
    if members & (members - 1) or part.size % (members * 1024):
        return lax.psum(part, axis) / members
    me = lax.axis_index(axis)
    rows = part.reshape(-1, 128)
    bits = members.bit_length() - 1
    for b in range(bits):
        mask = 1 << b
        half = rows.shape[0] // 2
        upper = (me // mask) % 2
        keep = lax.dynamic_slice_in_dim(rows, upper * half, half, 0)
        give = lax.dynamic_slice_in_dim(rows, (1 - upper) * half, half, 0)
        pairs = [(i, i ^ mask) for i in range(members)]
        rows = keep + lax.ppermute(give, axis, pairs)
    rows = rows / members
    for b in reversed(range(bits)):
        mask = 1 << b
        upper = (me // mask) % 2
        pairs = [(i, i ^ mask) for i in range(members)]
        other = lax.ppermute(rows, axis, pairs)
        rows = jnp.where(upper == 1, jnp.concatenate([other, rows]), jnp.concatenate([rows, other]))
    return rows.reshape(part.shape)


def swap_halos(sends, axis):
    count = lax.axis_size(axis)
    first = [(i, i ^ 1) for i in range(count) if i ^ 1 < count]
    second = [(i, i + 1) for i in range(1, count - 1, 2)] + [(i + 1, i) for i in range(1, count - 1, 2)]
    return lax.ppermute(sends[0], axis, first), lax.ppermute(sends[1], axis, second)


def halos(block, axis):
    planes = block.shape[0]
    odd = lax.axis_index(axis) % 2
    near = lax.dynamic_slice_in_dim(block, (1 - odd) * (planes - HALO), HALO, 0)
    far = lax.dynamic_slice_in_dim(block, odd * (planes - HALO), HALO, 0)
    return swap_halos((near, far), axis)


def inject(field, where, valid, values):
    flat = field.reshape(-1).at[where].add(jnp.where(valid, values, 0.0))
    return flat.reshape(field.shape)


def shards(
    courant,
    prev_field,
    cur_field,
    adj_prev,
    adj_cur,
    buoyancy,
    wavelet,
    src_cell,
    rec_cell,
    observed,
):
    speed = courant[0]
    planes, height, depth = buoyancy.shape
    volume = planes * height * depth
    offset = lax.axis_index("tile") * volume
    steps = wavelet.shape[0]

    def locate(cells):
        local = cells - offset
        valid = (local >= 0) & (local < volume)
        return (jnp.clip(local, 0, volume - 1), valid)

    src_local, src_valid = locate(src_cell)
    rec_local, rec_valid = locate(rec_cell)
    parity = (lax.axis_index("tile") % 2).astype(jnp.int32).reshape(1)
    b_lo, b_hi = halos(buoyancy, "tile")

    def spread(cells):
        return jnp.stack([cells // (height * depth), (cells // depth) % height, cells % depth])

    where = jnp.concatenate([spread(src_local)[:, 0], src_valid.astype(jnp.int32)])
    receivers = jnp.stack([rec_local // depth, rec_local % depth])
    older, now = (prev_field[0], cur_field[0])
    lo, hi = halos(now, "tile")
    forces = []
    samples = []
    grad_b = None
    for k in range(steps):
        track = (where, wavelet[k:k + 1], receivers)
        if grad_b is None:
            outs = apply_step(parity, lo, now, hi, (b_lo, buoyancy, b_hi), None, speed, older, track)
            force, newer = outs[:2]
            grad_b = outs[2:5]
            edge_lo, edge_hi, lines = outs[5:]
        else:
            outs = apply_step(parity, lo, now, hi, buoyancy, grad_b, speed, older, track, edges=k + 1 < steps)
            force, newer, lines = outs[0], outs[1], outs[-1]
            edge_lo, edge_hi = (outs[2], outs[3]) if k + 1 < steps else (None, None)
        if k + 1 < steps:
            lo, hi = swap_halos((edge_lo, edge_hi), "tile")
        samples.append(jnp.sum(lines, axis=1))
        forces.append(force)
        older, now = (now, newer)
    residual = jnp.where(rec_valid, jnp.stack(samples) - observed, 0.0)
    older, now = (adj_prev[0], adj_cur[0])
    image_part = jnp.zeros(buoyancy.shape, jnp.float32)
    for j in range(steps):
        lo, hi = halos(now, "tile")
        if j + 1 < steps:
            (newer,) = apply_step(parity, lo, now, hi, buoyancy, grad_b, speed, older, want_force=False)
            newer = inject(newer, rec_local, rec_valid, residual[steps - 1 - j])
        else:
            cells = jnp.stack([rec_local // (height * depth), (rec_local // depth) % height, rec_local % depth])
            valid = rec_valid.astype(jnp.int32)
            newer = apply_final(parity, lo, now, hi, buoyancy, grad_b, speed, older, cells, valid, residual[0])
        image_part = image_part + newer * forces[steps - 1 - j]
        older, now = (now, newer)
    image = reduce_members(image_part, "real")
    return (image, now[None])


def solution(mesh):
    in_specs = (
        P("real", "tile", None, None),
        P(("shot", "real"), "tile", None, None),
        P(("shot", "real"), "tile", None, None),
        P(("shot", "real"), "tile", None, None),
        P(("shot", "real"), "tile", None, None),
        P("tile", None, None),
        P("shot"),
        P("shot"),
        P("shot"),
        P("shot", None),
    )
    out_specs = (P(("shot", "tile"), None, None), P(("shot", "real"), "tile", None, None))
    return jax.shard_map(shards, mesh=mesh, in_specs=in_specs, out_specs=out_specs, check_vma=False)
```

```python
import functools
import jax
import jax.numpy as jnp
from jax import lax
from jax.experimental import pallas as pl
from jax.experimental.pallas import tpu as pltpu
from jax.sharding import PartitionSpec as P

SECOND = (-205.0 / 72.0, 8.0 / 5.0, -1.0 / 5.0, 8.0 / 315.0, -1.0 / 560.0)
FIRST = (4.0 / 5.0, -1.0 / 5.0, 4.0 / 105.0, -1.0 / 280.0)
HALO = 4
PADY = 8


def lane_shift(v, k, lane):
    width = v.shape[-1]
    if k > 0:
        rolled = pltpu.roll(v, width - k, 1)
        return jnp.where(lane < width - k, rolled, 0.0)
    rolled = pltpu.roll(v, -k, 1)
    return jnp.where(lane >= -k, rolled, 0.0)


def fill_padded(pad_ref, first_ref, mid_ref, second_ref, odd):
    planes, height, depth = mid_ref.shape
    pad_ref[...] = jnp.zeros(pad_ref.shape, jnp.float32)
    first = first_ref[...]
    second = second_ref[...]
    pad_ref[0:HALO, PADY:PADY + height, :] = jnp.where(odd, first, second)
    pad_ref[HALO:HALO + planes, PADY:PADY + height, :] = mid_ref[...]
    pad_ref[HALO + planes:, PADY:PADY + height, :] = jnp.where(odd, second, first)


def taps(pad_ref, plane, y0, rows, lane):
    def at(dx, dy):
        return pad_ref[plane + dx, pl.ds(PADY + y0 + dy, rows), :]
    centre = at(0, 0)
    lap = 3.0 * SECOND[0] * centre
    grads = []
    for axis in range(3):
        if axis == 0:
            get = lambda k: at(k, 0)
        elif axis == 1:
            get = lambda k: at(0, k)
        else:
            get = lambda k: lane_shift(centre, k, lane)
        vals = {k: get(k) for k in (1, 2, 3, 4, -1, -2, -3, -4)}
        for k in range(1, 5):
            lap = lap + SECOND[k] * (vals[k] + vals[-k])
        slope = FIRST[0] * (vals[1] - vals[-1])
        for k in range(2, 5):
            slope = slope + FIRST[k - 1] * (vals[k] - vals[-k])
        grads.append(slope)
    return centre, lap, grads


def step_kernel(*refs, block, rows, track, own_grad, want_force, edges):
    refs = list(refs)
    take = lambda n: [refs.pop(0) for _ in range(n)]
    (parity_ref,) = take(1)
    lo_ref, mid_ref, hi_ref = take(3)
    if own_grad:
        b_lo_ref, b_mid_ref, b_hi_ref = take(3)
    else:
        b_ref, g0_ref, g1_ref, g2_ref = take(4)
    c_ref, old_ref = take(2)
    if track:
        where_ref, amount_ref, rec_ref = take(3)
    force_ref = take(1)[0] if want_force else None
    (new_ref,) = take(1)
    if own_grad:
        g_out = take(3)
    if track and edges:
        edge_lo_ref, edge_hi_ref = take(2)
    if track:
        (sample_ref,) = take(1)
    (pad_ref,) = take(1)
    if own_grad:
        (b_pad_ref,) = take(1)
    if track:
        (keep_ref,) = take(1)
    i = pl.program_id(0)

    odd = parity_ref[0] == 1

    @pl.when(i == 0)
    def _():
        fill_padded(pad_ref, lo_ref, mid_ref, hi_ref, odd)
        if own_grad:
            fill_padded(b_pad_ref, b_lo_ref, b_mid_ref, b_hi_ref, odd)

    planes = mid_ref.shape[0]
    height = c_ref.shape[1]
    depth = c_ref.shape[2]
    lane = lax.broadcasted_iota(jnp.int32, (rows, depth), 1)
    row = lax.broadcasted_iota(jnp.int32, (rows, depth), 0)
    for p in range(block):
        plane = i * block + p + HALO
        for y0 in range(0, height, rows):
            sl = (p, pl.ds(y0, rows), slice(None))
            centre, lap, grads = taps(pad_ref, plane, y0, rows, lane)
            if own_grad:
                bvals, _, gb = taps(b_pad_ref, plane, y0, rows, lane)
                for out_ref, value in zip(g_out, gb):
                    out_ref[sl] = value
            else:
                bvals = b_ref[sl]
                gb = [g0_ref[sl], g1_ref[sl], g2_ref[sl]]
            force = bvals * lap + (gb[0] * grads[0] + gb[1] * grads[1] + gb[2] * grads[2])
            if want_force:
                force_ref[sl] = force
            newer = 2.0 * centre - old_ref[sl] + c_ref[sl] * force
            if track:
                hit = (where_ref[3] == 1) & (where_ref[0] == plane - HALO)
                mask = hit & (row == where_ref[1] - y0) & (lane == where_ref[2])
                newer = jnp.where(mask, newer + amount_ref[0], newer)
                keep_ref[pl.ds(pl.multiple_of((plane - HALO) * height + y0, 8), rows), :] = newer
            new_ref[sl] = newer

    if track:
        @pl.when(i == pl.num_programs(0) - 1)
        def _():
            if edges:
                for q in range(HALO):
                    bottom = keep_ref[q * height:(q + 1) * height, :]
                    top = keep_ref[(planes - HALO + q) * height:(planes - HALO + q + 1) * height, :]
                    edge_lo_ref[q] = jnp.where(odd, bottom, top)
                    edge_hi_ref[q] = jnp.where(odd, top, bottom)
            one_lane = lax.broadcasted_iota(jnp.int32, (1, depth), 1)

            def sample(r, carry):
                line = keep_ref[pl.ds(rec_ref[0, r], 1), :]
                sample_ref[pl.ds(r, 1), :] = jnp.where(one_lane == rec_ref[1, r], line, 0.0)
                return carry

            lax.fori_loop(0, sample_ref.shape[0], sample, 0, unroll=8)


def grad_kernel(lo_ref, mid_ref, hi_ref, g0_ref, g1_ref, g2_ref, pad_ref, *, block, rows):
    i = pl.program_id(0)

    @pl.when(i == 0)
    def _():
        fill_padded(pad_ref, lo_ref, mid_ref, hi_ref)

    height = mid_ref.shape[1]
    lane = lax.broadcasted_iota(jnp.int32, (rows, mid_ref.shape[2]), 1)
    for p in range(block):
        plane = i * block + p + HALO
        for y0 in range(0, height, rows):
            sl = (p, pl.ds(y0, rows), slice(None))
            _, _, grads = taps(pad_ref, plane, y0, rows, lane)
            g0_ref[sl] = grads[0]
            g1_ref[sl] = grads[1]
            g2_ref[sl] = grads[2]


def final_kernel(parity_ref, lo_ref, mid_ref, hi_ref, b_ref, g0_ref, g1_ref, g2_ref, c_ref, old_ref,
                 rec_ref, valid_ref, amount_ref, new_ref, pad_ref, *, block, rows):
    i = pl.program_id(0)
    odd = parity_ref[0] == 1

    @pl.when(i == 0)
    def _():
        fill_padded(pad_ref, lo_ref, mid_ref, hi_ref, odd)

    planes, height, depth = mid_ref.shape
    lane = lax.broadcasted_iota(jnp.int32, (rows, depth), 1)
    for p in range(block):
        plane = i * block + p + HALO
        for y0 in range(0, height, rows):
            sl = (p, pl.ds(y0, rows), slice(None))
            centre, lap, grads = taps(pad_ref, plane, y0, rows, lane)
            force = b_ref[sl] * lap + (g0_ref[sl] * grads[0] + g1_ref[sl] * grads[1] + g2_ref[sl] * grads[2])
            new_ref[plane - HALO, pl.ds(y0, rows), :] = 2.0 * centre - old_ref[sl] + c_ref[sl] * force

    @pl.when(i == pl.num_programs(0) - 1)
    def _():
        one_lane = lax.broadcasted_iota(jnp.int32, (1, depth), 1)

        def add(r, carry):
            x = rec_ref[0, r]
            y = rec_ref[1, r]
            hit = (one_lane == rec_ref[2, r]) & (valid_ref[r] == 1)
            line = new_ref[x, pl.ds(y, 1), :]
            new_ref[x, pl.ds(y, 1), :] = jnp.where(hit, line + amount_ref[r], line)
            return carry

        lax.fori_loop(0, amount_ref.shape[0], add, 0, unroll=8)


def apply_final(parity, lo, mid, hi, b, g, c, old, receivers, valid, amount, rows=40):
    planes, height, depth = mid.shape
    block = pick_block(planes)
    full, blk = specs(mid.shape, block)
    out = jax.ShapeDtypeStruct(mid.shape, jnp.float32)
    smem = pl.BlockSpec(memory_space=pltpu.SMEM)
    return pl.pallas_call(
        functools.partial(final_kernel, block=block, rows=rows),
        grid=(planes // block,),
        in_specs=[smem, full(lo.shape), full(mid.shape), full(hi.shape)] + [blk] * 6
        + [smem, smem, smem],
        out_specs=full(mid.shape),
        out_shape=out,
        scratch_shapes=[pltpu.VMEM((planes + 2 * HALO, height + 2 * PADY, depth), jnp.float32)],
        compiler_params=pltpu.CompilerParams(dimension_semantics=("arbitrary",)),
    )(parity, lo, mid, hi, b, g[0], g[1], g[2], c, old, receivers, valid, amount)


def pick_block(planes):
    for b in (4, 2, 1):
        if planes % b == 0:
            return b


def specs(shape, block):
    planes, height, depth = shape
    full = lambda s: pl.BlockSpec(s, lambda i: (0, 0, 0))
    blk = pl.BlockSpec((block, height, depth), lambda i: (i, 0, 0))
    return full, blk


def apply_step(parity, lo, mid, hi, b, g, c, old, track=None, rows=40, want_force=True, edges=True):
    planes, height, depth = mid.shape
    block = pick_block(planes)
    full, blk = specs(mid.shape, block)
    out = jax.ShapeDtypeStruct(mid.shape, jnp.float32)
    own_grad = g is None
    in_specs = [pl.BlockSpec(memory_space=pltpu.SMEM), full(lo.shape), full(mid.shape), full(hi.shape)]
    args = [parity, lo, mid, hi]
    if own_grad:
        in_specs += [full(b[0].shape), full(b[1].shape), full(b[2].shape)]
        args += list(b)
    else:
        in_specs += [blk] * 4
        args += [b, g[0], g[1], g[2]]
    in_specs += [blk, blk]
    args += [c, old]
    out_specs = [blk] if want_force else []
    out_shape = [out] if want_force else []
    out_specs.append(blk)
    out_shape.append(out)
    if own_grad:
        out_specs += [blk] * 3
        out_shape += [out] * 3
    scratch = [pltpu.VMEM((planes + 2 * HALO, height + 2 * PADY, depth), jnp.float32)]
    if own_grad:
        scratch.append(pltpu.VMEM((planes + 2 * HALO, height + 2 * PADY, depth), jnp.float32))
    if track is not None:
        smem = pl.BlockSpec(memory_space=pltpu.SMEM)
        in_specs += [smem, smem, smem]
        args += list(track)
        count = track[2].shape[1]
        edge = jax.ShapeDtypeStruct((HALO, height, depth), jnp.float32)
        lines = jax.ShapeDtypeStruct((count, depth), jnp.float32)
        if edges:
            out_specs += [full(edge.shape), full(edge.shape)]
            out_shape += [edge, edge]
        out_specs.append(pl.BlockSpec((count, depth), lambda i: (0, 0)))
        out_shape.append(lines)
        scratch.append(pltpu.VMEM((planes * height, depth), jnp.float32))
    kernel = functools.partial(
        step_kernel, block=block, rows=rows, track=track is not None, own_grad=own_grad, want_force=want_force,
        edges=edges,
    )
    return pl.pallas_call(
        kernel,
        grid=(planes // block,),
        in_specs=in_specs,
        out_specs=out_specs,
        out_shape=out_shape,
        scratch_shapes=scratch,
        compiler_params=pltpu.CompilerParams(dimension_semantics=("arbitrary",)),
    )(*args)


def apply_grad(lo, mid, hi, rows=40):
    planes, height, depth = mid.shape
    block = pick_block(planes)
    full, blk = specs(mid.shape, block)
    out = jax.ShapeDtypeStruct(mid.shape, jnp.float32)
    return pl.pallas_call(
        functools.partial(grad_kernel, block=block, rows=rows),
        grid=(planes // block,),
        in_specs=[full(lo.shape), full(mid.shape), full(hi.shape)],
        out_specs=[blk, blk, blk],
        out_shape=[out, out, out],
        scratch_shapes=[pltpu.VMEM((planes + 2 * HALO, height + 2 * PADY, depth), jnp.float32)],
        compiler_params=pltpu.CompilerParams(dimension_semantics=("arbitrary",)),
    )(lo, mid, hi)


def reduce_members(part, axis):
    members = lax.axis_size(axis)
    if members & (members - 1) or part.size % (members * 1024):
        return lax.psum(part, axis) / members
    me = lax.axis_index(axis)
    rows = part.reshape(-1, 128)
    bits = members.bit_length() - 1
    for b in range(bits):
        mask = 1 << b
        half = rows.shape[0] // 2
        upper = (me // mask) % 2
        keep = lax.dynamic_slice_in_dim(rows, upper * half, half, 0)
        give = lax.dynamic_slice_in_dim(rows, (1 - upper) * half, half, 0)
        pairs = [(i, i ^ mask) for i in range(members)]
        rows = keep + lax.ppermute(give, axis, pairs)
    rows = rows / members
    for b in reversed(range(bits)):
        mask = 1 << b
        upper = (me // mask) % 2
        pairs = [(i, i ^ mask) for i in range(members)]
        other = lax.ppermute(rows, axis, pairs)
        rows = jnp.where(upper == 1, jnp.concatenate([other, rows]), jnp.concatenate([rows, other]))
    return rows.reshape(part.shape)


def swap_halos(sends, axis):
    count = lax.axis_size(axis)
    first = [(i, i ^ 1) for i in range(count) if i ^ 1 < count]
    second = [(i, i + 1) for i in range(1, count - 1, 2)] + [(i + 1, i) for i in range(1, count - 1, 2)]
    return lax.ppermute(sends[0], axis, first), lax.ppermute(sends[1], axis, second)


def halos(block, axis):
    planes = block.shape[0]
    odd = lax.axis_index(axis) % 2
    near = lax.dynamic_slice_in_dim(block, (1 - odd) * (planes - HALO), HALO, 0)
    far = lax.dynamic_slice_in_dim(block, odd * (planes - HALO), HALO, 0)
    return swap_halos((near, far), axis)


def inject(field, where, valid, values):
    flat = field.reshape(-1).at[where].add(jnp.where(valid, values, 0.0))
    return flat.reshape(field.shape)


def shards(
    courant,
    prev_field,
    cur_field,
    adj_prev,
    adj_cur,
    buoyancy,
    wavelet,
    src_cell,
    rec_cell,
    observed,
):
    speed = courant[0]
    planes, height, depth = buoyancy.shape
    volume = planes * height * depth
    offset = lax.axis_index("tile") * volume
    steps = wavelet.shape[0]

    def locate(cells):
        local = cells - offset
        valid = (local >= 0) & (local < volume)
        return (jnp.clip(local, 0, volume - 1), valid)

    src_local, src_valid = locate(src_cell)
    rec_local, rec_valid = locate(rec_cell)
    parity = (lax.axis_index("tile") % 2).astype(jnp.int32).reshape(1)
    b_lo, b_hi = halos(buoyancy, "tile")

    def spread(cells):
        return jnp.stack([cells // (height * depth), (cells // depth) % height, cells % depth])

    where = jnp.concatenate([spread(src_local)[:, 0], src_valid.astype(jnp.int32)])
    receivers = jnp.stack([rec_local // depth, rec_local % depth])
    older, now = (prev_field[0], cur_field[0])
    lo, hi = halos(now, "tile")
    forces = []
    samples = []
    grad_b = None
    for k in range(steps):
        track = (where, wavelet[k:k + 1], receivers)
        if grad_b is None:
            outs = apply_step(parity, lo, now, hi, (b_lo, buoyancy, b_hi), None, speed, older, track)
            force, newer = outs[:2]
            grad_b = outs[2:5]
            edge_lo, edge_hi, lines = outs[5:]
        else:
            outs = apply_step(parity, lo, now, hi, buoyancy, grad_b, speed, older, track, edges=k + 1 < steps)
            force, newer, lines = outs[0], outs[1], outs[-1]
            edge_lo, edge_hi = (outs[2], outs[3]) if k + 1 < steps else (None, None)
        if k + 1 < steps:
            lo, hi = swap_halos((edge_lo, edge_hi), "tile")
        samples.append(jnp.sum(lines, axis=1))
        forces.append(force)
        older, now = (now, newer)
    residual = jnp.where(rec_valid, jnp.stack(samples) - observed, 0.0)
    older, now = (adj_prev[0], adj_cur[0])
    image_part = jnp.zeros(buoyancy.shape, jnp.float32)
    for j in range(steps):
        lo, hi = halos(now, "tile")
        if j + 1 < steps:
            (newer,) = apply_step(parity, lo, now, hi, buoyancy, grad_b, speed, older, want_force=False)
            newer = inject(newer, rec_local, rec_valid, residual[steps - 1 - j])
        else:
            cells = jnp.stack([rec_local // (height * depth), (rec_local // depth) % height, rec_local % depth])
            valid = rec_valid.astype(jnp.int32)
            newer = apply_final(parity, lo, now, hi, buoyancy, grad_b, speed, older, cells, valid, residual[0])
        image_part = image_part + newer * forces[steps - 1 - j]
        older, now = (now, newer)
    image = reduce_members(image_part, "real")
    return (image, now[None])


def solution(mesh):
    in_specs = (
        P("real", "tile", None, None),
        P(("shot", "real"), "tile", None, None),
        P(("shot", "real"), "tile", None, None),
        P(("shot", "real"), "tile", None, None),
        P(("shot", "real"), "tile", None, None),
        P("tile", None, None),
        P("shot"),
        P("shot"),
        P("shot"),
        P("shot", None),
    )
    out_specs = (P(("shot", "tile"), None, None), P(("shot", "real"), "tile", None, None))
    return jax.shard_map(shards, mesh=mesh, in_specs=in_specs, out_specs=out_specs, check_vma=False)
```

```python
import functools
import jax
import jax.numpy as jnp
from jax import lax
from jax.experimental import pallas as pl
from jax.experimental.pallas import tpu as pltpu
from jax.sharding import PartitionSpec as P

SECOND = (-205.0 / 72.0, 8.0 / 5.0, -1.0 / 5.0, 8.0 / 315.0, -1.0 / 560.0)
FIRST = (4.0 / 5.0, -1.0 / 5.0, 4.0 / 105.0, -1.0 / 280.0)
HALO = 4
PADY = 8


def lane_shift(v, k, lane):
    width = v.shape[-1]
    if k > 0:
        rolled = pltpu.roll(v, width - k, 1)
        return jnp.where(lane < width - k, rolled, 0.0)
    rolled = pltpu.roll(v, -k, 1)
    return jnp.where(lane >= -k, rolled, 0.0)


def fill_padded(pad_ref, first_ref, mid_ref, second_ref, odd):
    planes, height, depth = mid_ref.shape
    pad_ref[...] = jnp.zeros(pad_ref.shape, jnp.float32)
    first = first_ref[...]
    second = second_ref[...]
    pad_ref[0:HALO, PADY:PADY + height, :] = jnp.where(odd, first, second)
    pad_ref[HALO:HALO + planes, PADY:PADY + height, :] = mid_ref[...]
    pad_ref[HALO + planes:, PADY:PADY + height, :] = jnp.where(odd, second, first)


def taps(pad_ref, plane, y0, rows, lane):
    def at(dx, dy):
        return pad_ref[plane + dx, pl.ds(PADY + y0 + dy, rows), :]
    centre = at(0, 0)
    lap = 3.0 * SECOND[0] * centre
    grads = []
    for axis in range(3):
        if axis == 0:
            get = lambda k: at(k, 0)
        elif axis == 1:
            get = lambda k: at(0, k)
        else:
            get = lambda k: lane_shift(centre, k, lane)
        vals = {k: get(k) for k in (1, 2, 3, 4, -1, -2, -3, -4)}
        for k in range(1, 5):
            lap = lap + SECOND[k] * (vals[k] + vals[-k])
        slope = FIRST[0] * (vals[1] - vals[-1])
        for k in range(2, 5):
            slope = slope + FIRST[k - 1] * (vals[k] - vals[-k])
        grads.append(slope)
    return centre, lap, grads


def step_kernel(*refs, block, rows, track, own_grad, want_force, edges):
    refs = list(refs)
    take = lambda n: [refs.pop(0) for _ in range(n)]
    (parity_ref,) = take(1)
    lo_ref, mid_ref, hi_ref = take(3)
    if own_grad:
        b_lo_ref, b_mid_ref, b_hi_ref = take(3)
    else:
        b_ref, g0_ref, g1_ref, g2_ref = take(4)
    c_ref, old_ref = take(2)
    if track:
        where_ref, amount_ref, rec_ref = take(3)
    force_ref = take(1)[0] if want_force else None
    (new_ref,) = take(1)
    if own_grad:
        g_out = take(3)
    if track and edges:
        edge_lo_ref, edge_hi_ref = take(2)
    if track:
        (sample_ref,) = take(1)
    (pad_ref,) = take(1)
    if own_grad:
        (b_pad_ref,) = take(1)
    if track:
        (keep_ref,) = take(1)
    i = pl.program_id(0)

    odd = parity_ref[0] == 1

    @pl.when(i == 0)
    def _():
        fill_padded(pad_ref, lo_ref, mid_ref, hi_ref, odd)
        if own_grad:
            fill_padded(b_pad_ref, b_lo_ref, b_mid_ref, b_hi_ref, odd)

    planes = mid_ref.shape[0]
    height = c_ref.shape[1]
    depth = c_ref.shape[2]
    lane = lax.broadcasted_iota(jnp.int32, (rows, depth), 1)
    row = lax.broadcasted_iota(jnp.int32, (rows, depth), 0)
    for p in range(block):
        plane = i * block + p + HALO
        for y0 in range(0, height, rows):
            sl = (p, pl.ds(y0, rows), slice(None))
            centre, lap, grads = taps(pad_ref, plane, y0, rows, lane)
            if own_grad:
                bvals, _, gb = taps(b_pad_ref, plane, y0, rows, lane)
                for out_ref, value in zip(g_out, gb):
                    out_ref[sl] = value
            else:
                bvals = b_ref[sl]
                gb = [g0_ref[sl], g1_ref[sl], g2_ref[sl]]
            force = bvals * lap + (gb[0] * grads[0] + gb[1] * grads[1] + gb[2] * grads[2])
            if want_force:
                force_ref[sl] = force
            newer = 2.0 * centre - old_ref[sl] + c_ref[sl] * force
            if track:
                hit = (where_ref[3] == 1) & (where_ref[0] == plane - HALO)
                mask = hit & (row == where_ref[1] - y0) & (lane == where_ref[2])
                newer = jnp.where(mask, newer + amount_ref[0], newer)
                keep_ref[pl.ds(pl.multiple_of((plane - HALO) * height + y0, 8), rows), :] = newer
            new_ref[sl] = newer

    if track:
        @pl.when(i == pl.num_programs(0) - 1)
        def _():
            if edges:
                for q in range(HALO):
                    bottom = keep_ref[q * height:(q + 1) * height, :]
                    top = keep_ref[(planes - HALO + q) * height:(planes - HALO + q + 1) * height, :]
                    edge_lo_ref[q] = jnp.where(odd, bottom, top)
                    edge_hi_ref[q] = jnp.where(odd, top, bottom)
            one_lane = lax.broadcasted_iota(jnp.int32, (1, depth), 1)

            def sample(r, carry):
                line = keep_ref[pl.ds(rec_ref[0, r], 1), :]
                sample_ref[pl.ds(r, 1), :] = jnp.where(one_lane == rec_ref[1, r], line, 0.0)
                return carry

            lax.fori_loop(0, sample_ref.shape[0], sample, 0, unroll=8)


def grad_kernel(lo_ref, mid_ref, hi_ref, g0_ref, g1_ref, g2_ref, pad_ref, *, block, rows):
    i = pl.program_id(0)

    @pl.when(i == 0)
    def _():
        fill_padded(pad_ref, lo_ref, mid_ref, hi_ref)

    height = mid_ref.shape[1]
    lane = lax.broadcasted_iota(jnp.int32, (rows, mid_ref.shape[2]), 1)
    for p in range(block):
        plane = i * block + p + HALO
        for y0 in range(0, height, rows):
            sl = (p, pl.ds(y0, rows), slice(None))
            _, _, grads = taps(pad_ref, plane, y0, rows, lane)
            g0_ref[sl] = grads[0]
            g1_ref[sl] = grads[1]
            g2_ref[sl] = grads[2]


def final_kernel(parity_ref, lo_ref, mid_ref, hi_ref, b_ref, g0_ref, g1_ref, g2_ref, c_ref, old_ref,
                 rec_ref, valid_ref, amount_ref, new_ref, pad_ref, *, block, rows):
    i = pl.program_id(0)
    odd = parity_ref[0] == 1

    @pl.when(i == 0)
    def _():
        fill_padded(pad_ref, lo_ref, mid_ref, hi_ref, odd)

    planes, height, depth = mid_ref.shape
    lane = lax.broadcasted_iota(jnp.int32, (rows, depth), 1)
    for p in range(block):
        plane = i * block + p + HALO
        for y0 in range(0, height, rows):
            sl = (p, pl.ds(y0, rows), slice(None))
            centre, lap, grads = taps(pad_ref, plane, y0, rows, lane)
            force = b_ref[sl] * lap + (g0_ref[sl] * grads[0] + g1_ref[sl] * grads[1] + g2_ref[sl] * grads[2])
            new_ref[plane - HALO, pl.ds(y0, rows), :] = 2.0 * centre - old_ref[sl] + c_ref[sl] * force

    @pl.when(i == pl.num_programs(0) - 1)
    def _():
        one_lane = lax.broadcasted_iota(jnp.int32, (1, depth), 1)

        def add(r, carry):
            x = rec_ref[0, r]
            y = rec_ref[1, r]
            hit = (one_lane == rec_ref[2, r]) & (valid_ref[r] == 1)
            line = new_ref[x, pl.ds(y, 1), :]
            new_ref[x, pl.ds(y, 1), :] = jnp.where(hit, line + amount_ref[r], line)
            return carry

        lax.fori_loop(0, amount_ref.shape[0], add, 0, unroll=32)


def apply_final(parity, lo, mid, hi, b, g, c, old, receivers, valid, amount, rows=40):
    planes, height, depth = mid.shape
    block = pick_block(planes)
    full, blk = specs(mid.shape, block)
    out = jax.ShapeDtypeStruct(mid.shape, jnp.float32)
    smem = pl.BlockSpec(memory_space=pltpu.SMEM)
    return pl.pallas_call(
        functools.partial(final_kernel, block=block, rows=rows),
        grid=(planes // block,),
        in_specs=[smem, full(lo.shape), full(mid.shape), full(hi.shape)] + [blk] * 6
        + [smem, smem, smem],
        out_specs=full(mid.shape),
        out_shape=out,
        scratch_shapes=[pltpu.VMEM((planes + 2 * HALO, height + 2 * PADY, depth), jnp.float32)],
        compiler_params=pltpu.CompilerParams(dimension_semantics=("arbitrary",)),
    )(parity, lo, mid, hi, b, g[0], g[1], g[2], c, old, receivers, valid, amount)


def pick_block(planes):
    for b in (4, 2, 1):
        if planes % b == 0:
            return b


def specs(shape, block):
    planes, height, depth = shape
    full = lambda s: pl.BlockSpec(s, lambda i: (0, 0, 0))
    blk = pl.BlockSpec((block, height, depth), lambda i: (i, 0, 0))
    return full, blk


def apply_step(parity, lo, mid, hi, b, g, c, old, track=None, rows=40, want_force=True, edges=True):
    planes, height, depth = mid.shape
    block = pick_block(planes)
    full, blk = specs(mid.shape, block)
    out = jax.ShapeDtypeStruct(mid.shape, jnp.float32)
    own_grad = g is None
    in_specs = [pl.BlockSpec(memory_space=pltpu.SMEM), full(lo.shape), full(mid.shape), full(hi.shape)]
    args = [parity, lo, mid, hi]
    if own_grad:
        in_specs += [full(b[0].shape), full(b[1].shape), full(b[2].shape)]
        args += list(b)
    else:
        in_specs += [blk] * 4
        args += [b, g[0], g[1], g[2]]
    in_specs += [blk, blk]
    args += [c, old]
    out_specs = [blk] if want_force else []
    out_shape = [out] if want_force else []
    out_specs.append(blk)
    out_shape.append(out)
    if own_grad:
        out_specs += [blk] * 3
        out_shape += [out] * 3
    scratch = [pltpu.VMEM((planes + 2 * HALO, height + 2 * PADY, depth), jnp.float32)]
    if own_grad:
        scratch.append(pltpu.VMEM((planes + 2 * HALO, height + 2 * PADY, depth), jnp.float32))
    if track is not None:
        smem = pl.BlockSpec(memory_space=pltpu.SMEM)
        in_specs += [smem, smem, smem]
        args += list(track)
        count = track[2].shape[1]
        edge = jax.ShapeDtypeStruct((HALO, height, depth), jnp.float32)
        lines = jax.ShapeDtypeStruct((count, depth), jnp.float32)
        if edges:
            out_specs += [full(edge.shape), full(edge.shape)]
            out_shape += [edge, edge]
        out_specs.append(pl.BlockSpec((count, depth), lambda i: (0, 0)))
        out_shape.append(lines)
        scratch.append(pltpu.VMEM((planes * height, depth), jnp.float32))
    kernel = functools.partial(
        step_kernel, block=block, rows=rows, track=track is not None, own_grad=own_grad, want_force=want_force,
        edges=edges,
    )
    return pl.pallas_call(
        kernel,
        grid=(planes // block,),
        in_specs=in_specs,
        out_specs=out_specs,
        out_shape=out_shape,
        scratch_shapes=scratch,
        compiler_params=pltpu.CompilerParams(dimension_semantics=("arbitrary",)),
    )(*args)


def apply_grad(lo, mid, hi, rows=40):
    planes, height, depth = mid.shape
    block = pick_block(planes)
    full, blk = specs(mid.shape, block)
    out = jax.ShapeDtypeStruct(mid.shape, jnp.float32)
    return pl.pallas_call(
        functools.partial(grad_kernel, block=block, rows=rows),
        grid=(planes // block,),
        in_specs=[full(lo.shape), full(mid.shape), full(hi.shape)],
        out_specs=[blk, blk, blk],
        out_shape=[out, out, out],
        scratch_shapes=[pltpu.VMEM((planes + 2 * HALO, height + 2 * PADY, depth), jnp.float32)],
        compiler_params=pltpu.CompilerParams(dimension_semantics=("arbitrary",)),
    )(lo, mid, hi)


def reduce_members(part, axis):
    members = lax.axis_size(axis)
    if members & (members - 1) or part.size % (members * 1024):
        return lax.psum(part, axis) / members
    me = lax.axis_index(axis)
    rows = part.reshape(-1, 128)
    bits = members.bit_length() - 1
    for b in range(bits):
        mask = 1 << b
        half = rows.shape[0] // 2
        upper = (me // mask) % 2
        keep = lax.dynamic_slice_in_dim(rows, upper * half, half, 0)
        give = lax.dynamic_slice_in_dim(rows, (1 - upper) * half, half, 0)
        pairs = [(i, i ^ mask) for i in range(members)]
        rows = keep + lax.ppermute(give, axis, pairs)
    rows = rows / members
    for b in reversed(range(bits)):
        mask = 1 << b
        upper = (me // mask) % 2
        pairs = [(i, i ^ mask) for i in range(members)]
        other = lax.ppermute(rows, axis, pairs)
        rows = jnp.where(upper == 1, jnp.concatenate([other, rows]), jnp.concatenate([rows, other]))
    return rows.reshape(part.shape)


def swap_halos(sends, axis):
    count = lax.axis_size(axis)
    first = [(i, i ^ 1) for i in range(count) if i ^ 1 < count]
    second = [(i, i + 1) for i in range(1, count - 1, 2)] + [(i + 1, i) for i in range(1, count - 1, 2)]
    return lax.ppermute(sends[0], axis, first), lax.ppermute(sends[1], axis, second)


def halos(block, axis):
    planes = block.shape[0]
    odd = lax.axis_index(axis) % 2
    near = lax.dynamic_slice_in_dim(block, (1 - odd) * (planes - HALO), HALO, 0)
    far = lax.dynamic_slice_in_dim(block, odd * (planes - HALO), HALO, 0)
    return swap_halos((near, far), axis)


def inject(field, where, valid, values):
    flat = field.reshape(-1).at[where].add(jnp.where(valid, values, 0.0))
    return flat.reshape(field.shape)


def shards(
    courant,
    prev_field,
    cur_field,
    adj_prev,
    adj_cur,
    buoyancy,
    wavelet,
    src_cell,
    rec_cell,
    observed,
):
    speed = courant[0]
    planes, height, depth = buoyancy.shape
    volume = planes * height * depth
    offset = lax.axis_index("tile") * volume
    steps = wavelet.shape[0]

    def locate(cells):
        local = cells - offset
        valid = (local >= 0) & (local < volume)
        return (jnp.clip(local, 0, volume - 1), valid)

    src_local, src_valid = locate(src_cell)
    rec_local, rec_valid = locate(rec_cell)
    parity = (lax.axis_index("tile") % 2).astype(jnp.int32).reshape(1)
    b_lo, b_hi = halos(buoyancy, "tile")

    def spread(cells):
        return jnp.stack([cells // (height * depth), (cells // depth) % height, cells % depth])

    where = jnp.concatenate([spread(src_local)[:, 0], src_valid.astype(jnp.int32)])
    receivers = jnp.stack([rec_local // depth, rec_local % depth])
    older, now = (prev_field[0], cur_field[0])
    lo, hi = halos(now, "tile")
    forces = []
    samples = []
    grad_b = None
    for k in range(steps):
        track = (where, wavelet[k:k + 1], receivers)
        if grad_b is None:
            outs = apply_step(parity, lo, now, hi, (b_lo, buoyancy, b_hi), None, speed, older, track)
            force, newer = outs[:2]
            grad_b = outs[2:5]
            edge_lo, edge_hi, lines = outs[5:]
        else:
            outs = apply_step(parity, lo, now, hi, buoyancy, grad_b, speed, older, track, edges=k + 1 < steps)
            force, newer, lines = outs[0], outs[1], outs[-1]
            edge_lo, edge_hi = (outs[2], outs[3]) if k + 1 < steps else (None, None)
        if k + 1 < steps:
            lo, hi = swap_halos((edge_lo, edge_hi), "tile")
        samples.append(jnp.sum(lines, axis=1))
        forces.append(force)
        older, now = (now, newer)
    residual = jnp.where(rec_valid, jnp.stack(samples) - observed, 0.0)
    older, now = (adj_prev[0], adj_cur[0])
    image_part = jnp.zeros(buoyancy.shape, jnp.float32)
    for j in range(steps):
        lo, hi = halos(now, "tile")
        if j + 1 < steps:
            (newer,) = apply_step(parity, lo, now, hi, buoyancy, grad_b, speed, older, want_force=False)
            newer = inject(newer, rec_local, rec_valid, residual[steps - 1 - j])
        else:
            cells = jnp.stack([rec_local // (height * depth), (rec_local // depth) % height, rec_local % depth])
            valid = rec_valid.astype(jnp.int32)
            newer = apply_final(parity, lo, now, hi, buoyancy, grad_b, speed, older, cells, valid, residual[0])
        image_part = image_part + newer * forces[steps - 1 - j]
        older, now = (now, newer)
    image = reduce_members(image_part, "real")
    return (image, now[None])


def solution(mesh):
    in_specs = (
        P("real", "tile", None, None),
        P(("shot", "real"), "tile", None, None),
        P(("shot", "real"), "tile", None, None),
        P(("shot", "real"), "tile", None, None),
        P(("shot", "real"), "tile", None, None),
        P("tile", None, None),
        P("shot"),
        P("shot"),
        P("shot"),
        P("shot", None),
    )
    out_specs = (P(("shot", "tile"), None, None), P(("shot", "real"), "tile", None, None))
    return jax.shard_map(shards, mesh=mesh, in_specs=in_specs, out_specs=out_specs, check_vma=False)
```

```python
import functools
import jax
import jax.numpy as jnp
from jax import lax
from jax.experimental import pallas as pl
from jax.experimental.pallas import tpu as pltpu
from jax.sharding import PartitionSpec as P

SECOND = (-205.0 / 72.0, 8.0 / 5.0, -1.0 / 5.0, 8.0 / 315.0, -1.0 / 560.0)
FIRST = (4.0 / 5.0, -1.0 / 5.0, 4.0 / 105.0, -1.0 / 280.0)
HALO = 4
PADY = 8


def lane_shift(v, k, lane):
    width = v.shape[-1]
    if k > 0:
        rolled = pltpu.roll(v, width - k, 1)
        return jnp.where(lane < width - k, rolled, 0.0)
    rolled = pltpu.roll(v, -k, 1)
    return jnp.where(lane >= -k, rolled, 0.0)


def fill_padded(pad_ref, first_ref, mid_ref, second_ref, odd):
    planes, height, depth = mid_ref.shape
    pad_ref[...] = jnp.zeros(pad_ref.shape, jnp.float32)
    first = first_ref[...]
    second = second_ref[...]
    pad_ref[0:HALO, PADY:PADY + height, :] = jnp.where(odd, first, second)
    pad_ref[HALO:HALO + planes, PADY:PADY + height, :] = mid_ref[...]
    pad_ref[HALO + planes:, PADY:PADY + height, :] = jnp.where(odd, second, first)


def taps(pad_ref, plane, y0, rows, lane):
    def at(dx, dy):
        return pad_ref[plane + dx, pl.ds(PADY + y0 + dy, rows), :]
    centre = at(0, 0)
    lap = 3.0 * SECOND[0] * centre
    grads = []
    for axis in range(3):
        if axis == 0:
            get = lambda k: at(k, 0)
        elif axis == 1:
            get = lambda k: at(0, k)
        else:
            get = lambda k: lane_shift(centre, k, lane)
        vals = {k: get(k) for k in (1, 2, 3, 4, -1, -2, -3, -4)}
        for k in range(1, 5):
            lap = lap + SECOND[k] * (vals[k] + vals[-k])
        slope = FIRST[0] * (vals[1] - vals[-1])
        for k in range(2, 5):
            slope = slope + FIRST[k - 1] * (vals[k] - vals[-k])
        grads.append(slope)
    return centre, lap, grads


def step_kernel(*refs, block, rows, track, own_grad, want_force, edges):
    refs = list(refs)
    take = lambda n: [refs.pop(0) for _ in range(n)]
    (parity_ref,) = take(1)
    lo_ref, mid_ref, hi_ref = take(3)
    if own_grad:
        b_lo_ref, b_mid_ref, b_hi_ref = take(3)
    else:
        b_ref, g0_ref, g1_ref, g2_ref = take(4)
    c_ref, old_ref = take(2)
    if track:
        where_ref, amount_ref, rec_ref = take(3)
    force_ref = take(1)[0] if want_force else None
    (new_ref,) = take(1)
    if own_grad:
        g_out = take(3)
    if track and edges:
        edge_lo_ref, edge_hi_ref = take(2)
    if track:
        (sample_ref,) = take(1)
    (pad_ref,) = take(1)
    if own_grad:
        (b_pad_ref,) = take(1)
    if track:
        (keep_ref,) = take(1)
    i = pl.program_id(0)

    odd = parity_ref[0] == 1

    @pl.when(i == 0)
    def _():
        fill_padded(pad_ref, lo_ref, mid_ref, hi_ref, odd)
        if own_grad:
            fill_padded(b_pad_ref, b_lo_ref, b_mid_ref, b_hi_ref, odd)

    planes = mid_ref.shape[0]
    height = c_ref.shape[1]
    depth = c_ref.shape[2]
    lane = lax.broadcasted_iota(jnp.int32, (rows, depth), 1)
    row = lax.broadcasted_iota(jnp.int32, (rows, depth), 0)
    for p in range(block):
        plane = i * block + p + HALO
        for y0 in range(0, height, rows):
            sl = (p, pl.ds(y0, rows), slice(None))
            centre, lap, grads = taps(pad_ref, plane, y0, rows, lane)
            if own_grad:
                bvals, _, gb = taps(b_pad_ref, plane, y0, rows, lane)
                for out_ref, value in zip(g_out, gb):
                    out_ref[sl] = value
            else:
                bvals = b_ref[sl]
                gb = [g0_ref[sl], g1_ref[sl], g2_ref[sl]]
            force = bvals * lap + (gb[0] * grads[0] + gb[1] * grads[1] + gb[2] * grads[2])
            if want_force:
                force_ref[sl] = force
            newer = 2.0 * centre - old_ref[sl] + c_ref[sl] * force
            if track:
                hit = (where_ref[3] == 1) & (where_ref[0] == plane - HALO)
                mask = hit & (row == where_ref[1] - y0) & (lane == where_ref[2])
                newer = jnp.where(mask, newer + amount_ref[0], newer)
                keep_ref[pl.ds(pl.multiple_of((plane - HALO) * height + y0, 8), rows), :] = newer
            new_ref[sl] = newer

    if track:
        @pl.when(i == pl.num_programs(0) - 1)
        def _():
            if edges:
                for q in range(HALO):
                    bottom = keep_ref[q * height:(q + 1) * height, :]
                    top = keep_ref[(planes - HALO + q) * height:(planes - HALO + q + 1) * height, :]
                    edge_lo_ref[q] = jnp.where(odd, bottom, top)
                    edge_hi_ref[q] = jnp.where(odd, top, bottom)
            one_lane = lax.broadcasted_iota(jnp.int32, (1, depth), 1)

            def sample(r, carry):
                line = keep_ref[pl.ds(rec_ref[0, r], 1), :]
                sample_ref[pl.ds(r, 1), :] = jnp.where(one_lane == rec_ref[1, r], line, 0.0)
                return carry

            lax.fori_loop(0, sample_ref.shape[0], sample, 0, unroll=8)


def grad_kernel(lo_ref, mid_ref, hi_ref, g0_ref, g1_ref, g2_ref, pad_ref, *, block, rows):
    i = pl.program_id(0)

    @pl.when(i == 0)
    def _():
        fill_padded(pad_ref, lo_ref, mid_ref, hi_ref)

    height = mid_ref.shape[1]
    lane = lax.broadcasted_iota(jnp.int32, (rows, mid_ref.shape[2]), 1)
    for p in range(block):
        plane = i * block + p + HALO
        for y0 in range(0, height, rows):
            sl = (p, pl.ds(y0, rows), slice(None))
            _, _, grads = taps(pad_ref, plane, y0, rows, lane)
            g0_ref[sl] = grads[0]
            g1_ref[sl] = grads[1]
            g2_ref[sl] = grads[2]


def final_kernel(parity_ref, lo_ref, mid_ref, hi_ref, b_ref, g0_ref, g1_ref, g2_ref, c_ref, old_ref,
                 rec_ref, valid_ref, amount_ref, new_ref, pad_ref, *, block, rows):
    i = pl.program_id(0)
    odd = parity_ref[0] == 1

    @pl.when(i == 0)
    def _():
        fill_padded(pad_ref, lo_ref, mid_ref, hi_ref, odd)

    planes, height, depth = mid_ref.shape
    lane = lax.broadcasted_iota(jnp.int32, (rows, depth), 1)
    for p in range(block):
        plane = i * block + p + HALO
        for y0 in range(0, height, rows):
            sl = (p, pl.ds(y0, rows), slice(None))
            centre, lap, grads = taps(pad_ref, plane, y0, rows, lane)
            force = b_ref[sl] * lap + (g0_ref[sl] * grads[0] + g1_ref[sl] * grads[1] + g2_ref[sl] * grads[2])
            new_ref[plane - HALO, pl.ds(y0, rows), :] = 2.0 * centre - old_ref[sl] + c_ref[sl] * force

    @pl.when(i == pl.num_programs(0) - 1)
    def _():
        one_lane = lax.broadcasted_iota(jnp.int32, (1, depth), 1)

        def add(r, carry):
            x = rec_ref[0, r]
            y = rec_ref[1, r]
            hit = (one_lane == rec_ref[2, r]) & (valid_ref[r] == 1)
            line = new_ref[x, pl.ds(y, 1), :]
            new_ref[x, pl.ds(y, 1), :] = jnp.where(hit, line + amount_ref[r], line)
            return carry

        lax.fori_loop(0, amount_ref.shape[0], add, 0, unroll=8)


def apply_final(parity, lo, mid, hi, b, g, c, old, receivers, valid, amount, rows=40):
    planes, height, depth = mid.shape
    block = pick_block(planes)
    full, blk = specs(mid.shape, block)
    out = jax.ShapeDtypeStruct(mid.shape, jnp.float32)
    smem = pl.BlockSpec(memory_space=pltpu.SMEM)
    return pl.pallas_call(
        functools.partial(final_kernel, block=block, rows=rows),
        grid=(planes // block,),
        in_specs=[smem, full(lo.shape), full(mid.shape), full(hi.shape)] + [blk] * 6
        + [smem, smem, smem],
        out_specs=full(mid.shape),
        out_shape=out,
        scratch_shapes=[pltpu.VMEM((planes + 2 * HALO, height + 2 * PADY, depth), jnp.float32)],
        compiler_params=pltpu.CompilerParams(dimension_semantics=("arbitrary",)),
    )(parity, lo, mid, hi, b, g[0], g[1], g[2], c, old, receivers, valid, amount)


def pick_block(planes):
    for b in (4, 2, 1):
        if planes % b == 0:
            return b


def specs(shape, block):
    planes, height, depth = shape
    full = lambda s: pl.BlockSpec(s, lambda i: (0, 0, 0))
    blk = pl.BlockSpec((block, height, depth), lambda i: (i, 0, 0))
    return full, blk


def apply_step(parity, lo, mid, hi, b, g, c, old, track=None, rows=40, want_force=True, edges=True):
    planes, height, depth = mid.shape
    block = pick_block(planes)
    full, blk = specs(mid.shape, block)
    out = jax.ShapeDtypeStruct(mid.shape, jnp.float32)
    own_grad = g is None
    in_specs = [pl.BlockSpec(memory_space=pltpu.SMEM), full(lo.shape), full(mid.shape), full(hi.shape)]
    args = [parity, lo, mid, hi]
    if own_grad:
        in_specs += [full(b[0].shape), full(b[1].shape), full(b[2].shape)]
        args += list(b)
    else:
        in_specs += [blk] * 4
        args += [b, g[0], g[1], g[2]]
    in_specs += [blk, blk]
    args += [c, old]
    out_specs = [blk] if want_force else []
    out_shape = [out] if want_force else []
    out_specs.append(blk)
    out_shape.append(out)
    if own_grad:
        out_specs += [blk] * 3
        out_shape += [out] * 3
    scratch = [pltpu.VMEM((planes + 2 * HALO, height + 2 * PADY, depth), jnp.float32)]
    if own_grad:
        scratch.append(pltpu.VMEM((planes + 2 * HALO, height + 2 * PADY, depth), jnp.float32))
    if track is not None:
        smem = pl.BlockSpec(memory_space=pltpu.SMEM)
        in_specs += [smem, smem, smem]
        args += list(track)
        count = track[2].shape[1]
        edge = jax.ShapeDtypeStruct((HALO, height, depth), jnp.float32)
        lines = jax.ShapeDtypeStruct((count, depth), jnp.float32)
        if edges:
            out_specs += [full(edge.shape), full(edge.shape)]
            out_shape += [edge, edge]
        out_specs.append(pl.BlockSpec((count, depth), lambda i: (0, 0)))
        out_shape.append(lines)
        scratch.append(pltpu.VMEM((planes * height, depth), jnp.float32))
    kernel = functools.partial(
        step_kernel, block=block, rows=rows, track=track is not None, own_grad=own_grad, want_force=want_force,
        edges=edges,
    )
    return pl.pallas_call(
        kernel,
        grid=(planes // block,),
        in_specs=in_specs,
        out_specs=out_specs,
        out_shape=out_shape,
        scratch_shapes=scratch,
        compiler_params=pltpu.CompilerParams(dimension_semantics=("arbitrary",)),
    )(*args)


def apply_grad(lo, mid, hi, rows=40):
    planes, height, depth = mid.shape
    block = pick_block(planes)
    full, blk = specs(mid.shape, block)
    out = jax.ShapeDtypeStruct(mid.shape, jnp.float32)
    return pl.pallas_call(
        functools.partial(grad_kernel, block=block, rows=rows),
        grid=(planes // block,),
        in_specs=[full(lo.shape), full(mid.shape), full(hi.shape)],
        out_specs=[blk, blk, blk],
        out_shape=[out, out, out],
        scratch_shapes=[pltpu.VMEM((planes + 2 * HALO, height + 2 * PADY, depth), jnp.float32)],
        compiler_params=pltpu.CompilerParams(dimension_semantics=("arbitrary",)),
    )(lo, mid, hi)


def reduce_members(part, axis):
    members = lax.axis_size(axis)
    if members & (members - 1) or part.size % (members * 1024):
        return lax.psum(part, axis) / members
    me = lax.axis_index(axis)
    rows = part.reshape(-1, 128)
    bits = members.bit_length() - 1
    for b in range(bits):
        mask = 1 << b
        half = rows.shape[0] // 2
        upper = (me // mask) % 2
        keep = lax.dynamic_slice_in_dim(rows, upper * half, half, 0)
        give = lax.dynamic_slice_in_dim(rows, (1 - upper) * half, half, 0)
        pairs = [(i, i ^ mask) for i in range(members)]
        rows = keep + lax.ppermute(give, axis, pairs)
    rows = rows / members
    for b in reversed(range(bits)):
        mask = 1 << b
        upper = (me // mask) % 2
        pairs = [(i, i ^ mask) for i in range(members)]
        other = lax.ppermute(rows, axis, pairs)
        rows = jnp.where(upper == 1, jnp.concatenate([other, rows]), jnp.concatenate([rows, other]))
    return rows.reshape(part.shape)


def swap_halos(sends, axis):
    count = lax.axis_size(axis)
    first = [(i, i ^ 1) for i in range(count) if i ^ 1 < count]
    second = [(i, i + 1) for i in range(1, count - 1, 2)] + [(i + 1, i) for i in range(1, count - 1, 2)]
    return lax.ppermute(sends[0], axis, first), lax.ppermute(sends[1], axis, second)


def halos(block, axis):
    planes = block.shape[0]
    odd = lax.axis_index(axis) % 2
    near = lax.dynamic_slice_in_dim(block, (1 - odd) * (planes - HALO), HALO, 0)
    far = lax.dynamic_slice_in_dim(block, odd * (planes - HALO), HALO, 0)
    return swap_halos((near, far), axis)


def inject(field, where, valid, values):
    flat = field.reshape(-1).at[where].add(jnp.where(valid, values, 0.0))
    return flat.reshape(field.shape)


def shards(
    courant,
    prev_field,
    cur_field,
    adj_prev,
    adj_cur,
    buoyancy,
    wavelet,
    src_cell,
    rec_cell,
    observed,
):
    speed = courant[0]
    planes, height, depth = buoyancy.shape
    volume = planes * height * depth
    offset = lax.axis_index("tile") * volume
    steps = wavelet.shape[0]

    def locate(cells):
        local = cells - offset
        valid = (local >= 0) & (local < volume)
        return (jnp.clip(local, 0, volume - 1), valid)

    src_local, src_valid = locate(src_cell)
    rec_local, rec_valid = locate(rec_cell)
    parity = (lax.axis_index("tile") % 2).astype(jnp.int32).reshape(1)
    b_lo, b_hi = halos(buoyancy, "tile")

    def spread(cells):
        return jnp.stack([cells // (height * depth), (cells // depth) % height, cells % depth])

    where = jnp.concatenate([spread(src_local)[:, 0], src_valid.astype(jnp.int32)])
    receivers = jnp.stack([rec_local // depth, rec_local % depth])
    older, now = (prev_field[0], cur_field[0])
    lo, hi = halos(now, "tile")
    forces = []
    samples = []
    grad_b = None
    for k in range(steps):
        track = (where, wavelet[k:k + 1], receivers)
        if grad_b is None:
            outs = apply_step(parity, lo, now, hi, (b_lo, buoyancy, b_hi), None, speed, older, track)
            force, newer = outs[:2]
            grad_b = outs[2:5]
            edge_lo, edge_hi, lines = outs[5:]
        else:
            outs = apply_step(parity, lo, now, hi, buoyancy, grad_b, speed, older, track, edges=k + 1 < steps)
            force, newer, lines = outs[0], outs[1], outs[-1]
            edge_lo, edge_hi = (outs[2], outs[3]) if k + 1 < steps else (None, None)
        if k + 1 < steps:
            lo, hi = swap_halos((edge_lo, edge_hi), "tile")
        samples.append(jnp.sum(lines, axis=1))
        forces.append(force)
        older, now = (now, newer)
    residual = jnp.where(rec_valid, jnp.stack(samples) - observed, 0.0)
    older, now = (adj_prev[0], adj_cur[0])
    image_part = jnp.zeros(buoyancy.shape, jnp.float32)
    for j in range(steps):
        lo, hi = halos(now, "tile")
        cells = jnp.stack([rec_local // (height * depth), (rec_local // depth) % height, rec_local % depth])
        valid = rec_valid.astype(jnp.int32)
        values = residual[steps - 1 - j]
        newer = apply_final(parity, lo, now, hi, buoyancy, grad_b, speed, older, cells, valid, values)
        image_part = image_part + newer * forces[steps - 1 - j]
        older, now = (now, newer)
    image = reduce_members(image_part, "real")
    return (image, now[None])


def solution(mesh):
    in_specs = (
        P("real", "tile", None, None),
        P(("shot", "real"), "tile", None, None),
        P(("shot", "real"), "tile", None, None),
        P(("shot", "real"), "tile", None, None),
        P(("shot", "real"), "tile", None, None),
        P("tile", None, None),
        P("shot"),
        P("shot"),
        P("shot"),
        P("shot", None),
    )
    out_specs = (P(("shot", "tile"), None, None), P(("shot", "real"), "tile", None, None))
    return jax.shard_map(shards, mesh=mesh, in_specs=in_specs, out_specs=out_specs, check_vma=False)
```

```python
import functools
import jax
import jax.numpy as jnp
from jax import lax
from jax.experimental import pallas as pl
from jax.experimental.pallas import tpu as pltpu
from jax.sharding import PartitionSpec as P

SECOND = (-205.0 / 72.0, 8.0 / 5.0, -1.0 / 5.0, 8.0 / 315.0, -1.0 / 560.0)
FIRST = (4.0 / 5.0, -1.0 / 5.0, 4.0 / 105.0, -1.0 / 280.0)
HALO = 4
PADY = 8


def lane_shift(v, k, lane):
    width = v.shape[-1]
    if k > 0:
        rolled = pltpu.roll(v, width - k, 1)
        return jnp.where(lane < width - k, rolled, 0.0)
    rolled = pltpu.roll(v, -k, 1)
    return jnp.where(lane >= -k, rolled, 0.0)


def fill_padded(pad_ref, first_ref, mid_ref, second_ref, odd):
    planes, height, depth = mid_ref.shape
    pad_ref[...] = jnp.zeros(pad_ref.shape, jnp.float32)
    first = first_ref[...]
    second = second_ref[...]
    pad_ref[0:HALO, PADY:PADY + height, :] = jnp.where(odd, first, second)
    pad_ref[HALO:HALO + planes, PADY:PADY + height, :] = mid_ref[...]
    pad_ref[HALO + planes:, PADY:PADY + height, :] = jnp.where(odd, second, first)


def taps(pad_ref, plane, y0, rows, lane):
    def at(dx, dy):
        return pad_ref[plane + dx, pl.ds(PADY + y0 + dy, rows), :]
    centre = at(0, 0)
    lap = 3.0 * SECOND[0] * centre
    grads = []
    for axis in range(3):
        if axis == 0:
            get = lambda k: at(k, 0)
        elif axis == 1:
            get = lambda k: at(0, k)
        else:
            get = lambda k: lane_shift(centre, k, lane)
        vals = {k: get(k) for k in (1, 2, 3, 4, -1, -2, -3, -4)}
        for k in range(1, 5):
            lap = lap + SECOND[k] * (vals[k] + vals[-k])
        slope = FIRST[0] * (vals[1] - vals[-1])
        for k in range(2, 5):
            slope = slope + FIRST[k - 1] * (vals[k] - vals[-k])
        grads.append(slope)
    return centre, lap, grads


def step_kernel(*refs, block, rows, track, own_grad, want_force, edges):
    refs = list(refs)
    take = lambda n: [refs.pop(0) for _ in range(n)]
    (parity_ref,) = take(1)
    lo_ref, mid_ref, hi_ref = take(3)
    if own_grad:
        b_lo_ref, b_mid_ref, b_hi_ref = take(3)
    else:
        b_ref, g0_ref, g1_ref, g2_ref = take(4)
    c_ref, old_ref = take(2)
    if track:
        where_ref, amount_ref, rec_ref = take(3)
    force_ref = take(1)[0] if want_force else None
    (new_ref,) = take(1)
    if own_grad:
        g_out = take(3)
    if track and edges:
        edge_lo_ref, edge_hi_ref = take(2)
    if track:
        (sample_ref,) = take(1)
    (pad_ref,) = take(1)
    if own_grad:
        (b_pad_ref,) = take(1)
    if track:
        (keep_ref,) = take(1)
    i = pl.program_id(0)

    odd = parity_ref[0] == 1

    @pl.when(i == 0)
    def _():
        fill_padded(pad_ref, lo_ref, mid_ref, hi_ref, odd)
        if own_grad:
            fill_padded(b_pad_ref, b_lo_ref, b_mid_ref, b_hi_ref, odd)

    planes = mid_ref.shape[0]
    height = c_ref.shape[1]
    depth = c_ref.shape[2]
    lane = lax.broadcasted_iota(jnp.int32, (rows, depth), 1)
    row = lax.broadcasted_iota(jnp.int32, (rows, depth), 0)
    for p in range(block):
        plane = i * block + p + HALO
        for y0 in range(0, height, rows):
            sl = (p, pl.ds(y0, rows), slice(None))
            centre, lap, grads = taps(pad_ref, plane, y0, rows, lane)
            if own_grad:
                bvals, _, gb = taps(b_pad_ref, plane, y0, rows, lane)
                for out_ref, value in zip(g_out, gb):
                    out_ref[sl] = value
            else:
                bvals = b_ref[sl]
                gb = [g0_ref[sl], g1_ref[sl], g2_ref[sl]]
            force = bvals * lap + (gb[0] * grads[0] + gb[1] * grads[1] + gb[2] * grads[2])
            if want_force:
                force_ref[sl] = force
            newer = 2.0 * centre - old_ref[sl] + c_ref[sl] * force
            if track:
                hit = (where_ref[3] == 1) & (where_ref[0] == plane - HALO)
                mask = hit & (row == where_ref[1] - y0) & (lane == where_ref[2])
                newer = jnp.where(mask, newer + amount_ref[0], newer)
                keep_ref[pl.ds(pl.multiple_of((plane - HALO) * height + y0, 8), rows), :] = newer
            new_ref[sl] = newer

    if track:
        @pl.when(i == pl.num_programs(0) - 1)
        def _():
            if edges:
                for q in range(HALO):
                    bottom = keep_ref[q * height:(q + 1) * height, :]
                    top = keep_ref[(planes - HALO + q) * height:(planes - HALO + q + 1) * height, :]
                    edge_lo_ref[q] = jnp.where(odd, bottom, top)
                    edge_hi_ref[q] = jnp.where(odd, top, bottom)
            one_lane = lax.broadcasted_iota(jnp.int32, (1, depth), 1)

            def sample(r, carry):
                line = keep_ref[pl.ds(rec_ref[0, r], 1), :]
                sample_ref[pl.ds(r, 1), :] = jnp.where(one_lane == rec_ref[1, r], line, 0.0)
                return carry

            lax.fori_loop(0, sample_ref.shape[0], sample, 0, unroll=8)


def grad_kernel(lo_ref, mid_ref, hi_ref, g0_ref, g1_ref, g2_ref, pad_ref, *, block, rows):
    i = pl.program_id(0)

    @pl.when(i == 0)
    def _():
        fill_padded(pad_ref, lo_ref, mid_ref, hi_ref)

    height = mid_ref.shape[1]
    lane = lax.broadcasted_iota(jnp.int32, (rows, mid_ref.shape[2]), 1)
    for p in range(block):
        plane = i * block + p + HALO
        for y0 in range(0, height, rows):
            sl = (p, pl.ds(y0, rows), slice(None))
            _, _, grads = taps(pad_ref, plane, y0, rows, lane)
            g0_ref[sl] = grads[0]
            g1_ref[sl] = grads[1]
            g2_ref[sl] = grads[2]


def final_kernel(parity_ref, lo_ref, mid_ref, hi_ref, b_ref, g0_ref, g1_ref, g2_ref, c_ref, old_ref,
                 rec_ref, valid_ref, amount_ref, new_ref, pad_ref, *, block, rows):
    i = pl.program_id(0)
    odd = parity_ref[0] == 1

    @pl.when(i == 0)
    def _():
        fill_padded(pad_ref, lo_ref, mid_ref, hi_ref, odd)

    planes, height, depth = mid_ref.shape
    lane = lax.broadcasted_iota(jnp.int32, (rows, depth), 1)
    for p in range(block):
        plane = i * block + p + HALO
        for y0 in range(0, height, rows):
            sl = (p, pl.ds(y0, rows), slice(None))
            centre, lap, grads = taps(pad_ref, plane, y0, rows, lane)
            force = b_ref[sl] * lap + (g0_ref[sl] * grads[0] + g1_ref[sl] * grads[1] + g2_ref[sl] * grads[2])
            new_ref[plane - HALO, pl.ds(y0, rows), :] = 2.0 * centre - old_ref[sl] + c_ref[sl] * force

    @pl.when(i == pl.num_programs(0) - 1)
    def _():
        one_lane = lax.broadcasted_iota(jnp.int32, (1, depth), 1)

        def add(r, carry):
            x = rec_ref[0, r]
            y = rec_ref[1, r]
            hit = (one_lane == rec_ref[2, r]) & (valid_ref[r] == 1)
            line = new_ref[x, pl.ds(y, 1), :]
            new_ref[x, pl.ds(y, 1), :] = jnp.where(hit, line + amount_ref[r], line)
            return carry

        lax.fori_loop(0, amount_ref.shape[0], add, 0, unroll=8)


def apply_final(parity, lo, mid, hi, b, g, c, old, receivers, valid, amount, rows=40):
    planes, height, depth = mid.shape
    block = pick_block(planes)
    full, blk = specs(mid.shape, block)
    out = jax.ShapeDtypeStruct(mid.shape, jnp.float32)
    smem = pl.BlockSpec(memory_space=pltpu.SMEM)
    return pl.pallas_call(
        functools.partial(final_kernel, block=block, rows=rows),
        grid=(planes // block,),
        in_specs=[smem, full(lo.shape), full(mid.shape), full(hi.shape)] + [blk] * 6
        + [smem, smem, smem],
        out_specs=full(mid.shape),
        out_shape=out,
        scratch_shapes=[pltpu.VMEM((planes + 2 * HALO, height + 2 * PADY, depth), jnp.float32)],
        compiler_params=pltpu.CompilerParams(dimension_semantics=("arbitrary",)),
    )(parity, lo, mid, hi, b, g[0], g[1], g[2], c, old, receivers, valid, amount)


def pick_block(planes):
    for b in (4, 2, 1):
        if planes % b == 0:
            return b


def specs(shape, block):
    planes, height, depth = shape
    full = lambda s: pl.BlockSpec(s, lambda i: (0, 0, 0))
    blk = pl.BlockSpec((block, height, depth), lambda i: (i, 0, 0))
    return full, blk


def apply_step(parity, lo, mid, hi, b, g, c, old, track=None, rows=40, want_force=True, edges=True):
    planes, height, depth = mid.shape
    block = pick_block(planes)
    full, blk = specs(mid.shape, block)
    out = jax.ShapeDtypeStruct(mid.shape, jnp.float32)
    own_grad = g is None
    in_specs = [pl.BlockSpec(memory_space=pltpu.SMEM), full(lo.shape), full(mid.shape), full(hi.shape)]
    args = [parity, lo, mid, hi]
    if own_grad:
        in_specs += [full(b[0].shape), full(b[1].shape), full(b[2].shape)]
        args += list(b)
    else:
        in_specs += [blk] * 4
        args += [b, g[0], g[1], g[2]]
    in_specs += [blk, blk]
    args += [c, old]
    out_specs = [blk] if want_force else []
    out_shape = [out] if want_force else []
    out_specs.append(blk)
    out_shape.append(out)
    if own_grad:
        out_specs += [blk] * 3
        out_shape += [out] * 3
    scratch = [pltpu.VMEM((planes + 2 * HALO, height + 2 * PADY, depth), jnp.float32)]
    if own_grad:
        scratch.append(pltpu.VMEM((planes + 2 * HALO, height + 2 * PADY, depth), jnp.float32))
    if track is not None:
        smem = pl.BlockSpec(memory_space=pltpu.SMEM)
        in_specs += [smem, smem, smem]
        args += list(track)
        count = track[2].shape[1]
        edge = jax.ShapeDtypeStruct((HALO, height, depth), jnp.float32)
        lines = jax.ShapeDtypeStruct((count, depth), jnp.float32)
        if edges:
            out_specs += [full(edge.shape), full(edge.shape)]
            out_shape += [edge, edge]
        out_specs.append(pl.BlockSpec((count, depth), lambda i: (0, 0)))
        out_shape.append(lines)
        scratch.append(pltpu.VMEM((planes * height, depth), jnp.float32))
    kernel = functools.partial(
        step_kernel, block=block, rows=rows, track=track is not None, own_grad=own_grad, want_force=want_force,
        edges=edges,
    )
    return pl.pallas_call(
        kernel,
        grid=(planes // block,),
        in_specs=in_specs,
        out_specs=out_specs,
        out_shape=out_shape,
        scratch_shapes=scratch,
        compiler_params=pltpu.CompilerParams(dimension_semantics=("arbitrary",)),
    )(*args)


def apply_grad(lo, mid, hi, rows=40):
    planes, height, depth = mid.shape
    block = pick_block(planes)
    full, blk = specs(mid.shape, block)
    out = jax.ShapeDtypeStruct(mid.shape, jnp.float32)
    return pl.pallas_call(
        functools.partial(grad_kernel, block=block, rows=rows),
        grid=(planes // block,),
        in_specs=[full(lo.shape), full(mid.shape), full(hi.shape)],
        out_specs=[blk, blk, blk],
        out_shape=[out, out, out],
        scratch_shapes=[pltpu.VMEM((planes + 2 * HALO, height + 2 * PADY, depth), jnp.float32)],
        compiler_params=pltpu.CompilerParams(dimension_semantics=("arbitrary",)),
    )(lo, mid, hi)


def reduce_members(base, axis, scale=None, weight=None):
    part = base if scale is None else base + scale * weight
    members = lax.axis_size(axis)
    if members & (members - 1) or part.size % (members * 1024):
        return lax.psum(part, axis) / members
    me = lax.axis_index(axis)
    if scale is not None:
        flat = [x.reshape(-1, 128) for x in (base, scale, weight)]
        half = flat[0].shape[0] // 2
        upper = me % 2
        keep = [lax.dynamic_slice_in_dim(x, upper * half, half, 0) for x in flat]
        give = [lax.dynamic_slice_in_dim(x, (1 - upper) * half, half, 0) for x in flat]
        sent = lax.ppermute(give[0] + give[1] * give[2], axis, [(i, i ^ 1) for i in range(members)])
        rows = (keep[0] + keep[1] * keep[2]) + sent
    else:
        rows = part.reshape(-1, 128)
    bits = members.bit_length() - 1
    for b in range(0 if scale is None else 1, bits):
        mask = 1 << b
        half = rows.shape[0] // 2
        upper = (me // mask) % 2
        keep = lax.dynamic_slice_in_dim(rows, upper * half, half, 0)
        give = lax.dynamic_slice_in_dim(rows, (1 - upper) * half, half, 0)
        pairs = [(i, i ^ mask) for i in range(members)]
        rows = keep + lax.ppermute(give, axis, pairs)
    rows = rows / members
    for b in reversed(range(bits)):
        mask = 1 << b
        upper = (me // mask) % 2
        pairs = [(i, i ^ mask) for i in range(members)]
        other = lax.ppermute(rows, axis, pairs)
        rows = jnp.where(upper == 1, jnp.concatenate([other, rows]), jnp.concatenate([rows, other]))
    return rows.reshape(part.shape)


def swap_halos(sends, axis):
    count = lax.axis_size(axis)
    first = [(i, i ^ 1) for i in range(count) if i ^ 1 < count]
    second = [(i, i + 1) for i in range(1, count - 1, 2)] + [(i + 1, i) for i in range(1, count - 1, 2)]
    return lax.ppermute(sends[0], axis, first), lax.ppermute(sends[1], axis, second)


def halos(block, axis):
    planes = block.shape[0]
    odd = lax.axis_index(axis) % 2
    near = lax.dynamic_slice_in_dim(block, (1 - odd) * (planes - HALO), HALO, 0)
    far = lax.dynamic_slice_in_dim(block, odd * (planes - HALO), HALO, 0)
    return swap_halos((near, far), axis)


def inject(field, where, valid, values):
    flat = field.reshape(-1).at[where].add(jnp.where(valid, values, 0.0))
    return flat.reshape(field.shape)


def shards(
    courant,
    prev_field,
    cur_field,
    adj_prev,
    adj_cur,
    buoyancy,
    wavelet,
    src_cell,
    rec_cell,
    observed,
):
    speed = courant[0]
    planes, height, depth = buoyancy.shape
    volume = planes * height * depth
    offset = lax.axis_index("tile") * volume
    steps = wavelet.shape[0]

    def locate(cells):
        local = cells - offset
        valid = (local >= 0) & (local < volume)
        return (jnp.clip(local, 0, volume - 1), valid)

    src_local, src_valid = locate(src_cell)
    rec_local, rec_valid = locate(rec_cell)
    parity = (lax.axis_index("tile") % 2).astype(jnp.int32).reshape(1)
    b_lo, b_hi = halos(buoyancy, "tile")

    def spread(cells):
        return jnp.stack([cells // (height * depth), (cells // depth) % height, cells % depth])

    where = jnp.concatenate([spread(src_local)[:, 0], src_valid.astype(jnp.int32)])
    receivers = jnp.stack([rec_local // depth, rec_local % depth])
    older, now = (prev_field[0], cur_field[0])
    lo, hi = halos(now, "tile")
    forces = []
    samples = []
    grad_b = None
    for k in range(steps):
        track = (where, wavelet[k:k + 1], receivers)
        if grad_b is None:
            outs = apply_step(parity, lo, now, hi, (b_lo, buoyancy, b_hi), None, speed, older, track)
            force, newer = outs[:2]
            grad_b = outs[2:5]
            edge_lo, edge_hi, lines = outs[5:]
        else:
            outs = apply_step(parity, lo, now, hi, buoyancy, grad_b, speed, older, track, edges=k + 1 < steps)
            force, newer, lines = outs[0], outs[1], outs[-1]
            edge_lo, edge_hi = (outs[2], outs[3]) if k + 1 < steps else (None, None)
        if k + 1 < steps:
            lo, hi = swap_halos((edge_lo, edge_hi), "tile")
        samples.append(jnp.sum(lines, axis=1))
        forces.append(force)
        older, now = (now, newer)
    residual = jnp.where(rec_valid, jnp.stack(samples) - observed, 0.0)
    older, now = (adj_prev[0], adj_cur[0])
    image_part = jnp.zeros(buoyancy.shape, jnp.float32)
    for j in range(steps):
        lo, hi = halos(now, "tile")
        if j + 1 < steps:
            (newer,) = apply_step(parity, lo, now, hi, buoyancy, grad_b, speed, older, want_force=False)
            newer = inject(newer, rec_local, rec_valid, residual[steps - 1 - j])
        else:
            cells = jnp.stack([rec_local // (height * depth), (rec_local // depth) % height, rec_local % depth])
            valid = rec_valid.astype(jnp.int32)
            newer = apply_final(parity, lo, now, hi, buoyancy, grad_b, speed, older, cells, valid, residual[0])
        if j + 1 < steps:
            image_part = image_part + newer * forces[steps - 1 - j]
        older, now = (now, newer)
    image = reduce_members(image_part, "real", now, forces[0])
    return (image, now[None])


def solution(mesh):
    in_specs = (
        P("real", "tile", None, None),
        P(("shot", "real"), "tile", None, None),
        P(("shot", "real"), "tile", None, None),
        P(("shot", "real"), "tile", None, None),
        P(("shot", "real"), "tile", None, None),
        P("tile", None, None),
        P("shot"),
        P("shot"),
        P("shot"),
        P("shot", None),
    )
    out_specs = (P(("shot", "tile"), None, None), P(("shot", "real"), "tile", None, None))
    return jax.shard_map(shards, mesh=mesh, in_specs=in_specs, out_specs=out_specs, check_vma=False)
```

```python
import functools
import jax
import jax.numpy as jnp
from jax import lax
from jax.experimental import pallas as pl
from jax.experimental.pallas import tpu as pltpu
from jax.sharding import PartitionSpec as P

SECOND = (-205.0 / 72.0, 8.0 / 5.0, -1.0 / 5.0, 8.0 / 315.0, -1.0 / 560.0)
FIRST = (4.0 / 5.0, -1.0 / 5.0, 4.0 / 105.0, -1.0 / 280.0)
HALO = 4
PADY = 8


def lane_shift(v, k, lane):
    width = v.shape[-1]
    if k > 0:
        rolled = pltpu.roll(v, width - k, 1)
        return jnp.where(lane < width - k, rolled, 0.0)
    rolled = pltpu.roll(v, -k, 1)
    return jnp.where(lane >= -k, rolled, 0.0)


def fill_padded(pad_ref, first_ref, mid_ref, second_ref, odd):
    planes, height, depth = mid_ref.shape
    pad_ref[...] = jnp.zeros(pad_ref.shape, jnp.float32)
    first = first_ref[...]
    second = second_ref[...]
    pad_ref[0:HALO, PADY:PADY + height, :] = jnp.where(odd, first, second)
    pad_ref[HALO:HALO + planes, PADY:PADY + height, :] = mid_ref[...]
    pad_ref[HALO + planes:, PADY:PADY + height, :] = jnp.where(odd, second, first)


def taps(pad_ref, plane, y0, rows, lane):
    def at(dx, dy):
        return pad_ref[plane + dx, pl.ds(PADY + y0 + dy, rows), :]
    centre = at(0, 0)
    lap = 3.0 * SECOND[0] * centre
    grads = []
    for axis in range(3):
        if axis == 0:
            get = lambda k: at(k, 0)
        elif axis == 1:
            get = lambda k: at(0, k)
        else:
            get = lambda k: lane_shift(centre, k, lane)
        vals = {k: get(k) for k in (1, 2, 3, 4, -1, -2, -3, -4)}
        for k in range(1, 5):
            lap = lap + SECOND[k] * (vals[k] + vals[-k])
        slope = FIRST[0] * (vals[1] - vals[-1])
        for k in range(2, 5):
            slope = slope + FIRST[k - 1] * (vals[k] - vals[-k])
        grads.append(slope)
    return centre, lap, grads


def step_kernel(*refs, block, rows, track, own_grad, want_force, edges):
    refs = list(refs)
    take = lambda n: [refs.pop(0) for _ in range(n)]
    (parity_ref,) = take(1)
    lo_ref, mid_ref, hi_ref = take(3)
    if own_grad:
        b_lo_ref, b_mid_ref, b_hi_ref = take(3)
    else:
        b_ref, g0_ref, g1_ref, g2_ref = take(4)
    c_ref, old_ref = take(2)
    if track:
        where_ref, amount_ref, rec_ref = take(3)
    force_ref = take(1)[0] if want_force else None
    (new_ref,) = take(1)
    if own_grad:
        g_out = take(3)
    if track and edges:
        edge_lo_ref, edge_hi_ref = take(2)
    if track:
        (sample_ref,) = take(1)
    (pad_ref,) = take(1)
    if own_grad:
        (b_pad_ref,) = take(1)
    if track:
        (keep_ref,) = take(1)
    i = pl.program_id(0)

    odd = parity_ref[0] == 1

    @pl.when(i == 0)
    def _():
        fill_padded(pad_ref, lo_ref, mid_ref, hi_ref, odd)
        if own_grad:
            fill_padded(b_pad_ref, b_lo_ref, b_mid_ref, b_hi_ref, odd)

    planes = mid_ref.shape[0]
    height = c_ref.shape[1]
    depth = c_ref.shape[2]
    lane = lax.broadcasted_iota(jnp.int32, (rows, depth), 1)
    row = lax.broadcasted_iota(jnp.int32, (rows, depth), 0)
    for p in range(block):
        plane = i * block + p + HALO
        for y0 in range(0, height, rows):
            sl = (p, pl.ds(y0, rows), slice(None))
            centre, lap, grads = taps(pad_ref, plane, y0, rows, lane)
            if own_grad:
                bvals, _, gb = taps(b_pad_ref, plane, y0, rows, lane)
                for out_ref, value in zip(g_out, gb):
                    out_ref[sl] = value
            else:
                bvals = b_ref[sl]
                gb = [g0_ref[sl], g1_ref[sl], g2_ref[sl]]
            force = bvals * lap + (gb[0] * grads[0] + gb[1] * grads[1] + gb[2] * grads[2])
            if want_force:
                force_ref[sl] = force
            newer = 2.0 * centre - old_ref[sl] + c_ref[sl] * force
            if track:
                hit = (where_ref[3] == 1) & (where_ref[0] == plane - HALO)
                mask = hit & (row == where_ref[1] - y0) & (lane == where_ref[2])
                newer = jnp.where(mask, newer + amount_ref[0], newer)
                keep_ref[pl.ds(pl.multiple_of((plane - HALO) * height + y0, 8), rows), :] = newer
            new_ref[sl] = newer

    if track:
        @pl.when(i == pl.num_programs(0) - 1)
        def _():
            if edges:
                for q in range(HALO):
                    bottom = keep_ref[q * height:(q + 1) * height, :]
                    top = keep_ref[(planes - HALO + q) * height:(planes - HALO + q + 1) * height, :]
                    edge_lo_ref[q] = jnp.where(odd, bottom, top)
                    edge_hi_ref[q] = jnp.where(odd, top, bottom)
            one_lane = lax.broadcasted_iota(jnp.int32, (1, depth), 1)

            def sample(r, carry):
                line = keep_ref[pl.ds(rec_ref[0, r], 1), :]
                sample_ref[pl.ds(r, 1), :] = jnp.where(one_lane == rec_ref[1, r], line, 0.0)
                return carry

            lax.fori_loop(0, sample_ref.shape[0], sample, 0, unroll=8)


def grad_kernel(lo_ref, mid_ref, hi_ref, g0_ref, g1_ref, g2_ref, pad_ref, *, block, rows):
    i = pl.program_id(0)

    @pl.when(i == 0)
    def _():
        fill_padded(pad_ref, lo_ref, mid_ref, hi_ref)

    height = mid_ref.shape[1]
    lane = lax.broadcasted_iota(jnp.int32, (rows, mid_ref.shape[2]), 1)
    for p in range(block):
        plane = i * block + p + HALO
        for y0 in range(0, height, rows):
            sl = (p, pl.ds(y0, rows), slice(None))
            _, _, grads = taps(pad_ref, plane, y0, rows, lane)
            g0_ref[sl] = grads[0]
            g1_ref[sl] = grads[1]
            g2_ref[sl] = grads[2]


def final_kernel(parity_ref, lo_ref, mid_ref, hi_ref, b_ref, g0_ref, g1_ref, g2_ref, c_ref, old_ref,
                 rec_ref, valid_ref, amount_ref, new_ref, pad_ref, *, block, rows):
    i = pl.program_id(0)
    odd = parity_ref[0] == 1

    @pl.when(i == 0)
    def _():
        fill_padded(pad_ref, lo_ref, mid_ref, hi_ref, odd)

    planes, height, depth = mid_ref.shape
    lane = lax.broadcasted_iota(jnp.int32, (rows, depth), 1)
    for p in range(block):
        plane = i * block + p + HALO
        for y0 in range(0, height, rows):
            sl = (p, pl.ds(y0, rows), slice(None))
            centre, lap, grads = taps(pad_ref, plane, y0, rows, lane)
            force = b_ref[sl] * lap + (g0_ref[sl] * grads[0] + g1_ref[sl] * grads[1] + g2_ref[sl] * grads[2])
            new_ref[plane - HALO, pl.ds(y0, rows), :] = 2.0 * centre - old_ref[sl] + c_ref[sl] * force

    @pl.when(i == pl.num_programs(0) - 1)
    def _():
        one_lane = lax.broadcasted_iota(jnp.int32, (1, depth), 1)

        def add(r, carry):
            x = rec_ref[0, r]
            y = rec_ref[1, r]
            hit = (one_lane == rec_ref[2, r]) & (valid_ref[r] == 1)
            line = new_ref[x, pl.ds(y, 1), :]
            new_ref[x, pl.ds(y, 1), :] = jnp.where(hit, line + amount_ref[r], line)
            return carry

        lax.fori_loop(0, amount_ref.shape[0], add, 0, unroll=8)


def apply_final(parity, lo, mid, hi, b, g, c, old, receivers, valid, amount, rows=40):
    planes, height, depth = mid.shape
    block = pick_block(planes)
    full, blk = specs(mid.shape, block)
    out = jax.ShapeDtypeStruct(mid.shape, jnp.float32)
    smem = pl.BlockSpec(memory_space=pltpu.SMEM)
    return pl.pallas_call(
        functools.partial(final_kernel, block=block, rows=rows),
        grid=(planes // block,),
        in_specs=[smem, full(lo.shape), full(mid.shape), full(hi.shape)] + [blk] * 6
        + [smem, smem, smem],
        out_specs=full(mid.shape),
        out_shape=out,
        scratch_shapes=[pltpu.VMEM((planes + 2 * HALO, height + 2 * PADY, depth), jnp.float32)],
        compiler_params=pltpu.CompilerParams(dimension_semantics=("arbitrary",)),
        cost_estimate=pl.CostEstimate(flops=100 * mid.size, transcendentals=0, bytes_accessed=40 * mid.size),
    )(parity, lo, mid, hi, b, g[0], g[1], g[2], c, old, receivers, valid, amount)


def pick_block(planes):
    for b in (4, 2, 1):
        if planes % b == 0:
            return b


def specs(shape, block):
    planes, height, depth = shape
    full = lambda s: pl.BlockSpec(s, lambda i: (0, 0, 0))
    blk = pl.BlockSpec((block, height, depth), lambda i: (i, 0, 0))
    return full, blk


def apply_step(parity, lo, mid, hi, b, g, c, old, track=None, rows=40, want_force=True, edges=True):
    planes, height, depth = mid.shape
    block = pick_block(planes)
    full, blk = specs(mid.shape, block)
    out = jax.ShapeDtypeStruct(mid.shape, jnp.float32)
    own_grad = g is None
    in_specs = [pl.BlockSpec(memory_space=pltpu.SMEM), full(lo.shape), full(mid.shape), full(hi.shape)]
    args = [parity, lo, mid, hi]
    if own_grad:
        in_specs += [full(b[0].shape), full(b[1].shape), full(b[2].shape)]
        args += list(b)
    else:
        in_specs += [blk] * 4
        args += [b, g[0], g[1], g[2]]
    in_specs += [blk, blk]
    args += [c, old]
    out_specs = [blk] if want_force else []
    out_shape = [out] if want_force else []
    out_specs.append(blk)
    out_shape.append(out)
    if own_grad:
        out_specs += [blk] * 3
        out_shape += [out] * 3
    scratch = [pltpu.VMEM((planes + 2 * HALO, height + 2 * PADY, depth), jnp.float32)]
    if own_grad:
        scratch.append(pltpu.VMEM((planes + 2 * HALO, height + 2 * PADY, depth), jnp.float32))
    if track is not None:
        smem = pl.BlockSpec(memory_space=pltpu.SMEM)
        in_specs += [smem, smem, smem]
        args += list(track)
        count = track[2].shape[1]
        edge = jax.ShapeDtypeStruct((HALO, height, depth), jnp.float32)
        lines = jax.ShapeDtypeStruct((count, depth), jnp.float32)
        if edges:
            out_specs += [full(edge.shape), full(edge.shape)]
            out_shape += [edge, edge]
        out_specs.append(pl.BlockSpec((count, depth), lambda i: (0, 0)))
        out_shape.append(lines)
        scratch.append(pltpu.VMEM((planes * height, depth), jnp.float32))
    kernel = functools.partial(
        step_kernel, block=block, rows=rows, track=track is not None, own_grad=own_grad, want_force=want_force,
        edges=edges,
    )
    return pl.pallas_call(
        kernel,
        grid=(planes // block,),
        in_specs=in_specs,
        out_specs=out_specs,
        out_shape=out_shape,
        scratch_shapes=scratch,
        compiler_params=pltpu.CompilerParams(dimension_semantics=("arbitrary",)),
        cost_estimate=pl.CostEstimate(flops=100 * mid.size, transcendentals=0, bytes_accessed=40 * mid.size),
    )(*args)


def apply_grad(lo, mid, hi, rows=40):
    planes, height, depth = mid.shape
    block = pick_block(planes)
    full, blk = specs(mid.shape, block)
    out = jax.ShapeDtypeStruct(mid.shape, jnp.float32)
    return pl.pallas_call(
        functools.partial(grad_kernel, block=block, rows=rows),
        grid=(planes // block,),
        in_specs=[full(lo.shape), full(mid.shape), full(hi.shape)],
        out_specs=[blk, blk, blk],
        out_shape=[out, out, out],
        scratch_shapes=[pltpu.VMEM((planes + 2 * HALO, height + 2 * PADY, depth), jnp.float32)],
        compiler_params=pltpu.CompilerParams(dimension_semantics=("arbitrary",)),
        cost_estimate=pl.CostEstimate(flops=100 * mid.size, transcendentals=0, bytes_accessed=40 * mid.size),
    )(lo, mid, hi)


def reduce_members(part, axis):
    members = lax.axis_size(axis)
    if members & (members - 1) or part.size % (members * 1024):
        return lax.psum(part, axis) / members
    me = lax.axis_index(axis)
    rows = part.reshape(-1, 128)
    bits = members.bit_length() - 1
    for b in range(bits):
        mask = 1 << b
        half = rows.shape[0] // 2
        upper = (me // mask) % 2
        keep = lax.dynamic_slice_in_dim(rows, upper * half, half, 0)
        give = lax.dynamic_slice_in_dim(rows, (1 - upper) * half, half, 0)
        pairs = [(i, i ^ mask) for i in range(members)]
        rows = keep + lax.ppermute(give, axis, pairs)
    rows = rows / members
    for b in reversed(range(bits)):
        mask = 1 << b
        upper = (me // mask) % 2
        pairs = [(i, i ^ mask) for i in range(members)]
        other = lax.ppermute(rows, axis, pairs)
        rows = jnp.where(upper == 1, jnp.concatenate([other, rows]), jnp.concatenate([rows, other]))
    return rows.reshape(part.shape)


def swap_halos(sends, axis):
    count = lax.axis_size(axis)
    first = [(i, i ^ 1) for i in range(count) if i ^ 1 < count]
    second = [(i, i + 1) for i in range(1, count - 1, 2)] + [(i + 1, i) for i in range(1, count - 1, 2)]
    return lax.ppermute(sends[0], axis, first), lax.ppermute(sends[1], axis, second)


def halos(block, axis):
    planes = block.shape[0]
    odd = lax.axis_index(axis) % 2
    near = lax.dynamic_slice_in_dim(block, (1 - odd) * (planes - HALO), HALO, 0)
    far = lax.dynamic_slice_in_dim(block, odd * (planes - HALO), HALO, 0)
    return swap_halos((near, far), axis)


def inject(field, where, valid, values):
    flat = field.reshape(-1).at[where].add(jnp.where(valid, values, 0.0))
    return flat.reshape(field.shape)


def shards(
    courant,
    prev_field,
    cur_field,
    adj_prev,
    adj_cur,
    buoyancy,
    wavelet,
    src_cell,
    rec_cell,
    observed,
):
    speed = courant[0]
    planes, height, depth = buoyancy.shape
    volume = planes * height * depth
    offset = lax.axis_index("tile") * volume
    steps = wavelet.shape[0]

    def locate(cells):
        local = cells - offset
        valid = (local >= 0) & (local < volume)
        return (jnp.clip(local, 0, volume - 1), valid)

    src_local, src_valid = locate(src_cell)
    rec_local, rec_valid = locate(rec_cell)
    parity = (lax.axis_index("tile") % 2).astype(jnp.int32).reshape(1)
    b_lo, b_hi = halos(buoyancy, "tile")

    def spread(cells):
        return jnp.stack([cells // (height * depth), (cells // depth) % height, cells % depth])

    where = jnp.concatenate([spread(src_local)[:, 0], src_valid.astype(jnp.int32)])
    receivers = jnp.stack([rec_local // depth, rec_local % depth])
    older, now = (prev_field[0], cur_field[0])
    lo, hi = halos(now, "tile")
    forces = []
    samples = []
    grad_b = None
    for k in range(steps):
        track = (where, wavelet[k:k + 1], receivers)
        if grad_b is None:
            outs = apply_step(parity, lo, now, hi, (b_lo, buoyancy, b_hi), None, speed, older, track)
            force, newer = outs[:2]
            grad_b = outs[2:5]
            edge_lo, edge_hi, lines = outs[5:]
        else:
            outs = apply_step(parity, lo, now, hi, buoyancy, grad_b, speed, older, track, edges=k + 1 < steps)
            force, newer, lines = outs[0], outs[1], outs[-1]
            edge_lo, edge_hi = (outs[2], outs[3]) if k + 1 < steps else (None, None)
        if k + 1 < steps:
            lo, hi = swap_halos((edge_lo, edge_hi), "tile")
        samples.append(jnp.sum(lines, axis=1))
        forces.append(force)
        older, now = (now, newer)
    residual = jnp.where(rec_valid, jnp.stack(samples) - observed, 0.0)
    older, now = (adj_prev[0], adj_cur[0])
    image_part = jnp.zeros(buoyancy.shape, jnp.float32)
    for j in range(steps):
        lo, hi = halos(now, "tile")
        if j + 1 < steps:
            (newer,) = apply_step(parity, lo, now, hi, buoyancy, grad_b, speed, older, want_force=False)
            newer = inject(newer, rec_local, rec_valid, residual[steps - 1 - j])
        else:
            cells = jnp.stack([rec_local // (height * depth), (rec_local // depth) % height, rec_local % depth])
            valid = rec_valid.astype(jnp.int32)
            newer = apply_final(parity, lo, now, hi, buoyancy, grad_b, speed, older, cells, valid, residual[0])
        image_part = image_part + newer * forces[steps - 1 - j]
        older, now = (now, newer)
    image = reduce_members(image_part, "real")
    return (image, now[None])


def solution(mesh):
    in_specs = (
        P("real", "tile", None, None),
        P(("shot", "real"), "tile", None, None),
        P(("shot", "real"), "tile", None, None),
        P(("shot", "real"), "tile", None, None),
        P(("shot", "real"), "tile", None, None),
        P("tile", None, None),
        P("shot"),
        P("shot"),
        P("shot"),
        P("shot", None),
    )
    out_specs = (P(("shot", "tile"), None, None), P(("shot", "real"), "tile", None, None))
    return jax.shard_map(shards, mesh=mesh, in_specs=in_specs, out_specs=out_specs, check_vma=False)
```

```python
import functools
import jax
import jax.numpy as jnp
from jax import lax
from jax.experimental import pallas as pl
from jax.experimental.pallas import tpu as pltpu
from jax.sharding import PartitionSpec as P

SECOND = (-205.0 / 72.0, 8.0 / 5.0, -1.0 / 5.0, 8.0 / 315.0, -1.0 / 560.0)
FIRST = (4.0 / 5.0, -1.0 / 5.0, 4.0 / 105.0, -1.0 / 280.0)
HALO = 4
PADY = 8


def lane_shift(v, k, lane):
    width = v.shape[-1]
    if k > 0:
        rolled = pltpu.roll(v, width - k, 1)
        return jnp.where(lane < width - k, rolled, 0.0)
    rolled = pltpu.roll(v, -k, 1)
    return jnp.where(lane >= -k, rolled, 0.0)


def fill_padded(pad_ref, first_ref, mid_ref, second_ref, odd):
    planes, height, depth = mid_ref.shape
    pad_ref[...] = jnp.zeros(pad_ref.shape, jnp.float32)
    first = first_ref[...]
    second = second_ref[...]
    pad_ref[0:HALO, PADY:PADY + height, :] = jnp.where(odd, first, second)
    pad_ref[HALO:HALO + planes, PADY:PADY + height, :] = mid_ref[...]
    pad_ref[HALO + planes:, PADY:PADY + height, :] = jnp.where(odd, second, first)


def taps(pad_ref, plane, y0, rows, lane):
    def at(dx, dy):
        return pad_ref[plane + dx, pl.ds(PADY + y0 + dy, rows), :]
    centre = at(0, 0)
    lap = 3.0 * SECOND[0] * centre
    grads = []
    for axis in range(3):
        if axis == 0:
            get = lambda k: at(k, 0)
        elif axis == 1:
            get = lambda k: at(0, k)
        else:
            get = lambda k: lane_shift(centre, k, lane)
        vals = {k: get(k) for k in (1, 2, 3, 4, -1, -2, -3, -4)}
        for k in range(1, 5):
            lap = lap + SECOND[k] * (vals[k] + vals[-k])
        slope = FIRST[0] * (vals[1] - vals[-1])
        for k in range(2, 5):
            slope = slope + FIRST[k - 1] * (vals[k] - vals[-k])
        grads.append(slope)
    return centre, lap, grads


def step_kernel(*refs, block, rows, track, own_grad, want_force, edges):
    refs = list(refs)
    take = lambda n: [refs.pop(0) for _ in range(n)]
    (parity_ref,) = take(1)
    lo_ref, mid_ref, hi_ref = take(3)
    if own_grad:
        b_lo_ref, b_mid_ref, b_hi_ref = take(3)
    else:
        b_ref, g0_ref, g1_ref, g2_ref = take(4)
    c_ref, old_ref = take(2)
    if track:
        where_ref, amount_ref, rec_ref = take(3)
    force_ref = take(1)[0] if want_force else None
    (new_ref,) = take(1)
    if own_grad:
        g_out = take(3)
    if track and edges:
        edge_lo_ref, edge_hi_ref = take(2)
    if track:
        (sample_ref,) = take(1)
    (pad_ref,) = take(1)
    if own_grad:
        (b_pad_ref,) = take(1)
    if track:
        (keep_ref,) = take(1)
    i = pl.program_id(0)

    odd = parity_ref[0] == 1

    @pl.when(i == 0)
    def _():
        fill_padded(pad_ref, lo_ref, mid_ref, hi_ref, odd)
        if own_grad:
            fill_padded(b_pad_ref, b_lo_ref, b_mid_ref, b_hi_ref, odd)

    planes = mid_ref.shape[0]
    height = c_ref.shape[1]
    depth = c_ref.shape[2]
    lane = lax.broadcasted_iota(jnp.int32, (rows, depth), 1)
    row = lax.broadcasted_iota(jnp.int32, (rows, depth), 0)
    for p in range(block):
        plane = i * block + p + HALO
        for y0 in range(0, height, rows):
            sl = (p, pl.ds(y0, rows), slice(None))
            centre, lap, grads = taps(pad_ref, plane, y0, rows, lane)
            if own_grad:
                bvals, _, gb = taps(b_pad_ref, plane, y0, rows, lane)
                for out_ref, value in zip(g_out, gb):
                    out_ref[sl] = value
            else:
                bvals = b_ref[sl]
                gb = [g0_ref[sl], g1_ref[sl], g2_ref[sl]]
            force = bvals * lap + (gb[0] * grads[0] + gb[1] * grads[1] + gb[2] * grads[2])
            if want_force:
                force_ref[sl] = force
            newer = 2.0 * centre - old_ref[sl] + c_ref[sl] * force
            if track:
                hit = (where_ref[3] == 1) & (where_ref[0] == plane - HALO)
                mask = hit & (row == where_ref[1] - y0) & (lane == where_ref[2])
                newer = jnp.where(mask, newer + amount_ref[0], newer)
                keep_ref[pl.ds(pl.multiple_of((plane - HALO) * height + y0, 8), rows), :] = newer
            new_ref[sl] = newer

    if track:
        @pl.when(i == pl.num_programs(0) - 1)
        def _():
            if edges:
                for q in range(HALO):
                    bottom = keep_ref[q * height:(q + 1) * height, :]
                    top = keep_ref[(planes - HALO + q) * height:(planes - HALO + q + 1) * height, :]
                    edge_lo_ref[q] = jnp.where(odd, bottom, top)
                    edge_hi_ref[q] = jnp.where(odd, top, bottom)
            one_lane = lax.broadcasted_iota(jnp.int32, (1, depth), 1)

            def sample(r, carry):
                line = keep_ref[pl.ds(rec_ref[0, r], 1), :]
                sample_ref[pl.ds(r, 1), :] = jnp.where(one_lane == rec_ref[1, r], line, 0.0)
                return carry

            lax.fori_loop(0, sample_ref.shape[0], sample, 0, unroll=8)


def grad_kernel(lo_ref, mid_ref, hi_ref, g0_ref, g1_ref, g2_ref, pad_ref, *, block, rows):
    i = pl.program_id(0)

    @pl.when(i == 0)
    def _():
        fill_padded(pad_ref, lo_ref, mid_ref, hi_ref)

    height = mid_ref.shape[1]
    lane = lax.broadcasted_iota(jnp.int32, (rows, mid_ref.shape[2]), 1)
    for p in range(block):
        plane = i * block + p + HALO
        for y0 in range(0, height, rows):
            sl = (p, pl.ds(y0, rows), slice(None))
            _, _, grads = taps(pad_ref, plane, y0, rows, lane)
            g0_ref[sl] = grads[0]
            g1_ref[sl] = grads[1]
            g2_ref[sl] = grads[2]


def final_kernel(parity_ref, lo_ref, mid_ref, hi_ref, b_ref, g0_ref, g1_ref, g2_ref, c_ref, old_ref,
                 rec_ref, valid_ref, amount_ref, new_ref, pad_ref, *, block, rows):
    i = pl.program_id(0)
    odd = parity_ref[0] == 1

    @pl.when(i == 0)
    def _():
        fill_padded(pad_ref, lo_ref, mid_ref, hi_ref, odd)

    planes, height, depth = mid_ref.shape
    lane = lax.broadcasted_iota(jnp.int32, (rows, depth), 1)
    for p in range(block):
        plane = i * block + p + HALO
        for y0 in range(0, height, rows):
            sl = (p, pl.ds(y0, rows), slice(None))
            centre, lap, grads = taps(pad_ref, plane, y0, rows, lane)
            force = b_ref[sl] * lap + (g0_ref[sl] * grads[0] + g1_ref[sl] * grads[1] + g2_ref[sl] * grads[2])
            new_ref[plane - HALO, pl.ds(y0, rows), :] = 2.0 * centre - old_ref[sl] + c_ref[sl] * force

    @pl.when(i == pl.num_programs(0) - 1)
    def _():
        one_lane = lax.broadcasted_iota(jnp.int32, (1, depth), 1)

        def add(r, carry):
            x = rec_ref[0, r]
            y = rec_ref[1, r]
            hit = (one_lane == rec_ref[2, r]) & (valid_ref[r] == 1)
            line = new_ref[x, pl.ds(y, 1), :]
            new_ref[x, pl.ds(y, 1), :] = jnp.where(hit, line + amount_ref[r], line)
            return carry

        lax.fori_loop(0, amount_ref.shape[0], add, 0, unroll=8)


def apply_final(parity, lo, mid, hi, b, g, c, old, receivers, valid, amount, rows=40):
    planes, height, depth = mid.shape
    block = 8 if planes % 8 == 0 else pick_block(planes)
    full, blk = specs(mid.shape, block)
    out = jax.ShapeDtypeStruct(mid.shape, jnp.float32)
    smem = pl.BlockSpec(memory_space=pltpu.SMEM)
    return pl.pallas_call(
        functools.partial(final_kernel, block=block, rows=rows),
        grid=(planes // block,),
        in_specs=[smem, full(lo.shape), full(mid.shape), full(hi.shape)] + [blk] * 6
        + [smem, smem, smem],
        out_specs=full(mid.shape),
        out_shape=out,
        scratch_shapes=[pltpu.VMEM((planes + 2 * HALO, height + 2 * PADY, depth), jnp.float32)],
        compiler_params=pltpu.CompilerParams(dimension_semantics=("arbitrary",)),
    )(parity, lo, mid, hi, b, g[0], g[1], g[2], c, old, receivers, valid, amount)


def pick_block(planes):
    for b in (4, 2, 1):
        if planes % b == 0:
            return b


def specs(shape, block):
    planes, height, depth = shape
    full = lambda s: pl.BlockSpec(s, lambda i: (0, 0, 0))
    blk = pl.BlockSpec((block, height, depth), lambda i: (i, 0, 0))
    return full, blk


def apply_step(parity, lo, mid, hi, b, g, c, old, track=None, rows=40, want_force=True, edges=True):
    planes, height, depth = mid.shape
    block = pick_block(planes)
    full, blk = specs(mid.shape, block)
    out = jax.ShapeDtypeStruct(mid.shape, jnp.float32)
    own_grad = g is None
    in_specs = [pl.BlockSpec(memory_space=pltpu.SMEM), full(lo.shape), full(mid.shape), full(hi.shape)]
    args = [parity, lo, mid, hi]
    if own_grad:
        in_specs += [full(b[0].shape), full(b[1].shape), full(b[2].shape)]
        args += list(b)
    else:
        in_specs += [blk] * 4
        args += [b, g[0], g[1], g[2]]
    in_specs += [blk, blk]
    args += [c, old]
    out_specs = [blk] if want_force else []
    out_shape = [out] if want_force else []
    out_specs.append(blk)
    out_shape.append(out)
    if own_grad:
        out_specs += [blk] * 3
        out_shape += [out] * 3
    scratch = [pltpu.VMEM((planes + 2 * HALO, height + 2 * PADY, depth), jnp.float32)]
    if own_grad:
        scratch.append(pltpu.VMEM((planes + 2 * HALO, height + 2 * PADY, depth), jnp.float32))
    if track is not None:
        smem = pl.BlockSpec(memory_space=pltpu.SMEM)
        in_specs += [smem, smem, smem]
        args += list(track)
        count = track[2].shape[1]
        edge = jax.ShapeDtypeStruct((HALO, height, depth), jnp.float32)
        lines = jax.ShapeDtypeStruct((count, depth), jnp.float32)
        if edges:
            out_specs += [full(edge.shape), full(edge.shape)]
            out_shape += [edge, edge]
        out_specs.append(pl.BlockSpec((count, depth), lambda i: (0, 0)))
        out_shape.append(lines)
        scratch.append(pltpu.VMEM((planes * height, depth), jnp.float32))
    kernel = functools.partial(
        step_kernel, block=block, rows=rows, track=track is not None, own_grad=own_grad, want_force=want_force,
        edges=edges,
    )
    return pl.pallas_call(
        kernel,
        grid=(planes // block,),
        in_specs=in_specs,
        out_specs=out_specs,
        out_shape=out_shape,
        scratch_shapes=scratch,
        compiler_params=pltpu.CompilerParams(dimension_semantics=("arbitrary",)),
    )(*args)


def apply_grad(lo, mid, hi, rows=40):
    planes, height, depth = mid.shape
    block = pick_block(planes)
    full, blk = specs(mid.shape, block)
    out = jax.ShapeDtypeStruct(mid.shape, jnp.float32)
    return pl.pallas_call(
        functools.partial(grad_kernel, block=block, rows=rows),
        grid=(planes // block,),
        in_specs=[full(lo.shape), full(mid.shape), full(hi.shape)],
        out_specs=[blk, blk, blk],
        out_shape=[out, out, out],
        scratch_shapes=[pltpu.VMEM((planes + 2 * HALO, height + 2 * PADY, depth), jnp.float32)],
        compiler_params=pltpu.CompilerParams(dimension_semantics=("arbitrary",)),
    )(lo, mid, hi)


def reduce_members(part, axis):
    members = lax.axis_size(axis)
    if members & (members - 1) or part.size % (members * 1024):
        return lax.psum(part, axis) / members
    me = lax.axis_index(axis)
    rows = part.reshape(-1, 128)
    bits = members.bit_length() - 1
    for b in range(bits):
        mask = 1 << b
        half = rows.shape[0] // 2
        upper = (me // mask) % 2
        keep = lax.dynamic_slice_in_dim(rows, upper * half, half, 0)
        give = lax.dynamic_slice_in_dim(rows, (1 - upper) * half, half, 0)
        pairs = [(i, i ^ mask) for i in range(members)]
        rows = keep + lax.ppermute(give, axis, pairs)
    rows = rows / members
    for b in reversed(range(bits)):
        mask = 1 << b
        upper = (me // mask) % 2
        pairs = [(i, i ^ mask) for i in range(members)]
        other = lax.ppermute(rows, axis, pairs)
        rows = jnp.where(upper == 1, jnp.concatenate([other, rows]), jnp.concatenate([rows, other]))
    return rows.reshape(part.shape)


def swap_halos(sends, axis):
    count = lax.axis_size(axis)
    first = [(i, i ^ 1) for i in range(count) if i ^ 1 < count]
    second = [(i, i + 1) for i in range(1, count - 1, 2)] + [(i + 1, i) for i in range(1, count - 1, 2)]
    return lax.ppermute(sends[0], axis, first), lax.ppermute(sends[1], axis, second)


def halos(block, axis):
    planes = block.shape[0]
    odd = lax.axis_index(axis) % 2
    near = lax.dynamic_slice_in_dim(block, (1 - odd) * (planes - HALO), HALO, 0)
    far = lax.dynamic_slice_in_dim(block, odd * (planes - HALO), HALO, 0)
    return swap_halos((near, far), axis)


def inject(field, where, valid, values):
    flat = field.reshape(-1).at[where].add(jnp.where(valid, values, 0.0))
    return flat.reshape(field.shape)


def shards(
    courant,
    prev_field,
    cur_field,
    adj_prev,
    adj_cur,
    buoyancy,
    wavelet,
    src_cell,
    rec_cell,
    observed,
):
    speed = courant[0]
    planes, height, depth = buoyancy.shape
    volume = planes * height * depth
    offset = lax.axis_index("tile") * volume
    steps = wavelet.shape[0]

    def locate(cells):
        local = cells - offset
        valid = (local >= 0) & (local < volume)
        return (jnp.clip(local, 0, volume - 1), valid)

    src_local, src_valid = locate(src_cell)
    rec_local, rec_valid = locate(rec_cell)
    parity = (lax.axis_index("tile") % 2).astype(jnp.int32).reshape(1)
    b_lo, b_hi = halos(buoyancy, "tile")

    def spread(cells):
        return jnp.stack([cells // (height * depth), (cells // depth) % height, cells % depth])

    where = jnp.concatenate([spread(src_local)[:, 0], src_valid.astype(jnp.int32)])
    receivers = jnp.stack([rec_local // depth, rec_local % depth])
    older, now = (prev_field[0], cur_field[0])
    lo, hi = halos(now, "tile")
    forces = []
    samples = []
    grad_b = None
    for k in range(steps):
        track = (where, wavelet[k:k + 1], receivers)
        if grad_b is None:
            outs = apply_step(parity, lo, now, hi, (b_lo, buoyancy, b_hi), None, speed, older, track)
            force, newer = outs[:2]
            grad_b = outs[2:5]
            edge_lo, edge_hi, lines = outs[5:]
        else:
            outs = apply_step(parity, lo, now, hi, buoyancy, grad_b, speed, older, track, edges=k + 1 < steps)
            force, newer, lines = outs[0], outs[1], outs[-1]
            edge_lo, edge_hi = (outs[2], outs[3]) if k + 1 < steps else (None, None)
        if k + 1 < steps:
            lo, hi = swap_halos((edge_lo, edge_hi), "tile")
        samples.append(jnp.sum(lines, axis=1))
        forces.append(force)
        older, now = (now, newer)
    residual = jnp.where(rec_valid, jnp.stack(samples) - observed, 0.0)
    older, now = (adj_prev[0], adj_cur[0])
    image_part = jnp.zeros(buoyancy.shape, jnp.float32)
    for j in range(steps):
        lo, hi = halos(now, "tile")
        if j + 1 < steps:
            (newer,) = apply_step(parity, lo, now, hi, buoyancy, grad_b, speed, older, want_force=False)
            newer = inject(newer, rec_local, rec_valid, residual[steps - 1 - j])
        else:
            cells = jnp.stack([rec_local // (height * depth), (rec_local // depth) % height, rec_local % depth])
            valid = rec_valid.astype(jnp.int32)
            newer = apply_final(parity, lo, now, hi, buoyancy, grad_b, speed, older, cells, valid, residual[0])
        image_part = image_part + newer * forces[steps - 1 - j]
        older, now = (now, newer)
    image = reduce_members(image_part, "real")
    return (image, now[None])


def solution(mesh):
    in_specs = (
        P("real", "tile", None, None),
        P(("shot", "real"), "tile", None, None),
        P(("shot", "real"), "tile", None, None),
        P(("shot", "real"), "tile", None, None),
        P(("shot", "real"), "tile", None, None),
        P("tile", None, None),
        P("shot"),
        P("shot"),
        P("shot"),
        P("shot", None),
    )
    out_specs = (P(("shot", "tile"), None, None), P(("shot", "real"), "tile", None, None))
    return jax.shard_map(shards, mesh=mesh, in_specs=in_specs, out_specs=out_specs, check_vma=False)
```
